32 devices in a mesh: groups: 2 (over y), ctx: 8 (over z, x), tp: 2 (over core).
Axes of the slice: x: 2, y: 2, z: 4, core: 2. Of those that a mesh axis runs over, the one named last changes fastest.
Arguments:
- tokens: bfloat16 [4096, 2688], P(('groups', 'ctx', 'tp')), parts along dimension 0, may hold values from -6 to 6
- output_gradient: bfloat16 [4096, 2688], P(('groups', 'ctx', 'tp')), parts along dimension 0, may hold values from -6 to 6
- document_index: int32 [4096], P(('groups', 'ctx')), parts along dimension 0, may hold values from 0 to 3, never falling along the last dimension, each value on 1 to 1024 neighbouring positions
- real_token_count: int32 [16], P(('groups', 'ctx')), parts along dimension 0, may hold values from 64 to 256, as said below
- input_norm_gain: float32 [2688], replicated, may hold values from 0.1 to 1.9
- query_norm_gain: float32 [128], replicated, may hold values from 0.1 to 1.9
- key_norm_gain: float32 [128], replicated, may hold values from 0.1 to 1.9
- output_norm_gain: float32 [2688], replicated, may hold values from 0.1 to 1.9
- query_projection: bfloat16 [2688, 512], P(None, 'tp'), may hold values from -0.125 to 0.125
- key_projection: bfloat16 [2688, 256], P(None, 'tp'), may hold values from -0.125 to 0.125
- value_projection: bfloat16 [2688, 256], P(None, 'tp'), may hold values from -0.125 to 0.125
- output_projection: bfloat16 [512, 2688], P('tp'), may hold values from -0.25 to 0.25
- adapter_down_maps: bfloat16 [2688, 48], replicated, may hold values from -0.125 to 0.125
- adapter_query_up: bfloat16 [16, 512], P(None, 'tp'), may hold values from -0.375 to 0.375
- adapter_key_up: bfloat16 [16, 256], P(None, 'tp'), may hold values from -0.375 to 0.375
- adapter_value_up: bfloat16 [16, 256], P(None, 'tp'), may hold values from -0.375 to 0.375
- adapter_output_down: bfloat16 [512, 16], P('tp'), may hold values from -0.25 to 0.25
- adapter_output_up: bfloat16 [16, 2688], replicated, may hold values from -0.375 to 0.375
Outputs:
- layer_out: bfloat16 [4096, 2688], P(('groups', 'ctx', 'tp')), parts along dimension 0
- grad_in: bfloat16 [4096, 2688], P(('groups', 'ctx', 'tp')), parts along dimension 0
- grad_down: float32 [5376, 48], P(('groups', 'tp')), parts along dimension 0
- query_up_gradient: float32 [32, 512], P('groups', 'tp'), parts along dimension 0
- key_up_gradient: float32 [32, 256], P('groups', 'tp'), parts along dimension 0
- value_up_gradient: float32 [32, 256], P('groups', 'tp'), parts along dimension 0
- grad_down_out: float32 [1024, 16], P(('groups', 'tp')), parts along dimension 0
- output_up_gradient: float32 [32, 2688], P('groups', 'tp'), parts along dimension 0
The draws below stay inside these ranges and needn't reach their ends.
There are 2 independent parts, one for each index of `groups`. The reference program is written for one: setup_inputs(seed, part) draws one part's arguments, and reference() takes and returns one part's arrays. A program takes and returns all parts, laid end to end along the dimension named above; an argument that names none is the same for every part. Nothing has to cross between parts.
Inputs may be any that keep to these rules, and one draw needn't show every extreme that they name: `document_index`: document numbers never fall along the tokens; a document has 1 to 1024 tokens and one has exactly that many. `real_token_count`: the real tokens of a block come first and the rest is padding; some block is full and some holds 64 real tokens.
All inputs are finite; a program needn't handle non-finite values.
Results may differ from the reference program's by a relative error of at most 0.034.
Values may be sent and summed in bfloat16 or wider, within the bound.
No kernel may reach another device: no remote copies, remote signals or barrier semaphores. Data moves between devices by JAX's collectives and lax.ppermute only.
A program may use at most 64 MiB of HBM per device.

```python
import math
import jax
import jax.numpy as jnp
import numpy as np
from jax import lax

MODEL_DIMENSION = 2688
HEAD_DIMENSION = 128
HEADS_DEV = 2
ADAPTER_RANK = 16
WINDOW = 1024
T_CTX = 256
QUERY_HEAD_COUNT = 4
KEY_VALUE_HEADS = 2
TOKENS = 2048
N_CTX = 8
N_TP = 2


def draw_real_token_count(key, part):
    first_key, second_key, third_key = jax.random.split(key, 3)
    counts_drawn = jax.random.randint(first_key, (N_CTX,), T_CTX // 4, T_CTX + 1)
    full_at = jax.random.randint(second_key, (), 0, N_CTX)
    short_at = (full_at + 1 + jax.random.randint(third_key, (), 0, N_CTX - 1)) % N_CTX
    places = jnp.arange(N_CTX)
    counts_drawn = jnp.where(places == full_at, T_CTX, counts_drawn)
    counts_drawn = jnp.where(places == short_at, T_CTX // 4, counts_drawn)
    return counts_drawn.astype(jnp.int32)


def block_scale(key, dims, cuts, low, top_value):
    loudness = 1.0
    for position, blocks in cuts:
        heights = jax.random.uniform(jax.random.fold_in(jax.random.fold_in(key, 6), position), (blocks,), jnp.float32, low / len(cuts), top_value / len(cuts))
        loudness = loudness * jnp.repeat(jnp.exp(heights), dims[position] // blocks).reshape((-1,) + (1,) * (len(dims) - 1 - position))
    return loudness


def length_profile(number_of, total, limit, slope):
    portions = [(1 << 20) // math.isqrt(standing ** slope) + 1 for standing in range(2, number_of + 1)]
    rest, given = total - limit - (number_of - 1), [1] * (number_of - 1)
    while rest > 0:
        free = [i for i in range(number_of - 1) if given[i] < limit]
        mass, budget = sum([portions[i] for i in free]), rest
        for i in free:
            more = min(limit - given[i], max(1, budget * portions[i] // mass), rest)
            given[i] = given[i] + more
            rest = rest - more
    return np.array([limit] + given)


def uneven(stream_key, amount, total, limit, skew):
    if amount == 2:
        one = jax.random.randint(stream_key, (), max(1, total - limit), min(limit, total - 1) + 1)
        return jnp.stack([one, total - one])
    sizes = jnp.asarray(length_profile(amount, total, limit, skew), jnp.int32)
    twos = (amount - 1) // 2
    giver, receiver = sizes[1:1 + 2 * twos:2], sizes[2:2 + 2 * twos:2]
    margin = jnp.minimum(giver - 1, limit - receiver)
    shifted = jax.random.randint(jax.random.fold_in(stream_key, 1), (twos,), 0, 1 << 20) % (margin + 1)
    sizes = sizes.at[1:1 + 2 * twos:2].set(giver - shifted).at[2:2 + 2 * twos:2].set(receiver + shifted)
    return sizes[jax.random.permutation(jax.random.fold_in(stream_key, 2), amount)]


def gaussian(stream_key, shape, spread, most, cuts=(), held_as=jnp.bfloat16):
    entries = jax.random.normal(stream_key, shape, jnp.float32) * spread
    if len(cuts) > 0:
        entries = block_scale(stream_key, shape, cuts, -0.22, 0.18) * entries
    return jnp.clip(entries, min=-most, max=most).astype(held_as)


def setup_inputs(seed: int = 0, part: int = 0) -> dict:
    key_list = jax.random.split(jax.random.key(seed), 19)
    own_keys = jax.random.split(jax.random.fold_in(key_list[18], part), 19)
    tokens = gaussian(own_keys[0], (TOKENS, MODEL_DIMENSION), 1.0, 6.0, ((0, 16),))
    output_gradient = gaussian(own_keys[1], (TOKENS, MODEL_DIMENSION), 1.0, 6.0, ((0, 16),))
    document_index = jnp.searchsorted(jnp.cumsum(uneven(own_keys[2], max(2, N_CTX // 2), TOKENS, TOKENS // 2, 2)), jnp.arange(TOKENS), side="right").astype(jnp.int32)
    real_token_count = draw_real_token_count(jax.random.fold_in(jax.random.fold_in(key_list[18], part), 71), part)
    input_norm_gain = jnp.clip(1.0 + 0.18 * jax.random.normal(key_list[4], (MODEL_DIMENSION,), jnp.float32), 0.1, 1.9)
    query_norm_gain = jnp.clip(1.0 + 0.18 * jax.random.normal(key_list[5], (HEAD_DIMENSION,), jnp.float32), 0.1, 1.9)
    key_norm_gain = jnp.clip(1.0 + 0.18 * jax.random.normal(key_list[6], (HEAD_DIMENSION,), jnp.float32), 0.1, 1.9)
    output_norm_gain = jnp.clip(1.0 + 0.18 * jax.random.normal(key_list[7], (MODEL_DIMENSION,), jnp.float32), 0.1, 1.9)
    query_projection = gaussian(key_list[8], (MODEL_DIMENSION, QUERY_HEAD_COUNT * HEAD_DIMENSION), MODEL_DIMENSION ** -0.5, 0.125, ((1, 2),))
    key_projection = gaussian(key_list[9], (MODEL_DIMENSION, KEY_VALUE_HEADS * HEAD_DIMENSION), MODEL_DIMENSION ** -0.5, 0.125, ((1, 2),))
    value_projection = gaussian(key_list[10], (MODEL_DIMENSION, KEY_VALUE_HEADS * HEAD_DIMENSION), MODEL_DIMENSION ** -0.5, 0.125, ((1, 2),))
    output_projection = gaussian(key_list[11], (QUERY_HEAD_COUNT * HEAD_DIMENSION, MODEL_DIMENSION), (QUERY_HEAD_COUNT * HEAD_DIMENSION) ** -0.5, 0.25, ((0, 2),))
    adapter_down_maps = gaussian(key_list[12], (MODEL_DIMENSION, 3 * ADAPTER_RANK), MODEL_DIMENSION ** -0.5, 0.125)
    adapter_query_up = gaussian(key_list[13], (ADAPTER_RANK, QUERY_HEAD_COUNT * HEAD_DIMENSION), (16 * ADAPTER_RANK) ** -0.5, 0.375, ((1, 2),))
    adapter_key_up = gaussian(key_list[14], (ADAPTER_RANK, KEY_VALUE_HEADS * HEAD_DIMENSION), (16 * ADAPTER_RANK) ** -0.5, 0.375, ((1, 2),))
    adapter_value_up = gaussian(key_list[15], (ADAPTER_RANK, KEY_VALUE_HEADS * HEAD_DIMENSION), (16 * ADAPTER_RANK) ** -0.5, 0.375, ((1, 2),))
    adapter_output_down = gaussian(key_list[16], (QUERY_HEAD_COUNT * HEAD_DIMENSION, ADAPTER_RANK), (QUERY_HEAD_COUNT * HEAD_DIMENSION) ** -0.5, 0.25, ((0, 2),))
    adapter_output_up = gaussian(key_list[17], (ADAPTER_RANK, MODEL_DIMENSION), (16 * ADAPTER_RANK) ** -0.5, 0.375)
    return dict(tokens=tokens, output_gradient=output_gradient, document_index=document_index, real_token_count=real_token_count, input_norm_gain=input_norm_gain, query_norm_gain=query_norm_gain, key_norm_gain=key_norm_gain, output_norm_gain=output_norm_gain, query_projection=query_projection, key_projection=key_projection, value_projection=value_projection, output_projection=output_projection, adapter_down_maps=adapter_down_maps, adapter_query_up=adapter_query_up, adapter_key_up=adapter_key_up, adapter_value_up=adapter_value_up, adapter_output_down=adapter_output_down, adapter_output_up=adapter_output_up)


epsilon = 1e-06
adapter_scale = 2.0
score_scale = 168.0 ** (-0.5)

def norm_rows(source, gain_vec):
    inverse = lax.rsqrt(lax.optimization_barrier(jnp.mean(source * source, axis=-1, keepdims=True)) + epsilon)
    return source * inverse * gain_vec

def norm_back(source, gain_vec, incoming):
    inverse = lax.rsqrt(lax.optimization_barrier(jnp.mean(source * source, axis=-1, keepdims=True)) + epsilon)
    scaled = source * inverse
    upward = incoming * gain_vec
    return inverse * (upward - scaled * lax.optimization_barrier(jnp.mean(upward * scaled, axis=-1, keepdims=True)))

def matrix_product(first_op, second_op):
    return jnp.dot(first_op, second_op, preferred_element_type=jnp.float32)

def rounded(source):
    return lax.optimization_barrier(source.astype(jnp.bfloat16)).astype(jnp.float32)

def window_mask(query_segs, key_codes):
    query_count = query_segs.shape[0]
    key_total = key_codes.shape[0]
    distance = (key_total - query_count + jnp.arange(query_count))[:, None] - jnp.arange(key_total)[None, :]
    same_doc = key_codes[None, :] == query_segs[:, None] + 1
    return (distance == 0) | (distance > 0) & (distance < WINDOW) & same_doc

def divide_groups(source, head_groups, per_width):
    return jnp.swapaxes(source.reshape(source.shape[0], head_groups, per_width), 0, 1)

def reference(tokens, output_gradient, document_index, real_token_count, input_norm_gain, query_norm_gain, key_norm_gain, output_norm_gain, query_projection, key_projection, value_projection, output_projection, adapter_down_maps, adapter_query_up, adapter_key_up, adapter_value_up, adapter_output_down, adapter_output_up):
    head_groups = N_TP
    head_total = HEADS_DEV * head_groups
    heads_per_group = HEADS_DEV * HEAD_DIMENSION
    tok_float = tokens.astype(jnp.float32)
    is_valid = (jnp.arange(T_CTX, dtype=jnp.int32)[None, :] < real_token_count[:, None]).reshape(TOKENS)
    real_token_fraction = is_valid.astype(jnp.float32)
    codes_all = jnp.where(is_valid, document_index + 1, 0).astype(jnp.int32)
    normalized_input = norm_rows(tok_float, input_norm_gain).astype(jnp.bfloat16)
    middle_list = matrix_product(normalized_input, adapter_down_maps).astype(jnp.bfloat16)
    middle_query = middle_list[:, :ADAPTER_RANK]
    middle_key = middle_list[:, ADAPTER_RANK:2 * ADAPTER_RANK]
    middle_value = middle_list[:, 2 * ADAPTER_RANK:]
    query_before_norm = matrix_product(normalized_input, query_projection) + adapter_scale * matrix_product(middle_query, adapter_query_up)
    key_before_norm = matrix_product(normalized_input, key_projection) + adapter_scale * matrix_product(middle_key, adapter_key_up)
    value_before_norm = matrix_product(normalized_input, value_projection) + adapter_scale * matrix_product(middle_value, adapter_value_up)
    query_heads = query_before_norm.reshape(TOKENS, head_groups, HEADS_DEV, HEAD_DIMENSION)
    query_normed = norm_rows(query_heads, query_norm_gain).astype(jnp.bfloat16)
    key_heads = key_before_norm.reshape(TOKENS, head_groups, HEAD_DIMENSION)
    key_normed = norm_rows(key_heads, key_norm_gain).astype(jnp.bfloat16)
    value_cast = value_before_norm.reshape(TOKENS, head_groups, HEAD_DIMENSION).astype(jnp.bfloat16)
    key_padded = jnp.concatenate([jnp.zeros((WINDOW, head_groups, HEAD_DIMENSION), jnp.bfloat16), key_normed], 0)
    value_padded = jnp.concatenate([jnp.zeros((WINDOW, head_groups, HEAD_DIMENSION), jnp.bfloat16), value_cast], 0)
    code_padded = jnp.concatenate([jnp.zeros((WINDOW,), jnp.int32), codes_all], 0)
    key_span = WINDOW + T_CTX

    def block_probs(block_start):
        queries = lax.dynamic_slice_in_dim(query_normed, block_start, T_CTX, 0).astype(jnp.float32)
        keys_here = lax.dynamic_slice_in_dim(key_padded, block_start, key_span, 0).astype(jnp.float32)
        values_here = lax.dynamic_slice_in_dim(value_padded, block_start, key_span, 0).astype(jnp.float32)
        codes_here = lax.dynamic_slice_in_dim(code_padded, block_start, key_span, 0)
        segs_here = lax.dynamic_slice_in_dim(document_index, block_start, T_CTX, 0)
        allowed = window_mask(segs_here, codes_here)
        scores = jnp.einsum('tgjd,sgd->gjts', queries, keys_here) * score_scale
        weights = jnp.where(allowed, jnp.exp(scores), 0.0)
        attn_probs = weights / lax.optimization_barrier(jnp.sum(weights, axis=-1, keepdims=True))
        return (queries, keys_here, values_here, attn_probs)

    def attend(block_index):
        block_start = (block_index * T_CTX).astype(jnp.int32)
        queries, keys_here, values_here, attn_probs = block_probs(block_start)
        result = jnp.einsum('gjts,sgd->tgjd', rounded(attn_probs), values_here)
        mask_rows = lax.dynamic_slice_in_dim(real_token_fraction, block_start, T_CTX, 0)
        return (result * mask_rows[:, None, None, None]).astype(jnp.bfloat16)
    blocks = jnp.arange(N_CTX, dtype=jnp.int32)
    attention_result = lax.map(attend, blocks).reshape(TOKENS, head_total * HEAD_DIMENSION)
    att_groups = divide_groups(attention_result, head_groups, heads_per_group)
    out_groups = output_projection.reshape(head_groups, heads_per_group, MODEL_DIMENSION)
    down_weight_groups = adapter_output_down.reshape(head_groups, heads_per_group, ADAPTER_RANK)

    def add_group(carried, pieces):
        total_out, total_mid = carried
        att_piece, out_piece, down_piece = pieces
        total_out = total_out + rounded(matrix_product(att_piece, out_piece))
        total_mid = total_mid + rounded(matrix_product(att_piece, down_piece))
        return ((total_out, total_mid), None)
    start_sums = (jnp.zeros((TOKENS, MODEL_DIMENSION), jnp.float32), jnp.zeros((TOKENS, ADAPTER_RANK), jnp.float32))
    (output_total, mid_sum), ignored = lax.scan(add_group, start_sums, (att_groups, out_groups, down_weight_groups))
    middle_output = mid_sum.astype(jnp.bfloat16)
    apply_prenorm = output_total + adapter_scale * matrix_product(middle_output, adapter_output_up)
    layer_out = norm_rows(apply_prenorm, output_norm_gain).astype(jnp.bfloat16)
    prenorm_gradient = norm_back(apply_prenorm, output_norm_gain, output_gradient.astype(jnp.float32)).astype(jnp.bfloat16)
    middle_output_gradient = (adapter_scale * matrix_product(prenorm_gradient, adapter_output_up.T)).astype(jnp.bfloat16)
    output_up_gradient = adapter_scale * matrix_product(middle_output.T, prenorm_gradient)
    attention_gradient = (matrix_product(prenorm_gradient, output_projection.T) + matrix_product(middle_output_gradient, adapter_output_down.T)) * real_token_fraction[:, None]
    attention_gradient = attention_gradient.astype(jnp.bfloat16)
    grad_down_out = matrix_product(attention_result.T, middle_output_gradient)
    grad_att_heads = attention_gradient.reshape(TOKENS, head_groups, HEADS_DEV, HEAD_DIMENSION)

    def back_block(carried, block_index):
        key_acc, value_acc = carried
        block_start = (block_index * T_CTX).astype(jnp.int32)
        queries, keys_here, values_here, attn_probs = block_probs(block_start)
        grad_heads = lax.dynamic_slice_in_dim(grad_att_heads, block_start, T_CTX, 0).astype(jnp.float32)
        grad_probs = jnp.einsum('tgjd,sgd->gjts', grad_heads, values_here)
        inner_sum = lax.optimization_barrier(jnp.sum(attn_probs * grad_probs, axis=-1, keepdims=True))
        grad_scores = rounded(attn_probs * (grad_probs - inner_sum) * score_scale)
        grad_query = jnp.einsum('gjts,sgd->tgjd', grad_scores, keys_here)
        grad_keys = jnp.einsum('gjts,tgjd->sgd', grad_scores, queries)
        grad_values = jnp.einsum('gjts,tgjd->sgd', rounded(attn_probs), grad_heads)
        key_acc = lax.dynamic_update_slice_in_dim(key_acc, lax.dynamic_slice_in_dim(key_acc, block_start, key_span, 0) + grad_keys, block_start, 0)
        value_acc = lax.dynamic_update_slice_in_dim(value_acc, lax.dynamic_slice_in_dim(value_acc, block_start, key_span, 0) + grad_values, block_start, 0)
        return ((key_acc, value_acc), grad_query)
    zeros_pad = jnp.zeros((WINDOW + TOKENS, head_groups, HEAD_DIMENSION), jnp.float32)
    (key_acc, value_acc), grad_query_blocks = lax.scan(back_block, (zeros_pad, zeros_pad), blocks)
    grad_query_all = grad_query_blocks.reshape(TOKENS, head_groups, HEADS_DEV, HEAD_DIMENSION)
    query_prenorm_gradient = norm_back(query_heads, query_norm_gain, grad_query_all).reshape(TOKENS, head_total * HEAD_DIMENSION).astype(jnp.bfloat16)
    key_prenorm_gradient = norm_back(key_heads, key_norm_gain, key_acc[WINDOW:]).reshape(TOKENS, head_groups * HEAD_DIMENSION).astype(jnp.bfloat16)
    value_prenorm_gradient = value_acc[WINDOW:].reshape(TOKENS, head_groups * HEAD_DIMENSION).astype(jnp.bfloat16)
    query_up_gradient = adapter_scale * matrix_product(middle_query.T, query_prenorm_gradient)
    key_up_gradient = adapter_scale * matrix_product(middle_key.T, key_prenorm_gradient)
    value_up_gradient = adapter_scale * matrix_product(middle_value.T, value_prenorm_gradient)
    collected_pieces = (divide_groups(query_prenorm_gradient, head_groups, heads_per_group), divide_groups(key_prenorm_gradient, head_groups, HEAD_DIMENSION), divide_groups(value_prenorm_gradient, head_groups, HEAD_DIMENSION), jnp.swapaxes(query_projection.reshape(MODEL_DIMENSION, head_groups, heads_per_group), 0, 1), jnp.swapaxes(key_projection.reshape(MODEL_DIMENSION, head_groups, HEAD_DIMENSION), 0, 1), jnp.swapaxes(value_projection.reshape(MODEL_DIMENSION, head_groups, HEAD_DIMENSION), 0, 1), jnp.swapaxes(adapter_query_up.reshape(ADAPTER_RANK, head_groups, heads_per_group), 0, 1), jnp.swapaxes(adapter_key_up.reshape(ADAPTER_RANK, head_groups, HEAD_DIMENSION), 0, 1), jnp.swapaxes(adapter_value_up.reshape(ADAPTER_RANK, head_groups, HEAD_DIMENSION), 0, 1))

    def back_group(carried, pieces):
        total_grad, total_down = carried
        query_gradient, key_gradient, value_gradient, query_weight_total, key_weight_total, value_weight_total, query_up_product, key_up_product, value_up_product = pieces
        middle_gradient_list = jnp.concatenate([adapter_scale * matrix_product(query_gradient, query_up_product.T), adapter_scale * matrix_product(key_gradient, key_up_product.T), adapter_scale * matrix_product(value_gradient, value_up_product.T)], 1).astype(jnp.bfloat16)
        group_contribution = matrix_product(query_gradient, query_weight_total.T) + matrix_product(key_gradient, key_weight_total.T) + matrix_product(value_gradient, value_weight_total.T) + matrix_product(middle_gradient_list, adapter_down_maps.T)
        total_grad = total_grad + rounded(group_contribution)
        total_down = total_down + matrix_product(normalized_input.T, middle_gradient_list)
        return ((total_grad, total_down), None)
    start_back = (jnp.zeros((TOKENS, MODEL_DIMENSION), jnp.float32), jnp.zeros((MODEL_DIMENSION, 3 * ADAPTER_RANK), jnp.float32))
    (grad_normed, grad_down), ignored = lax.scan(back_group, start_back, collected_pieces)
    grad_in = norm_back(tok_float, input_norm_gain, grad_normed).astype(jnp.bfloat16)
    return (layer_out, grad_in, grad_down, query_up_gradient, key_up_gradient, value_up_gradient, grad_down_out, output_up_gradient)
```

```python
import jax
import jax.numpy as jnp
from jax import lax
from jax.sharding import PartitionSpec as P

WINDOW = 1024


epsilon = 1e-06
adapter_scale = 2.0
score_scale = 168.0 ** (-0.5)


def passed_along(value, axis, steps):
    count = lax.axis_size(axis)
    leading, last = (max(0, -steps), min(count, count - steps))
    return lax.ppermute(value, axis, [(source, source + steps) for source in range(leading, last)])


def norm_rows(source, gain_vec):
    inverse = lax.rsqrt(jnp.mean(source * source, axis=-1, keepdims=True) + epsilon)
    return source * inverse * gain_vec


def norm_back(source, gain_vec, incoming):
    inverse = lax.rsqrt(jnp.mean(source * source, axis=-1, keepdims=True) + epsilon)
    scaled = source * inverse
    upward = incoming * gain_vec
    return inverse * (upward - scaled * jnp.mean(upward * scaled, axis=-1, keepdims=True))


def matrix_product(first_op, second_op):
    return jnp.dot(first_op, second_op, preferred_element_type=jnp.float32)


def multiply_by_transpose(first_op, second_op):
    return lax.dot_general(
        first_op, second_op, (((1,), (1,)), ((), ())), preferred_element_type=jnp.float32
    )


def transpose_multiply(first_op, second_op):
    return lax.dot_general(
        first_op, second_op, (((0,), (0,)), ((), ())), preferred_element_type=jnp.float32
    )


def window_mask(query_segs, key_codes):
    query_count = query_segs.shape[0]
    key_total = key_codes.shape[0]
    distance = (key_total - query_count + jnp.arange(query_count))[:, None] - jnp.arange(key_total)[
        None, :
    ]
    same_doc = key_codes[None, :] == query_segs[:, None] + 1
    return (distance == 0) | (distance > 0) & (distance < WINDOW) & same_doc


def ctx_sum(parts):
    count = lax.axis_size("ctx")
    if count & (count - 1):
        return [lax.psum(p.astype(jnp.bfloat16), "ctx").astype(jnp.float32) for p in parts]
    flat = jnp.concatenate([p.astype(jnp.float32).reshape(-1) for p in parts])
    step = 1
    while step < count:
        flat = flat + lax.ppermute(flat, "ctx", [(i, i ^ step) for i in range(count)])
        step *= 2
    results, offset = [], 0
    for p in parts:
        results.append(flat[offset : offset + p.size].reshape(p.shape))
        offset += p.size
    return results


def on_device(
    tokens,
    output_gradient,
    document_index,
    real_token_count,
    input_norm_gain,
    query_norm_gain,
    key_norm_gain,
    output_norm_gain,
    query_projection,
    key_projection,
    value_projection,
    output_projection,
    adapter_down_maps,
    adapter_query_up,
    adapter_key_up,
    adapter_value_up,
    adapter_output_down,
    adapter_output_up,
):
    row_count, model_width = tokens.shape
    shard_len = document_index.shape[0]
    head_dim = key_projection.shape[1]
    adapter_product = adapter_key_up.shape[0]
    heads_here = query_projection.shape[1] // head_dim
    ctx_size = lax.axis_size("ctx")
    tp_index = lax.axis_index("tp")
    slice_width = model_width // lax.axis_size("tp")
    reach_shards = WINDOW // shard_len
    send_count = min(reach_shards, ctx_size - 1)
    tok_float = tokens.astype(jnp.float32)
    normed_rows = norm_rows(tok_float, input_norm_gain).astype(jnp.bfloat16)
    normalized_input = lax.all_gather(normed_rows, "tp", axis=0, tiled=True)
    middle_list = matrix_product(normalized_input, adapter_down_maps).astype(jnp.bfloat16)
    middle_query = middle_list[:, :adapter_product]
    middle_key = middle_list[:, adapter_product : 2 * adapter_product]
    middle_value = middle_list[:, 2 * adapter_product :]
    query_before_norm = matrix_product(
        normalized_input, query_projection
    ) + adapter_scale * matrix_product(middle_query, adapter_query_up)
    key_before_norm = matrix_product(
        normalized_input, key_projection
    ) + adapter_scale * matrix_product(middle_key, adapter_key_up)
    value_before_norm = matrix_product(
        normalized_input, value_projection
    ) + adapter_scale * matrix_product(middle_value, adapter_value_up)
    query_heads = query_before_norm.reshape(shard_len, heads_here, head_dim)
    query_normed = norm_rows(query_heads, query_norm_gain).astype(jnp.bfloat16)
    key_normed = norm_rows(key_before_norm, key_norm_gain).astype(jnp.bfloat16)
    value_cast = value_before_norm.astype(jnp.bfloat16)
    positions = jnp.arange(shard_len)
    is_valid = positions < real_token_count[0]
    valid_rows = is_valid.astype(jnp.float32)
    local_codes = jnp.where(is_valid, document_index + 1, 0)
    local_pair = jnp.concatenate([key_normed, value_cast], axis=1)
    received = []
    for hop_index in range(1, send_count + 1):
        received.append(passed_along((local_pair, local_codes), "ctx", hop_index))
    missing = reach_shards - send_count
    blank_pair = jnp.zeros_like(local_pair)
    blank_codes = jnp.zeros_like(local_codes)
    earlier = [(blank_pair, blank_codes)] * missing + list(reversed(received))
    key_pairs = jnp.concatenate([entry[0] for entry in earlier] + [local_pair], axis=0)
    key_codes_all = jnp.concatenate([entry[1] for entry in earlier] + [local_codes], axis=0)
    keys_all = key_pairs[:, :head_dim]
    values_all = key_pairs[:, head_dim:]
    allowed = window_mask(document_index, key_codes_all)
    scores = (
        jnp.einsum("thd,sd->hts", query_normed, keys_all, preferred_element_type=jnp.float32)
        * score_scale
    )
    weights = jnp.where(allowed[None], jnp.exp(scores), 0.0)
    attn_probs = weights / jnp.sum(weights, axis=-1, keepdims=True)
    probs_cast = attn_probs.astype(jnp.bfloat16)
    attention_result = jnp.einsum(
        "hts,sd->thd", probs_cast, values_all, preferred_element_type=jnp.float32
    )
    attention_result = (
        (attention_result * valid_rows[:, None, None])
        .astype(jnp.bfloat16)
        .reshape(shard_len, heads_here * head_dim)
    )
    part_out = matrix_product(attention_result, output_projection)
    partial_middle = matrix_product(attention_result, adapter_output_down)
    output_total, mid_sum = (
        lax.psum_scatter(
            part_out.astype(jnp.bfloat16), "tp", scatter_dimension=0, tiled=True
        ).astype(jnp.float32),
        lax.psum_scatter(
            partial_middle.astype(jnp.bfloat16), "tp", scatter_dimension=0, tiled=True
        ).astype(jnp.float32),
    )
    middle_output = mid_sum.astype(jnp.bfloat16)
    apply_prenorm = output_total + adapter_scale * matrix_product(middle_output, adapter_output_up)
    layer_out = norm_rows(apply_prenorm, output_norm_gain).astype(jnp.bfloat16)
    prenorm_gradient = norm_back(
        apply_prenorm, output_norm_gain, output_gradient.astype(jnp.float32)
    ).astype(jnp.bfloat16)
    middle_output_gradient = (
        adapter_scale * multiply_by_transpose(prenorm_gradient, adapter_output_up)
    ).astype(jnp.bfloat16)
    complete_gradient, middle_complete_gradient, middle_complete = (
        lax.all_gather(prenorm_gradient, "tp", axis=0, tiled=True),
        lax.all_gather(middle_output_gradient, "tp", axis=0, tiled=True),
        lax.all_gather(middle_output, "tp", axis=0, tiled=True),
    )
    gradient_portion = lax.dynamic_slice_in_dim(
        complete_gradient, tp_index * slice_width, slice_width, 1
    )
    output_up_contribution = adapter_scale * transpose_multiply(middle_complete, gradient_portion)
    attention_gradient = multiply_by_transpose(
        complete_gradient, output_projection
    ) + multiply_by_transpose(middle_complete_gradient, adapter_output_down)
    attention_gradient = (attention_gradient * valid_rows[:, None]).astype(jnp.bfloat16)
    down_out_term = transpose_multiply(attention_result, middle_complete_gradient)
    grad_heads = attention_gradient.reshape(shard_len, heads_here, head_dim)
    grad_probs = jnp.einsum(
        "thd,sd->hts", grad_heads, values_all, preferred_element_type=jnp.float32
    )
    inner_sum = jnp.sum(attn_probs * grad_probs, axis=-1, keepdims=True)
    grad_scores = (attn_probs * (grad_probs - inner_sum) * score_scale).astype(jnp.bfloat16)
    grad_query = jnp.einsum(
        "hts,sd->thd", grad_scores, keys_all, preferred_element_type=jnp.float32
    )
    grad_keys = jnp.einsum(
        "hts,thd->sd", grad_scores, query_normed, preferred_element_type=jnp.float32
    )
    grad_values = jnp.einsum(
        "hts,thd->sd", probs_cast, grad_heads, preferred_element_type=jnp.float32
    )
    grad_pairs = jnp.concatenate([grad_keys, grad_values], axis=1)
    own_grads = grad_pairs[reach_shards * shard_len :]
    for hop_index in range(1, send_count + 1):
        own_grads = own_grads + passed_along(
            grad_pairs[
                (reach_shards - hop_index) * shard_len : (reach_shards - hop_index + 1) * shard_len
            ].astype(jnp.bfloat16),
            "ctx",
            -hop_index,
        ).astype(jnp.float32)
    query_prenorm_gradient = (
        norm_back(query_heads, query_norm_gain, grad_query)
        .reshape(shard_len, heads_here * head_dim)
        .astype(jnp.bfloat16)
    )
    key_prenorm_gradient = norm_back(
        key_before_norm, key_norm_gain, own_grads[:, :head_dim]
    ).astype(jnp.bfloat16)
    value_prenorm_gradient = own_grads[:, head_dim:].astype(jnp.bfloat16)
    query_up_contribution = adapter_scale * transpose_multiply(middle_query, query_prenorm_gradient)
    key_up_contribution = adapter_scale * transpose_multiply(middle_key, key_prenorm_gradient)
    value_up_contribution = adapter_scale * transpose_multiply(middle_value, value_prenorm_gradient)
    middle_gradients = jnp.concatenate(
        [
            adapter_scale * multiply_by_transpose(query_prenorm_gradient, adapter_query_up),
            adapter_scale * multiply_by_transpose(key_prenorm_gradient, adapter_key_up),
            adapter_scale * multiply_by_transpose(value_prenorm_gradient, adapter_value_up),
        ],
        axis=1,
    ).astype(jnp.bfloat16)
    grad_normed = (
        multiply_by_transpose(query_prenorm_gradient, query_projection)
        + multiply_by_transpose(key_prenorm_gradient, key_projection)
        + multiply_by_transpose(value_prenorm_gradient, value_projection)
        + multiply_by_transpose(middle_gradients, adapter_down_maps)
    )
    grad_normed_rows = lax.psum_scatter(
        grad_normed.astype(jnp.bfloat16), "tp", scatter_dimension=0, tiled=True
    ).astype(jnp.float32)
    grad_in = norm_back(tok_float, input_norm_gain, grad_normed_rows).astype(jnp.bfloat16)
    down_term = lax.psum_scatter(
        transpose_multiply(normalized_input, middle_gradients).astype(jnp.bfloat16),
        "tp",
        scatter_dimension=0,
        tiled=True,
    )
    adapter_totals = ctx_sum(
        [
            down_term,
            query_up_contribution,
            key_up_contribution,
            value_up_contribution,
            down_out_term,
            output_up_contribution,
        ]
    )
    return (
        layer_out,
        grad_in,
        adapter_totals[0],
        adapter_totals[1],
        adapter_totals[2],
        adapter_totals[3],
        adapter_totals[4],
        adapter_totals[5],
    )


def solution(mesh):
    in_specs = (
        P(("groups", "ctx", "tp"), None),
        P(("groups", "ctx", "tp"), None),
        P(("groups", "ctx")),
        P(("groups", "ctx")),
        P(),
        P(),
        P(),
        P(),
        P(None, "tp"),
        P(None, "tp"),
        P(None, "tp"),
        P("tp", None),
        P(),
        P(None, "tp"),
        P(None, "tp"),
        P(None, "tp"),
        P("tp", None),
        P(),
    )
    out_specs = (
        P(("groups", "ctx", "tp"), None),
        P(("groups", "ctx", "tp"), None),
        P(("groups", "tp"), None),
        P("groups", "tp"),
        P("groups", "tp"),
        P("groups", "tp"),
        P(("groups", "tp"), None),
        P("groups", "tp"),
    )
    return jax.shard_map(
        on_device, mesh=mesh, in_specs=in_specs, out_specs=out_specs, check_vma=False
    )
```

```python
import jax
import jax.numpy as jnp
from jax import lax
from jax.sharding import PartitionSpec as P

WINDOW = 1024


epsilon = 1e-06
adapter_scale = 2.0
score_scale = 168.0 ** (-0.5)


def passed_along(value, axis, steps):
    count = lax.axis_size(axis)
    leading, last = (max(0, -steps), min(count, count - steps))
    return lax.ppermute(value, axis, [(source, source + steps) for source in range(leading, last)])


def norm_rows(source, gain_vec):
    inverse = lax.rsqrt(jnp.mean(source * source, axis=-1, keepdims=True) + epsilon)
    return source * inverse * gain_vec


def norm_back(source, gain_vec, incoming):
    inverse = lax.rsqrt(jnp.mean(source * source, axis=-1, keepdims=True) + epsilon)
    scaled = source * inverse
    upward = incoming * gain_vec
    return inverse * (upward - scaled * jnp.mean(upward * scaled, axis=-1, keepdims=True))


def matrix_product(first_op, second_op):
    return jnp.dot(first_op, second_op, preferred_element_type=jnp.float32)


def multiply_by_transpose(first_op, second_op):
    return lax.dot_general(
        first_op, second_op, (((1,), (1,)), ((), ())), preferred_element_type=jnp.float32
    )


def transpose_multiply(first_op, second_op):
    return lax.dot_general(
        first_op, second_op, (((0,), (0,)), ((), ())), preferred_element_type=jnp.float32
    )


def window_mask(query_segs, key_codes):
    query_count = query_segs.shape[0]
    key_total = key_codes.shape[0]
    distance = (key_total - query_count + jnp.arange(query_count))[:, None] - jnp.arange(key_total)[
        None, :
    ]
    same_doc = key_codes[None, :] == query_segs[:, None] + 1
    return (distance == 0) | (distance > 0) & (distance < WINDOW) & same_doc


def tp_sum_scatter(value):
    if lax.axis_size("tp") != 2:
        return lax.psum_scatter(value, "tp", scatter_dimension=0, tiled=True).astype(jnp.float32)
    half = value.shape[0] // 2
    tp_index = lax.axis_index("tp")
    mine = lax.dynamic_slice_in_dim(value, tp_index * half, half, 0)
    theirs = lax.dynamic_slice_in_dim(value, (1 - tp_index) * half, half, 0)
    received = lax.ppermute(theirs, "tp", [(0, 1), (1, 0)])
    return mine.astype(jnp.float32) + received.astype(jnp.float32)


def ctx_sum(parts):
    count = lax.axis_size("ctx")
    if count & (count - 1):
        return [lax.psum(p.astype(jnp.bfloat16), "ctx").astype(jnp.float32) for p in parts]
    flat = jnp.concatenate([p.astype(jnp.float32).reshape(-1) for p in parts])
    step = 1
    while step < count:
        flat = flat + lax.ppermute(flat, "ctx", [(i, i ^ step) for i in range(count)])
        step *= 2
    results, offset = [], 0
    for p in parts:
        results.append(flat[offset : offset + p.size].reshape(p.shape))
        offset += p.size
    return results


def on_device(
    tokens,
    output_gradient,
    document_index,
    real_token_count,
    input_norm_gain,
    query_norm_gain,
    key_norm_gain,
    output_norm_gain,
    query_projection,
    key_projection,
    value_projection,
    output_projection,
    adapter_down_maps,
    adapter_query_up,
    adapter_key_up,
    adapter_value_up,
    adapter_output_down,
    adapter_output_up,
):
    row_count, model_width = tokens.shape
    shard_len = document_index.shape[0]
    head_dim = key_projection.shape[1]
    adapter_product = adapter_key_up.shape[0]
    heads_here = query_projection.shape[1] // head_dim
    ctx_size = lax.axis_size("ctx")
    tp_index = lax.axis_index("tp")
    slice_width = model_width // lax.axis_size("tp")
    reach_shards = WINDOW // shard_len
    send_count = min(reach_shards, ctx_size - 1)
    tok_float = tokens.astype(jnp.float32)
    normed_rows = norm_rows(tok_float, input_norm_gain).astype(jnp.bfloat16)
    normalized_input = lax.all_gather(normed_rows, "tp", axis=0, tiled=True)
    middle_list = matrix_product(normalized_input, adapter_down_maps).astype(jnp.bfloat16)
    middle_query = middle_list[:, :adapter_product]
    middle_key = middle_list[:, adapter_product : 2 * adapter_product]
    middle_value = middle_list[:, 2 * adapter_product :]
    query_before_norm = matrix_product(
        normalized_input, query_projection
    ) + adapter_scale * matrix_product(middle_query, adapter_query_up)
    key_before_norm = matrix_product(
        normalized_input, key_projection
    ) + adapter_scale * matrix_product(middle_key, adapter_key_up)
    value_before_norm = matrix_product(
        normalized_input, value_projection
    ) + adapter_scale * matrix_product(middle_value, adapter_value_up)
    query_heads = query_before_norm.reshape(shard_len, heads_here, head_dim)
    query_normed = norm_rows(query_heads, query_norm_gain).astype(jnp.bfloat16)
    key_normed = norm_rows(key_before_norm, key_norm_gain).astype(jnp.bfloat16)
    value_cast = value_before_norm.astype(jnp.bfloat16)
    positions = jnp.arange(shard_len)
    is_valid = positions < real_token_count[0]
    valid_rows = is_valid.astype(jnp.float32)
    local_codes = jnp.where(is_valid, document_index + 1, 0)
    local_pair = jnp.concatenate([key_normed, value_cast], axis=1)
    received = []
    for hop_index in range(1, send_count + 1):
        received.append(passed_along((local_pair, local_codes), "ctx", hop_index))
    missing = reach_shards - send_count
    blank_pair = jnp.zeros_like(local_pair)
    blank_codes = jnp.zeros_like(local_codes)
    earlier = [(blank_pair, blank_codes)] * missing + list(reversed(received))
    key_pairs = jnp.concatenate([entry[0] for entry in earlier] + [local_pair], axis=0)
    key_codes_all = jnp.concatenate([entry[1] for entry in earlier] + [local_codes], axis=0)
    keys_all = key_pairs[:, :head_dim]
    values_all = key_pairs[:, head_dim:]
    allowed = window_mask(document_index, key_codes_all)
    scores = (
        jnp.einsum("thd,sd->hts", query_normed, keys_all, preferred_element_type=jnp.float32)
        * score_scale
    )
    weights = jnp.where(allowed[None], jnp.exp(scores), 0.0)
    attn_probs = weights / jnp.sum(weights, axis=-1, keepdims=True)
    probs_cast = attn_probs.astype(jnp.bfloat16)
    attention_result = jnp.einsum(
        "hts,sd->thd", probs_cast, values_all, preferred_element_type=jnp.float32
    )
    attention_result = (
        (attention_result * valid_rows[:, None, None])
        .astype(jnp.bfloat16)
        .reshape(shard_len, heads_here * head_dim)
    )
    part_out = matrix_product(attention_result, output_projection)
    partial_middle = matrix_product(attention_result, adapter_output_down)
    output_total = tp_sum_scatter(part_out.astype(jnp.bfloat16))
    mid_sum = tp_sum_scatter(partial_middle.astype(jnp.bfloat16))
    middle_output = mid_sum.astype(jnp.bfloat16)
    apply_prenorm = output_total + adapter_scale * matrix_product(middle_output, adapter_output_up)
    layer_out = norm_rows(apply_prenorm, output_norm_gain).astype(jnp.bfloat16)
    prenorm_gradient = norm_back(
        apply_prenorm, output_norm_gain, output_gradient.astype(jnp.float32)
    ).astype(jnp.bfloat16)
    middle_output_gradient = (
        adapter_scale * multiply_by_transpose(prenorm_gradient, adapter_output_up)
    ).astype(jnp.bfloat16)
    complete_gradient, middle_complete_gradient, middle_complete = (
        lax.all_gather(prenorm_gradient, "tp", axis=0, tiled=True),
        lax.all_gather(middle_output_gradient, "tp", axis=0, tiled=True),
        lax.all_gather(middle_output, "tp", axis=0, tiled=True),
    )
    gradient_portion = lax.dynamic_slice_in_dim(
        complete_gradient, tp_index * slice_width, slice_width, 1
    )
    output_up_contribution = adapter_scale * transpose_multiply(middle_complete, gradient_portion)
    attention_gradient = multiply_by_transpose(
        complete_gradient, output_projection
    ) + multiply_by_transpose(middle_complete_gradient, adapter_output_down)
    attention_gradient = (attention_gradient * valid_rows[:, None]).astype(jnp.bfloat16)
    down_out_term = transpose_multiply(attention_result, middle_complete_gradient)
    grad_heads = attention_gradient.reshape(shard_len, heads_here, head_dim)
    grad_probs = jnp.einsum(
        "thd,sd->hts", grad_heads, values_all, preferred_element_type=jnp.float32
    )
    inner_sum = jnp.sum(attn_probs * grad_probs, axis=-1, keepdims=True)
    grad_scores = (attn_probs * (grad_probs - inner_sum) * score_scale).astype(jnp.bfloat16)
    grad_query = jnp.einsum(
        "hts,sd->thd", grad_scores, keys_all, preferred_element_type=jnp.float32
    )
    grad_keys = jnp.einsum(
        "hts,thd->sd", grad_scores, query_normed, preferred_element_type=jnp.float32
    )
    grad_values = jnp.einsum(
        "hts,thd->sd", probs_cast, grad_heads, preferred_element_type=jnp.float32
    )
    grad_pairs = jnp.concatenate([grad_keys, grad_values], axis=1)
    own_grads = grad_pairs[reach_shards * shard_len :]
    for hop_index in range(1, send_count + 1):
        own_grads = own_grads + passed_along(
            grad_pairs[
                (reach_shards - hop_index) * shard_len : (reach_shards - hop_index + 1) * shard_len
            ].astype(jnp.bfloat16),
            "ctx",
            -hop_index,
        ).astype(jnp.float32)
    query_prenorm_gradient = (
        norm_back(query_heads, query_norm_gain, grad_query)
        .reshape(shard_len, heads_here * head_dim)
        .astype(jnp.bfloat16)
    )
    key_prenorm_gradient = norm_back(
        key_before_norm, key_norm_gain, own_grads[:, :head_dim]
    ).astype(jnp.bfloat16)
    value_prenorm_gradient = own_grads[:, head_dim:].astype(jnp.bfloat16)
    query_up_contribution = adapter_scale * transpose_multiply(middle_query, query_prenorm_gradient)
    key_up_contribution = adapter_scale * transpose_multiply(middle_key, key_prenorm_gradient)
    value_up_contribution = adapter_scale * transpose_multiply(middle_value, value_prenorm_gradient)
    middle_gradients = jnp.concatenate(
        [
            adapter_scale * multiply_by_transpose(query_prenorm_gradient, adapter_query_up),
            adapter_scale * multiply_by_transpose(key_prenorm_gradient, adapter_key_up),
            adapter_scale * multiply_by_transpose(value_prenorm_gradient, adapter_value_up),
        ],
        axis=1,
    ).astype(jnp.bfloat16)
    grad_normed = (
        multiply_by_transpose(query_prenorm_gradient, query_projection)
        + multiply_by_transpose(key_prenorm_gradient, key_projection)
        + multiply_by_transpose(value_prenorm_gradient, value_projection)
        + multiply_by_transpose(middle_gradients, adapter_down_maps)
    )
    grad_normed_rows = tp_sum_scatter(grad_normed.astype(jnp.bfloat16))
    grad_in = norm_back(tok_float, input_norm_gain, grad_normed_rows).astype(jnp.bfloat16)
    down_term = lax.psum_scatter(
        transpose_multiply(normalized_input, middle_gradients).astype(jnp.bfloat16),
        "tp",
        scatter_dimension=0,
        tiled=True,
    )
    adapter_totals = ctx_sum(
        [
            down_term,
            query_up_contribution,
            key_up_contribution,
            value_up_contribution,
            down_out_term,
            output_up_contribution,
        ]
    )
    return (
        layer_out,
        grad_in,
        adapter_totals[0],
        adapter_totals[1],
        adapter_totals[2],
        adapter_totals[3],
        adapter_totals[4],
        adapter_totals[5],
    )


def solution(mesh):
    in_specs = (
        P(("groups", "ctx", "tp"), None),
        P(("groups", "ctx", "tp"), None),
        P(("groups", "ctx")),
        P(("groups", "ctx")),
        P(),
        P(),
        P(),
        P(),
        P(None, "tp"),
        P(None, "tp"),
        P(None, "tp"),
        P("tp", None),
        P(),
        P(None, "tp"),
        P(None, "tp"),
        P(None, "tp"),
        P("tp", None),
        P(),
    )
    out_specs = (
        P(("groups", "ctx", "tp"), None),
        P(("groups", "ctx", "tp"), None),
        P(("groups", "tp"), None),
        P("groups", "tp"),
        P("groups", "tp"),
        P("groups", "tp"),
        P(("groups", "tp"), None),
        P("groups", "tp"),
    )
    return jax.shard_map(
        on_device, mesh=mesh, in_specs=in_specs, out_specs=out_specs, check_vma=False
    )
```

```python
import jax
import jax.numpy as jnp
from jax import lax
from jax.sharding import PartitionSpec as P

WINDOW = 1024


epsilon = 1e-06
adapter_scale = 2.0
score_scale = 168.0 ** (-0.5)


def passed_along(value, axis, steps):
    count = lax.axis_size(axis)
    leading, last = (max(0, -steps), min(count, count - steps))
    return lax.ppermute(value, axis, [(source, source + steps) for source in range(leading, last)])


def norm_rows(source, gain_vec):
    inverse = lax.rsqrt(jnp.mean(source * source, axis=-1, keepdims=True) + epsilon)
    return source * inverse * gain_vec


def norm_back(source, gain_vec, incoming):
    inverse = lax.rsqrt(jnp.mean(source * source, axis=-1, keepdims=True) + epsilon)
    scaled = source * inverse
    upward = incoming * gain_vec
    return inverse * (upward - scaled * jnp.mean(upward * scaled, axis=-1, keepdims=True))


def matrix_product(first_op, second_op):
    return jnp.dot(first_op, second_op, preferred_element_type=jnp.float32)


def multiply_by_transpose(first_op, second_op):
    return lax.dot_general(
        first_op, second_op, (((1,), (1,)), ((), ())), preferred_element_type=jnp.float32
    )


def transpose_multiply(first_op, second_op):
    return lax.dot_general(
        first_op, second_op, (((0,), (0,)), ((), ())), preferred_element_type=jnp.float32
    )


def window_mask(query_segs, key_codes):
    query_count = query_segs.shape[0]
    key_total = key_codes.shape[0]
    distance = (key_total - query_count + jnp.arange(query_count))[:, None] - jnp.arange(key_total)[
        None, :
    ]
    same_doc = key_codes[None, :] == query_segs[:, None] + 1
    return (distance == 0) | (distance > 0) & (distance < WINDOW) & same_doc


def tp_sum_scatter(value):
    if lax.axis_size("tp") != 2:
        return lax.psum_scatter(value, "tp", scatter_dimension=0, tiled=True).astype(jnp.float32)
    half = value.shape[0] // 2
    tp_index = lax.axis_index("tp")
    mine = lax.dynamic_slice_in_dim(value, tp_index * half, half, 0)
    theirs = lax.dynamic_slice_in_dim(value, (1 - tp_index) * half, half, 0)
    received = lax.ppermute(theirs, "tp", [(0, 1), (1, 0)])
    return mine.astype(jnp.float32) + received.astype(jnp.float32)


def tp_gather(value):
    if lax.axis_size("tp") != 2:
        return lax.all_gather(value, "tp", axis=0, tiled=True)
    received = lax.ppermute(value, "tp", [(0, 1), (1, 0)])
    first = lax.axis_index("tp") == 0
    return jnp.concatenate(
        [jnp.where(first, value, received), jnp.where(first, received, value)], axis=0
    )


def ctx_sum(parts):
    count = lax.axis_size("ctx")
    if count & (count - 1):
        return [lax.psum(p.astype(jnp.bfloat16), "ctx").astype(jnp.float32) for p in parts]
    flat = jnp.concatenate([p.astype(jnp.float32).reshape(-1) for p in parts])
    step = 1
    while step < count:
        flat = flat + lax.ppermute(flat, "ctx", [(i, i ^ step) for i in range(count)])
        step *= 2
    results, offset = [], 0
    for p in parts:
        results.append(flat[offset : offset + p.size].reshape(p.shape))
        offset += p.size
    return results


def on_device(
    tokens,
    output_gradient,
    document_index,
    real_token_count,
    input_norm_gain,
    query_norm_gain,
    key_norm_gain,
    output_norm_gain,
    query_projection,
    key_projection,
    value_projection,
    output_projection,
    adapter_down_maps,
    adapter_query_up,
    adapter_key_up,
    adapter_value_up,
    adapter_output_down,
    adapter_output_up,
):
    row_count, model_width = tokens.shape
    shard_len = document_index.shape[0]
    head_dim = key_projection.shape[1]
    adapter_product = adapter_key_up.shape[0]
    heads_here = query_projection.shape[1] // head_dim
    ctx_size = lax.axis_size("ctx")
    tp_index = lax.axis_index("tp")
    slice_width = model_width // lax.axis_size("tp")
    reach_shards = WINDOW // shard_len
    send_count = min(reach_shards, ctx_size - 1)
    tok_float = tokens.astype(jnp.float32)
    normed_rows = norm_rows(tok_float, input_norm_gain).astype(jnp.bfloat16)
    normalized_input = lax.all_gather(normed_rows, "tp", axis=0, tiled=True)
    middle_list = matrix_product(normalized_input, adapter_down_maps).astype(jnp.bfloat16)
    middle_query = middle_list[:, :adapter_product]
    middle_key = middle_list[:, adapter_product : 2 * adapter_product]
    middle_value = middle_list[:, 2 * adapter_product :]
    query_before_norm = matrix_product(
        normalized_input, query_projection
    ) + adapter_scale * matrix_product(middle_query, adapter_query_up)
    key_before_norm = matrix_product(
        normalized_input, key_projection
    ) + adapter_scale * matrix_product(middle_key, adapter_key_up)
    value_before_norm = matrix_product(
        normalized_input, value_projection
    ) + adapter_scale * matrix_product(middle_value, adapter_value_up)
    query_heads = query_before_norm.reshape(shard_len, heads_here, head_dim)
    query_normed = norm_rows(query_heads, query_norm_gain).astype(jnp.bfloat16)
    key_normed = norm_rows(key_before_norm, key_norm_gain).astype(jnp.bfloat16)
    value_cast = value_before_norm.astype(jnp.bfloat16)
    positions = jnp.arange(shard_len)
    is_valid = positions < real_token_count[0]
    valid_rows = is_valid.astype(jnp.float32)
    local_codes = jnp.where(is_valid, document_index + 1, 0)
    local_pair = jnp.concatenate([key_normed, value_cast], axis=1)
    received = []
    for hop_index in range(1, send_count + 1):
        received.append(passed_along((local_pair, local_codes), "ctx", hop_index))
    missing = reach_shards - send_count
    blank_pair = jnp.zeros_like(local_pair)
    blank_codes = jnp.zeros_like(local_codes)
    earlier = [(blank_pair, blank_codes)] * missing + list(reversed(received))
    key_pairs = jnp.concatenate([entry[0] for entry in earlier] + [local_pair], axis=0)
    key_codes_all = jnp.concatenate([entry[1] for entry in earlier] + [local_codes], axis=0)
    keys_all = key_pairs[:, :head_dim]
    values_all = key_pairs[:, head_dim:]
    allowed = window_mask(document_index, key_codes_all)
    scores = (
        jnp.einsum("thd,sd->hts", query_normed, keys_all, preferred_element_type=jnp.float32)
        * score_scale
    )
    weights = jnp.where(allowed[None], jnp.exp(scores), 0.0)
    attn_probs = weights / jnp.sum(weights, axis=-1, keepdims=True)
    probs_cast = attn_probs.astype(jnp.bfloat16)
    attention_result = jnp.einsum(
        "hts,sd->thd", probs_cast, values_all, preferred_element_type=jnp.float32
    )
    attention_result = (
        (attention_result * valid_rows[:, None, None])
        .astype(jnp.bfloat16)
        .reshape(shard_len, heads_here * head_dim)
    )
    part_out = matrix_product(attention_result, output_projection)
    partial_middle = matrix_product(attention_result, adapter_output_down)
    output_total = tp_sum_scatter(part_out.astype(jnp.bfloat16))
    mid_sum = tp_sum_scatter(partial_middle.astype(jnp.bfloat16))
    middle_output = mid_sum.astype(jnp.bfloat16)
    apply_prenorm = output_total + adapter_scale * matrix_product(middle_output, adapter_output_up)
    layer_out = norm_rows(apply_prenorm, output_norm_gain).astype(jnp.bfloat16)
    prenorm_gradient = norm_back(
        apply_prenorm, output_norm_gain, output_gradient.astype(jnp.float32)
    ).astype(jnp.bfloat16)
    middle_output_gradient = (
        adapter_scale * multiply_by_transpose(prenorm_gradient, adapter_output_up)
    ).astype(jnp.bfloat16)
    complete_gradient = tp_gather(prenorm_gradient)
    middle_pair = tp_gather(jnp.concatenate([middle_output_gradient, middle_output], axis=1))
    middle_complete_gradient = middle_pair[:, :adapter_product]
    middle_complete = middle_pair[:, adapter_product:]
    gradient_portion = lax.dynamic_slice_in_dim(
        complete_gradient, tp_index * slice_width, slice_width, 1
    )
    output_up_contribution = adapter_scale * transpose_multiply(middle_complete, gradient_portion)
    attention_gradient = multiply_by_transpose(
        complete_gradient, output_projection
    ) + multiply_by_transpose(middle_complete_gradient, adapter_output_down)
    attention_gradient = (attention_gradient * valid_rows[:, None]).astype(jnp.bfloat16)
    down_out_term = transpose_multiply(attention_result, middle_complete_gradient)
    grad_heads = attention_gradient.reshape(shard_len, heads_here, head_dim)
    grad_probs = jnp.einsum(
        "thd,sd->hts", grad_heads, values_all, preferred_element_type=jnp.float32
    )
    inner_sum = jnp.sum(attn_probs * grad_probs, axis=-1, keepdims=True)
    grad_scores = (attn_probs * (grad_probs - inner_sum) * score_scale).astype(jnp.bfloat16)
    grad_query = jnp.einsum(
        "hts,sd->thd", grad_scores, keys_all, preferred_element_type=jnp.float32
    )
    grad_keys = jnp.einsum(
        "hts,thd->sd", grad_scores, query_normed, preferred_element_type=jnp.float32
    )
    grad_values = jnp.einsum(
        "hts,thd->sd", probs_cast, grad_heads, preferred_element_type=jnp.float32
    )
    grad_pairs = jnp.concatenate([grad_keys, grad_values], axis=1)
    own_grads = grad_pairs[reach_shards * shard_len :]
    for hop_index in range(1, send_count + 1):
        own_grads = own_grads + passed_along(
            grad_pairs[
                (reach_shards - hop_index) * shard_len : (reach_shards - hop_index + 1) * shard_len
            ].astype(jnp.bfloat16),
            "ctx",
            -hop_index,
        ).astype(jnp.float32)
    query_prenorm_gradient = (
        norm_back(query_heads, query_norm_gain, grad_query)
        .reshape(shard_len, heads_here * head_dim)
        .astype(jnp.bfloat16)
    )
    key_prenorm_gradient = norm_back(
        key_before_norm, key_norm_gain, own_grads[:, :head_dim]
    ).astype(jnp.bfloat16)
    value_prenorm_gradient = own_grads[:, head_dim:].astype(jnp.bfloat16)
    query_up_contribution = adapter_scale * transpose_multiply(middle_query, query_prenorm_gradient)
    key_up_contribution = adapter_scale * transpose_multiply(middle_key, key_prenorm_gradient)
    value_up_contribution = adapter_scale * transpose_multiply(middle_value, value_prenorm_gradient)
    middle_gradients = jnp.concatenate(
        [
            adapter_scale * multiply_by_transpose(query_prenorm_gradient, adapter_query_up),
            adapter_scale * multiply_by_transpose(key_prenorm_gradient, adapter_key_up),
            adapter_scale * multiply_by_transpose(value_prenorm_gradient, adapter_value_up),
        ],
        axis=1,
    ).astype(jnp.bfloat16)
    grad_normed = (
        multiply_by_transpose(query_prenorm_gradient, query_projection)
        + multiply_by_transpose(key_prenorm_gradient, key_projection)
        + multiply_by_transpose(value_prenorm_gradient, value_projection)
        + multiply_by_transpose(middle_gradients, adapter_down_maps)
    )
    grad_normed_rows = tp_sum_scatter(grad_normed.astype(jnp.bfloat16))
    grad_in = norm_back(tok_float, input_norm_gain, grad_normed_rows).astype(jnp.bfloat16)
    down_term = tp_sum_scatter(
        transpose_multiply(normalized_input, middle_gradients).astype(jnp.bfloat16)
    )
    adapter_totals = ctx_sum(
        [
            down_term,
            query_up_contribution,
            key_up_contribution,
            value_up_contribution,
            down_out_term,
            output_up_contribution,
        ]
    )
    return (
        layer_out,
        grad_in,
        adapter_totals[0],
        adapter_totals[1],
        adapter_totals[2],
        adapter_totals[3],
        adapter_totals[4],
        adapter_totals[5],
    )


def solution(mesh):
    in_specs = (
        P(("groups", "ctx", "tp"), None),
        P(("groups", "ctx", "tp"), None),
        P(("groups", "ctx")),
        P(("groups", "ctx")),
        P(),
        P(),
        P(),
        P(),
        P(None, "tp"),
        P(None, "tp"),
        P(None, "tp"),
        P("tp", None),
        P(),
        P(None, "tp"),
        P(None, "tp"),
        P(None, "tp"),
        P("tp", None),
        P(),
    )
    out_specs = (
        P(("groups", "ctx", "tp"), None),
        P(("groups", "ctx", "tp"), None),
        P(("groups", "tp"), None),
        P("groups", "tp"),
        P("groups", "tp"),
        P("groups", "tp"),
        P(("groups", "tp"), None),
        P("groups", "tp"),
    )
    return jax.shard_map(
        on_device, mesh=mesh, in_specs=in_specs, out_specs=out_specs, check_vma=False
    )
```

```python
import jax
import jax.numpy as jnp
from jax import lax
from jax.sharding import PartitionSpec as P

WINDOW = 1024


epsilon = 1e-06
adapter_scale = 2.0
score_scale = 168.0 ** (-0.5)


def passed_along(value, axis, steps):
    count = lax.axis_size(axis)
    leading, last = (max(0, -steps), min(count, count - steps))
    return lax.ppermute(value, axis, [(source, source + steps) for source in range(leading, last)])


def norm_rows(source, gain_vec):
    inverse = lax.rsqrt(jnp.mean(source * source, axis=-1, keepdims=True) + epsilon)
    return source * inverse * gain_vec


def norm_back(source, gain_vec, incoming):
    inverse = lax.rsqrt(jnp.mean(source * source, axis=-1, keepdims=True) + epsilon)
    scaled = source * inverse
    upward = incoming * gain_vec
    return inverse * (upward - scaled * jnp.mean(upward * scaled, axis=-1, keepdims=True))


def matrix_product(first_op, second_op):
    return jnp.dot(first_op, second_op, preferred_element_type=jnp.float32)


def multiply_by_transpose(first_op, second_op):
    return lax.dot_general(
        first_op, second_op, (((1,), (1,)), ((), ())), preferred_element_type=jnp.float32
    )


def transpose_multiply(first_op, second_op):
    return lax.dot_general(
        first_op, second_op, (((0,), (0,)), ((), ())), preferred_element_type=jnp.float32
    )


def window_mask(query_segs, key_codes):
    query_count = query_segs.shape[0]
    key_total = key_codes.shape[0]
    distance = (key_total - query_count + jnp.arange(query_count))[:, None] - jnp.arange(key_total)[
        None, :
    ]
    same_doc = key_codes[None, :] == query_segs[:, None] + 1
    return (distance == 0) | (distance > 0) & (distance < WINDOW) & same_doc


def tp_sum_scatter(value):
    if lax.axis_size("tp") != 2:
        return lax.psum_scatter(value, "tp", scatter_dimension=0, tiled=True).astype(jnp.float32)
    half = value.shape[0] // 2
    tp_index = lax.axis_index("tp")
    mine = lax.dynamic_slice_in_dim(value, tp_index * half, half, 0)
    theirs = lax.dynamic_slice_in_dim(value, (1 - tp_index) * half, half, 0)
    received = lax.ppermute(theirs, "tp", [(0, 1), (1, 0)])
    return mine.astype(jnp.float32) + received.astype(jnp.float32)


def tp_gather(value):
    if lax.axis_size("tp") != 2:
        return lax.all_gather(value, "tp", axis=0, tiled=True)
    received = lax.ppermute(value, "tp", [(0, 1), (1, 0)])
    first = lax.axis_index("tp") == 0
    return jnp.concatenate(
        [jnp.where(first, value, received), jnp.where(first, received, value)], axis=0
    )


def ctx_sum(parts):
    count = lax.axis_size("ctx")
    if count & (count - 1):
        return [lax.psum(p.astype(jnp.bfloat16), "ctx").astype(jnp.float32) for p in parts]
    flat = jnp.concatenate([p.astype(jnp.float32).reshape(-1) for p in parts])
    step = 1
    while step < count:
        sent = flat.astype(jnp.bfloat16)
        received = lax.ppermute(sent, "ctx", [(i, i ^ step) for i in range(count)])
        flat = sent.astype(jnp.float32) + received.astype(jnp.float32)
        step *= 2
    results, offset = [], 0
    for p in parts:
        results.append(flat[offset : offset + p.size].reshape(p.shape))
        offset += p.size
    return results


def on_device(
    tokens,
    output_gradient,
    document_index,
    real_token_count,
    input_norm_gain,
    query_norm_gain,
    key_norm_gain,
    output_norm_gain,
    query_projection,
    key_projection,
    value_projection,
    output_projection,
    adapter_down_maps,
    adapter_query_up,
    adapter_key_up,
    adapter_value_up,
    adapter_output_down,
    adapter_output_up,
):
    row_count, model_width = tokens.shape
    shard_len = document_index.shape[0]
    head_dim = key_projection.shape[1]
    adapter_product = adapter_key_up.shape[0]
    heads_here = query_projection.shape[1] // head_dim
    ctx_size = lax.axis_size("ctx")
    tp_index = lax.axis_index("tp")
    slice_width = model_width // lax.axis_size("tp")
    reach_shards = WINDOW // shard_len
    send_count = min(reach_shards, ctx_size - 1)
    tok_float = tokens.astype(jnp.float32)
    normed_rows = norm_rows(tok_float, input_norm_gain).astype(jnp.bfloat16)
    normalized_input = lax.all_gather(normed_rows, "tp", axis=0, tiled=True)
    middle_list = matrix_product(normalized_input, adapter_down_maps).astype(jnp.bfloat16)
    middle_query = middle_list[:, :adapter_product]
    middle_key = middle_list[:, adapter_product : 2 * adapter_product]
    middle_value = middle_list[:, 2 * adapter_product :]
    query_before_norm = matrix_product(
        normalized_input, query_projection
    ) + adapter_scale * matrix_product(middle_query, adapter_query_up)
    key_before_norm = matrix_product(
        normalized_input, key_projection
    ) + adapter_scale * matrix_product(middle_key, adapter_key_up)
    value_before_norm = matrix_product(
        normalized_input, value_projection
    ) + adapter_scale * matrix_product(middle_value, adapter_value_up)
    query_heads = query_before_norm.reshape(shard_len, heads_here, head_dim)
    query_normed = norm_rows(query_heads, query_norm_gain).astype(jnp.bfloat16)
    key_normed = norm_rows(key_before_norm, key_norm_gain).astype(jnp.bfloat16)
    value_cast = value_before_norm.astype(jnp.bfloat16)
    positions = jnp.arange(shard_len)
    is_valid = positions < real_token_count[0]
    valid_rows = is_valid.astype(jnp.float32)
    local_codes = jnp.where(is_valid, document_index + 1, 0)
    local_pair = jnp.concatenate([key_normed, value_cast], axis=1)
    received = []
    for hop_index in range(1, send_count + 1):
        received.append(passed_along((local_pair, local_codes), "ctx", hop_index))
    missing = reach_shards - send_count
    blank_pair = jnp.zeros_like(local_pair)
    blank_codes = jnp.zeros_like(local_codes)
    earlier = [(blank_pair, blank_codes)] * missing + list(reversed(received))
    key_pairs = jnp.concatenate([entry[0] for entry in earlier] + [local_pair], axis=0)
    key_codes_all = jnp.concatenate([entry[1] for entry in earlier] + [local_codes], axis=0)
    keys_all = key_pairs[:, :head_dim]
    values_all = key_pairs[:, head_dim:]
    allowed = window_mask(document_index, key_codes_all)
    scores = (
        jnp.einsum("thd,sd->hts", query_normed, keys_all, preferred_element_type=jnp.float32)
        * score_scale
    )
    weights = jnp.where(allowed[None], jnp.exp(scores), 0.0)
    attn_probs = weights / jnp.sum(weights, axis=-1, keepdims=True)
    probs_cast = attn_probs.astype(jnp.bfloat16)
    attention_result = jnp.einsum(
        "hts,sd->thd", probs_cast, values_all, preferred_element_type=jnp.float32
    )
    attention_result = (
        (attention_result * valid_rows[:, None, None])
        .astype(jnp.bfloat16)
        .reshape(shard_len, heads_here * head_dim)
    )
    part_out = matrix_product(attention_result, output_projection)
    partial_middle = matrix_product(attention_result, adapter_output_down)
    output_total = tp_sum_scatter(part_out.astype(jnp.bfloat16))
    mid_sum = tp_sum_scatter(partial_middle.astype(jnp.bfloat16))
    middle_output = mid_sum.astype(jnp.bfloat16)
    apply_prenorm = output_total + adapter_scale * matrix_product(middle_output, adapter_output_up)
    layer_out = norm_rows(apply_prenorm, output_norm_gain).astype(jnp.bfloat16)
    prenorm_gradient = norm_back(
        apply_prenorm, output_norm_gain, output_gradient.astype(jnp.float32)
    ).astype(jnp.bfloat16)
    middle_output_gradient = (
        adapter_scale * multiply_by_transpose(prenorm_gradient, adapter_output_up)
    ).astype(jnp.bfloat16)
    complete_gradient = tp_gather(prenorm_gradient)
    middle_pair = tp_gather(jnp.concatenate([middle_output_gradient, middle_output], axis=1))
    middle_complete_gradient = middle_pair[:, :adapter_product]
    middle_complete = middle_pair[:, adapter_product:]
    gradient_portion = lax.dynamic_slice_in_dim(
        complete_gradient, tp_index * slice_width, slice_width, 1
    )
    output_up_contribution = adapter_scale * transpose_multiply(middle_complete, gradient_portion)
    attention_gradient = multiply_by_transpose(
        complete_gradient, output_projection
    ) + multiply_by_transpose(middle_complete_gradient, adapter_output_down)
    attention_gradient = (attention_gradient * valid_rows[:, None]).astype(jnp.bfloat16)
    down_out_term = transpose_multiply(attention_result, middle_complete_gradient)
    grad_heads = attention_gradient.reshape(shard_len, heads_here, head_dim)
    grad_probs = jnp.einsum(
        "thd,sd->hts", grad_heads, values_all, preferred_element_type=jnp.float32
    )
    inner_sum = jnp.sum(attn_probs * grad_probs, axis=-1, keepdims=True)
    grad_scores = (attn_probs * (grad_probs - inner_sum) * score_scale).astype(jnp.bfloat16)
    grad_query = jnp.einsum(
        "hts,sd->thd", grad_scores, keys_all, preferred_element_type=jnp.float32
    )
    grad_keys = jnp.einsum(
        "hts,thd->sd", grad_scores, query_normed, preferred_element_type=jnp.float32
    )
    grad_values = jnp.einsum(
        "hts,thd->sd", probs_cast, grad_heads, preferred_element_type=jnp.float32
    )
    grad_pairs = jnp.concatenate([grad_keys, grad_values], axis=1)
    own_grads = grad_pairs[reach_shards * shard_len :]
    for hop_index in range(1, send_count + 1):
        own_grads = own_grads + passed_along(
            grad_pairs[
                (reach_shards - hop_index) * shard_len : (reach_shards - hop_index + 1) * shard_len
            ].astype(jnp.bfloat16),
            "ctx",
            -hop_index,
        ).astype(jnp.float32)
    query_prenorm_gradient = (
        norm_back(query_heads, query_norm_gain, grad_query)
        .reshape(shard_len, heads_here * head_dim)
        .astype(jnp.bfloat16)
    )
    key_prenorm_gradient = norm_back(
        key_before_norm, key_norm_gain, own_grads[:, :head_dim]
    ).astype(jnp.bfloat16)
    value_prenorm_gradient = own_grads[:, head_dim:].astype(jnp.bfloat16)
    query_up_contribution = adapter_scale * transpose_multiply(middle_query, query_prenorm_gradient)
    key_up_contribution = adapter_scale * transpose_multiply(middle_key, key_prenorm_gradient)
    value_up_contribution = adapter_scale * transpose_multiply(middle_value, value_prenorm_gradient)
    middle_gradients = jnp.concatenate(
        [
            adapter_scale * multiply_by_transpose(query_prenorm_gradient, adapter_query_up),
            adapter_scale * multiply_by_transpose(key_prenorm_gradient, adapter_key_up),
            adapter_scale * multiply_by_transpose(value_prenorm_gradient, adapter_value_up),
        ],
        axis=1,
    ).astype(jnp.bfloat16)
    grad_normed = (
        multiply_by_transpose(query_prenorm_gradient, query_projection)
        + multiply_by_transpose(key_prenorm_gradient, key_projection)
        + multiply_by_transpose(value_prenorm_gradient, value_projection)
        + multiply_by_transpose(middle_gradients, adapter_down_maps)
    )
    grad_normed_rows = tp_sum_scatter(grad_normed.astype(jnp.bfloat16))
    grad_in = norm_back(tok_float, input_norm_gain, grad_normed_rows).astype(jnp.bfloat16)
    down_term = tp_sum_scatter(
        transpose_multiply(normalized_input, middle_gradients).astype(jnp.bfloat16)
    )
    adapter_totals = ctx_sum(
        [
            down_term,
            query_up_contribution,
            key_up_contribution,
            value_up_contribution,
            down_out_term,
            output_up_contribution,
        ]
    )
    return (
        layer_out,
        grad_in,
        adapter_totals[0],
        adapter_totals[1],
        adapter_totals[2],
        adapter_totals[3],
        adapter_totals[4],
        adapter_totals[5],
    )


def solution(mesh):
    in_specs = (
        P(("groups", "ctx", "tp"), None),
        P(("groups", "ctx", "tp"), None),
        P(("groups", "ctx")),
        P(("groups", "ctx")),
        P(),
        P(),
        P(),
        P(),
        P(None, "tp"),
        P(None, "tp"),
        P(None, "tp"),
        P("tp", None),
        P(),
        P(None, "tp"),
        P(None, "tp"),
        P(None, "tp"),
        P("tp", None),
        P(),
    )
    out_specs = (
        P(("groups", "ctx", "tp"), None),
        P(("groups", "ctx", "tp"), None),
        P(("groups", "tp"), None),
        P("groups", "tp"),
        P("groups", "tp"),
        P("groups", "tp"),
        P(("groups", "tp"), None),
        P("groups", "tp"),
    )
    return jax.shard_map(
        on_device, mesh=mesh, in_specs=in_specs, out_specs=out_specs, check_vma=False
    )
```

```python
import jax
import jax.numpy as jnp
from jax import lax
from jax.sharding import PartitionSpec as P

WINDOW = 1024


epsilon = 1e-06
adapter_scale = 2.0
score_scale = 168.0 ** (-0.5)


def passed_along(value, axis, steps):
    count = lax.axis_size(axis)
    leading, last = (max(0, -steps), min(count, count - steps))
    return lax.ppermute(value, axis, [(source, source + steps) for source in range(leading, last)])


def norm_rows(source, gain_vec):
    inverse = lax.rsqrt(jnp.mean(source * source, axis=-1, keepdims=True) + epsilon)
    return source * inverse * gain_vec


def norm_back(source, gain_vec, incoming):
    inverse = lax.rsqrt(jnp.mean(source * source, axis=-1, keepdims=True) + epsilon)
    scaled = source * inverse
    upward = incoming * gain_vec
    return inverse * (upward - scaled * jnp.mean(upward * scaled, axis=-1, keepdims=True))


def matrix_product(first_op, second_op):
    return jnp.dot(first_op, second_op, preferred_element_type=jnp.float32)


def multiply_by_transpose(first_op, second_op):
    return lax.dot_general(
        first_op, second_op, (((1,), (1,)), ((), ())), preferred_element_type=jnp.float32
    )


def transpose_multiply(first_op, second_op):
    return lax.dot_general(
        first_op, second_op, (((0,), (0,)), ((), ())), preferred_element_type=jnp.float32
    )


def window_mask(query_segs, key_codes):
    query_count = query_segs.shape[0]
    key_total = key_codes.shape[0]
    distance = (key_total - query_count + jnp.arange(query_count))[:, None] - jnp.arange(key_total)[
        None, :
    ]
    same_doc = key_codes[None, :] == query_segs[:, None] + 1
    return (distance == 0) | (distance > 0) & (distance < WINDOW) & same_doc


def tp_sum_scatter(value):
    if lax.axis_size("tp") != 2:
        return lax.psum_scatter(value, "tp", scatter_dimension=0, tiled=True).astype(jnp.float32)
    half = value.shape[0] // 2
    tp_index = lax.axis_index("tp")
    mine = lax.dynamic_slice_in_dim(value, tp_index * half, half, 0)
    theirs = lax.dynamic_slice_in_dim(value, (1 - tp_index) * half, half, 0)
    received = lax.ppermute(theirs, "tp", [(0, 1), (1, 0)])
    return mine.astype(jnp.float32) + received.astype(jnp.float32)


def tp_gather(value):
    if lax.axis_size("tp") != 2:
        return lax.all_gather(value, "tp", axis=0, tiled=True)
    received = lax.ppermute(value, "tp", [(0, 1), (1, 0)])
    first = lax.axis_index("tp") == 0
    return jnp.concatenate(
        [jnp.where(first, value, received), jnp.where(first, received, value)], axis=0
    )


def ctx_sum(parts):
    count = lax.axis_size("ctx")
    if count & (count - 1):
        return [lax.psum(p.astype(jnp.bfloat16), "ctx").astype(jnp.float32) for p in parts]
    flat = jnp.concatenate([p.astype(jnp.float32).reshape(-1) for p in parts])
    step = 1
    while step < count:
        sent = flat.astype(jnp.bfloat16)
        received = lax.ppermute(sent, "ctx", [(i, i ^ step) for i in range(count)])
        flat = sent.astype(jnp.float32) + received.astype(jnp.float32)
        step *= 2
    results, offset = [], 0
    for p in parts:
        results.append(flat[offset : offset + p.size].reshape(p.shape))
        offset += p.size
    return results


def on_device(
    tokens,
    output_gradient,
    document_index,
    real_token_count,
    input_norm_gain,
    query_norm_gain,
    key_norm_gain,
    output_norm_gain,
    query_projection,
    key_projection,
    value_projection,
    output_projection,
    adapter_down_maps,
    adapter_query_up,
    adapter_key_up,
    adapter_value_up,
    adapter_output_down,
    adapter_output_up,
):
    row_count, model_width = tokens.shape
    shard_len = document_index.shape[0]
    head_dim = key_projection.shape[1]
    adapter_product = adapter_key_up.shape[0]
    heads_here = query_projection.shape[1] // head_dim
    ctx_size = lax.axis_size("ctx")
    tp_index = lax.axis_index("tp")
    slice_width = model_width // lax.axis_size("tp")
    reach_shards = WINDOW // shard_len
    send_count = min(reach_shards, ctx_size - 1)
    tok_float = tokens.astype(jnp.float32)
    normed_rows = norm_rows(tok_float, input_norm_gain).astype(jnp.bfloat16)
    normalized_input = lax.all_gather(normed_rows, "tp", axis=0, tiled=True)
    middle_list = matrix_product(normalized_input, adapter_down_maps).astype(jnp.bfloat16)
    middle_query = middle_list[:, :adapter_product]
    middle_key = middle_list[:, adapter_product : 2 * adapter_product]
    middle_value = middle_list[:, 2 * adapter_product :]
    query_before_norm = matrix_product(
        normalized_input, query_projection
    ) + adapter_scale * matrix_product(middle_query, adapter_query_up)
    key_before_norm = matrix_product(
        normalized_input, key_projection
    ) + adapter_scale * matrix_product(middle_key, adapter_key_up)
    value_before_norm = matrix_product(
        normalized_input, value_projection
    ) + adapter_scale * matrix_product(middle_value, adapter_value_up)
    query_heads = query_before_norm.reshape(shard_len, heads_here, head_dim)
    query_normed = norm_rows(query_heads, query_norm_gain).astype(jnp.bfloat16)
    key_normed = norm_rows(key_before_norm, key_norm_gain).astype(jnp.bfloat16)
    value_cast = value_before_norm.astype(jnp.bfloat16)
    positions = jnp.arange(shard_len)
    is_valid = positions < real_token_count[0]
    valid_rows = is_valid.astype(jnp.float32)
    local_codes = jnp.where(is_valid, document_index + 1, 0)
    local_pair = jnp.concatenate([key_normed, value_cast], axis=1)
    code_rows = jnp.zeros((16, local_pair.shape[1]), jnp.bfloat16)
    code_rows = code_rows.at[0, :shard_len].set(local_codes.astype(jnp.bfloat16))
    payload = jnp.concatenate([local_pair, code_rows], axis=0)
    received = []
    for hop_index in range(1, send_count + 1):
        arrived = passed_along(payload, "ctx", hop_index)
        received.append(
            (arrived[:shard_len], arrived[shard_len, :shard_len].astype(jnp.int32))
        )
    missing = reach_shards - send_count
    blank_pair = jnp.zeros_like(local_pair)
    blank_codes = jnp.zeros_like(local_codes)
    earlier = [(blank_pair, blank_codes)] * missing + list(reversed(received))
    key_pairs = jnp.concatenate([entry[0] for entry in earlier] + [local_pair], axis=0)
    key_codes_all = jnp.concatenate([entry[1] for entry in earlier] + [local_codes], axis=0)
    keys_all = key_pairs[:, :head_dim]
    values_all = key_pairs[:, head_dim:]
    allowed = window_mask(document_index, key_codes_all)
    scores = (
        jnp.einsum("thd,sd->hts", query_normed, keys_all, preferred_element_type=jnp.float32)
        * score_scale
    )
    weights = jnp.where(allowed[None], jnp.exp(scores), 0.0)
    attn_probs = weights / jnp.sum(weights, axis=-1, keepdims=True)
    probs_cast = attn_probs.astype(jnp.bfloat16)
    attention_result = jnp.einsum(
        "hts,sd->thd", probs_cast, values_all, preferred_element_type=jnp.float32
    )
    attention_result = (
        (attention_result * valid_rows[:, None, None])
        .astype(jnp.bfloat16)
        .reshape(shard_len, heads_here * head_dim)
    )
    part_out = matrix_product(attention_result, output_projection)
    partial_middle = matrix_product(attention_result, adapter_output_down)
    output_total = tp_sum_scatter(part_out.astype(jnp.bfloat16))
    mid_sum = tp_sum_scatter(partial_middle.astype(jnp.bfloat16))
    middle_output = mid_sum.astype(jnp.bfloat16)
    apply_prenorm = output_total + adapter_scale * matrix_product(middle_output, adapter_output_up)
    layer_out = norm_rows(apply_prenorm, output_norm_gain).astype(jnp.bfloat16)
    prenorm_gradient = norm_back(
        apply_prenorm, output_norm_gain, output_gradient.astype(jnp.float32)
    ).astype(jnp.bfloat16)
    middle_output_gradient = (
        adapter_scale * multiply_by_transpose(prenorm_gradient, adapter_output_up)
    ).astype(jnp.bfloat16)
    complete_gradient = tp_gather(prenorm_gradient)
    middle_pair = tp_gather(jnp.concatenate([middle_output_gradient, middle_output], axis=1))
    middle_complete_gradient = middle_pair[:, :adapter_product]
    middle_complete = middle_pair[:, adapter_product:]
    gradient_portion = lax.dynamic_slice_in_dim(
        complete_gradient, tp_index * slice_width, slice_width, 1
    )
    output_up_contribution = adapter_scale * transpose_multiply(middle_complete, gradient_portion)
    attention_gradient = multiply_by_transpose(
        complete_gradient, output_projection
    ) + multiply_by_transpose(middle_complete_gradient, adapter_output_down)
    attention_gradient = (attention_gradient * valid_rows[:, None]).astype(jnp.bfloat16)
    down_out_term = transpose_multiply(attention_result, middle_complete_gradient)
    grad_heads = attention_gradient.reshape(shard_len, heads_here, head_dim)
    grad_probs = jnp.einsum(
        "thd,sd->hts", grad_heads, values_all, preferred_element_type=jnp.float32
    )
    inner_sum = jnp.sum(attn_probs * grad_probs, axis=-1, keepdims=True)
    grad_scores = (attn_probs * (grad_probs - inner_sum) * score_scale).astype(jnp.bfloat16)
    grad_query = jnp.einsum(
        "hts,sd->thd", grad_scores, keys_all, preferred_element_type=jnp.float32
    )
    grad_keys = jnp.einsum(
        "hts,thd->sd", grad_scores, query_normed, preferred_element_type=jnp.float32
    )
    grad_values = jnp.einsum(
        "hts,thd->sd", probs_cast, grad_heads, preferred_element_type=jnp.float32
    )
    grad_pairs = jnp.concatenate([grad_keys, grad_values], axis=1)
    own_grads = grad_pairs[reach_shards * shard_len :]
    for hop_index in range(1, send_count + 1):
        own_grads = own_grads + passed_along(
            grad_pairs[
                (reach_shards - hop_index) * shard_len : (reach_shards - hop_index + 1) * shard_len
            ].astype(jnp.bfloat16),
            "ctx",
            -hop_index,
        ).astype(jnp.float32)
    query_prenorm_gradient = (
        norm_back(query_heads, query_norm_gain, grad_query)
        .reshape(shard_len, heads_here * head_dim)
        .astype(jnp.bfloat16)
    )
    key_prenorm_gradient = norm_back(
        key_before_norm, key_norm_gain, own_grads[:, :head_dim]
    ).astype(jnp.bfloat16)
    value_prenorm_gradient = own_grads[:, head_dim:].astype(jnp.bfloat16)
    query_up_contribution = adapter_scale * transpose_multiply(middle_query, query_prenorm_gradient)
    key_up_contribution = adapter_scale * transpose_multiply(middle_key, key_prenorm_gradient)
    value_up_contribution = adapter_scale * transpose_multiply(middle_value, value_prenorm_gradient)
    middle_gradients = jnp.concatenate(
        [
            adapter_scale * multiply_by_transpose(query_prenorm_gradient, adapter_query_up),
            adapter_scale * multiply_by_transpose(key_prenorm_gradient, adapter_key_up),
            adapter_scale * multiply_by_transpose(value_prenorm_gradient, adapter_value_up),
        ],
        axis=1,
    ).astype(jnp.bfloat16)
    grad_normed = (
        multiply_by_transpose(query_prenorm_gradient, query_projection)
        + multiply_by_transpose(key_prenorm_gradient, key_projection)
        + multiply_by_transpose(value_prenorm_gradient, value_projection)
        + multiply_by_transpose(middle_gradients, adapter_down_maps)
    )
    grad_normed_rows = tp_sum_scatter(grad_normed.astype(jnp.bfloat16))
    grad_in = norm_back(tok_float, input_norm_gain, grad_normed_rows).astype(jnp.bfloat16)
    down_term = tp_sum_scatter(
        transpose_multiply(normalized_input, middle_gradients).astype(jnp.bfloat16)
    )
    adapter_totals = ctx_sum(
        [
            down_term,
            query_up_contribution,
            key_up_contribution,
            value_up_contribution,
            down_out_term,
            output_up_contribution,
        ]
    )
    return (
        layer_out,
        grad_in,
        adapter_totals[0],
        adapter_totals[1],
        adapter_totals[2],
        adapter_totals[3],
        adapter_totals[4],
        adapter_totals[5],
    )


def solution(mesh):
    in_specs = (
        P(("groups", "ctx", "tp"), None),
        P(("groups", "ctx", "tp"), None),
        P(("groups", "ctx")),
        P(("groups", "ctx")),
        P(),
        P(),
        P(),
        P(),
        P(None, "tp"),
        P(None, "tp"),
        P(None, "tp"),
        P("tp", None),
        P(),
        P(None, "tp"),
        P(None, "tp"),
        P(None, "tp"),
        P("tp", None),
        P(),
    )
    out_specs = (
        P(("groups", "ctx", "tp"), None),
        P(("groups", "ctx", "tp"), None),
        P(("groups", "tp"), None),
        P("groups", "tp"),
        P("groups", "tp"),
        P("groups", "tp"),
        P(("groups", "tp"), None),
        P("groups", "tp"),
    )
    return jax.shard_map(
        on_device, mesh=mesh, in_specs=in_specs, out_specs=out_specs, check_vma=False
    )
```

```python
import jax
import jax.numpy as jnp
from jax import lax
from jax.sharding import PartitionSpec as P

WINDOW = 1024


epsilon = 1e-06
adapter_scale = 2.0
score_scale = 168.0 ** (-0.5)


def passed_along(value, axis, steps):
    count = lax.axis_size(axis)
    leading, last = (max(0, -steps), min(count, count - steps))
    return lax.ppermute(value, axis, [(source, source + steps) for source in range(leading, last)])


def norm_rows(source, gain_vec):
    inverse = lax.rsqrt(jnp.mean(source * source, axis=-1, keepdims=True) + epsilon)
    return source * inverse * gain_vec


def norm_back(source, gain_vec, incoming):
    inverse = lax.rsqrt(jnp.mean(source * source, axis=-1, keepdims=True) + epsilon)
    scaled = source * inverse
    upward = incoming * gain_vec
    return inverse * (upward - scaled * jnp.mean(upward * scaled, axis=-1, keepdims=True))


def matrix_product(first_op, second_op):
    return jnp.dot(first_op, second_op, preferred_element_type=jnp.float32)


def multiply_by_transpose(first_op, second_op):
    return lax.dot_general(
        first_op, second_op, (((1,), (1,)), ((), ())), preferred_element_type=jnp.float32
    )


def transpose_multiply(first_op, second_op):
    return lax.dot_general(
        first_op, second_op, (((0,), (0,)), ((), ())), preferred_element_type=jnp.float32
    )


def window_mask(query_segs, key_codes):
    query_count = query_segs.shape[0]
    key_total = key_codes.shape[0]
    distance = (key_total - query_count + jnp.arange(query_count))[:, None] - jnp.arange(key_total)[
        None, :
    ]
    same_doc = key_codes[None, :] == query_segs[:, None] + 1
    return (distance == 0) | (distance > 0) & (distance < WINDOW) & same_doc


def tp_sum_scatter(value):
    if lax.axis_size("tp") != 2:
        return lax.psum_scatter(value, "tp", scatter_dimension=0, tiled=True).astype(jnp.float32)
    half = value.shape[0] // 2
    tp_index = lax.axis_index("tp")
    mine = lax.dynamic_slice_in_dim(value, tp_index * half, half, 0)
    theirs = lax.dynamic_slice_in_dim(value, (1 - tp_index) * half, half, 0)
    received = lax.ppermute(theirs, "tp", [(0, 1), (1, 0)])
    return mine.astype(jnp.float32) + received.astype(jnp.float32)


def tp_gather(value):
    if lax.axis_size("tp") != 2:
        return lax.all_gather(value, "tp", axis=0, tiled=True)
    received = lax.ppermute(value, "tp", [(0, 1), (1, 0)])
    first = lax.axis_index("tp") == 0
    return jnp.concatenate(
        [jnp.where(first, value, received), jnp.where(first, received, value)], axis=0
    )


def ctx_sum(parts):
    count = lax.axis_size("ctx")
    if count & (count - 1):
        return [lax.psum(p.astype(jnp.bfloat16), "ctx").astype(jnp.float32) for p in parts]
    flat = jnp.concatenate([p.astype(jnp.float32).reshape(-1) for p in parts])
    step = 1
    while step < count:
        sent = flat.astype(jnp.bfloat16)
        received = lax.ppermute(sent, "ctx", [(i, i ^ step) for i in range(count)])
        flat = sent.astype(jnp.float32) + received.astype(jnp.float32)
        step *= 2
    results, offset = [], 0
    for p in parts:
        results.append(flat[offset : offset + p.size].reshape(p.shape))
        offset += p.size
    return results


def on_device(
    tokens,
    output_gradient,
    document_index,
    real_token_count,
    input_norm_gain,
    query_norm_gain,
    key_norm_gain,
    output_norm_gain,
    query_projection,
    key_projection,
    value_projection,
    output_projection,
    adapter_down_maps,
    adapter_query_up,
    adapter_key_up,
    adapter_value_up,
    adapter_output_down,
    adapter_output_up,
):
    row_count, model_width = tokens.shape
    shard_len = document_index.shape[0]
    head_dim = key_projection.shape[1]
    adapter_product = adapter_key_up.shape[0]
    heads_here = query_projection.shape[1] // head_dim
    ctx_size = lax.axis_size("ctx")
    tp_index = lax.axis_index("tp")
    slice_width = model_width // lax.axis_size("tp")
    reach_shards = WINDOW // shard_len
    send_count = min(reach_shards, ctx_size - 1)
    tok_float = tokens.astype(jnp.float32)
    normed_rows = norm_rows(tok_float, input_norm_gain).astype(jnp.bfloat16)
    normalized_input = tp_gather(normed_rows)
    middle_list = matrix_product(normalized_input, adapter_down_maps).astype(jnp.bfloat16)
    middle_query = middle_list[:, :adapter_product]
    middle_key = middle_list[:, adapter_product : 2 * adapter_product]
    middle_value = middle_list[:, 2 * adapter_product :]
    query_before_norm = matrix_product(
        normalized_input, query_projection
    ) + adapter_scale * matrix_product(middle_query, adapter_query_up)
    key_before_norm = matrix_product(
        normalized_input, key_projection
    ) + adapter_scale * matrix_product(middle_key, adapter_key_up)
    value_before_norm = matrix_product(
        normalized_input, value_projection
    ) + adapter_scale * matrix_product(middle_value, adapter_value_up)
    query_heads = query_before_norm.reshape(shard_len, heads_here, head_dim)
    query_normed = norm_rows(query_heads, query_norm_gain).astype(jnp.bfloat16)
    key_normed = norm_rows(key_before_norm, key_norm_gain).astype(jnp.bfloat16)
    value_cast = value_before_norm.astype(jnp.bfloat16)
    positions = jnp.arange(shard_len)
    is_valid = positions < real_token_count[0]
    valid_rows = is_valid.astype(jnp.float32)
    local_codes = jnp.where(is_valid, document_index + 1, 0)
    local_pair = jnp.concatenate([key_normed, value_cast], axis=1)
    code_rows = jnp.zeros((16, local_pair.shape[1]), jnp.bfloat16)
    code_rows = code_rows.at[0, :shard_len].set(local_codes.astype(jnp.bfloat16))
    payload = jnp.concatenate([local_pair, code_rows], axis=0)
    received = []
    for hop_index in range(1, send_count + 1):
        arrived = passed_along(payload, "ctx", hop_index)
        received.append(
            (arrived[:shard_len], arrived[shard_len, :shard_len].astype(jnp.int32))
        )
    missing = reach_shards - send_count
    blank_pair = jnp.zeros_like(local_pair)
    blank_codes = jnp.zeros_like(local_codes)
    earlier = [(blank_pair, blank_codes)] * missing + list(reversed(received))
    key_pairs = jnp.concatenate([entry[0] for entry in earlier] + [local_pair], axis=0)
    key_codes_all = jnp.concatenate([entry[1] for entry in earlier] + [local_codes], axis=0)
    keys_all = key_pairs[:, :head_dim]
    values_all = key_pairs[:, head_dim:]
    allowed = window_mask(document_index, key_codes_all)
    scores = (
        jnp.einsum("thd,sd->hts", query_normed, keys_all, preferred_element_type=jnp.float32)
        * score_scale
    )
    weights = jnp.where(allowed[None], jnp.exp(scores), 0.0)
    attn_probs = weights / jnp.sum(weights, axis=-1, keepdims=True)
    probs_cast = attn_probs.astype(jnp.bfloat16)
    attention_result = jnp.einsum(
        "hts,sd->thd", probs_cast, values_all, preferred_element_type=jnp.float32
    )
    attention_result = (
        (attention_result * valid_rows[:, None, None])
        .astype(jnp.bfloat16)
        .reshape(shard_len, heads_here * head_dim)
    )
    part_out = matrix_product(attention_result, output_projection)
    partial_middle = matrix_product(attention_result, adapter_output_down)
    output_total = tp_sum_scatter(part_out.astype(jnp.bfloat16))
    mid_sum = tp_sum_scatter(partial_middle.astype(jnp.bfloat16))
    middle_output = mid_sum.astype(jnp.bfloat16)
    apply_prenorm = output_total + adapter_scale * matrix_product(middle_output, adapter_output_up)
    layer_out = norm_rows(apply_prenorm, output_norm_gain).astype(jnp.bfloat16)
    prenorm_gradient = norm_back(
        apply_prenorm, output_norm_gain, output_gradient.astype(jnp.float32)
    ).astype(jnp.bfloat16)
    middle_output_gradient = (
        adapter_scale * multiply_by_transpose(prenorm_gradient, adapter_output_up)
    ).astype(jnp.bfloat16)
    complete_gradient = tp_gather(prenorm_gradient)
    middle_pair = tp_gather(jnp.concatenate([middle_output_gradient, middle_output], axis=1))
    middle_complete_gradient = middle_pair[:, :adapter_product]
    middle_complete = middle_pair[:, adapter_product:]
    gradient_portion = lax.dynamic_slice_in_dim(
        complete_gradient, tp_index * slice_width, slice_width, 1
    )
    output_up_contribution = adapter_scale * transpose_multiply(middle_complete, gradient_portion)
    attention_gradient = multiply_by_transpose(
        complete_gradient, output_projection
    ) + multiply_by_transpose(middle_complete_gradient, adapter_output_down)
    attention_gradient = (attention_gradient * valid_rows[:, None]).astype(jnp.bfloat16)
    down_out_term = transpose_multiply(attention_result, middle_complete_gradient)
    grad_heads = attention_gradient.reshape(shard_len, heads_here, head_dim)
    grad_probs = jnp.einsum(
        "thd,sd->hts", grad_heads, values_all, preferred_element_type=jnp.float32
    )
    inner_sum = jnp.sum(attn_probs * grad_probs, axis=-1, keepdims=True)
    grad_scores = (attn_probs * (grad_probs - inner_sum) * score_scale).astype(jnp.bfloat16)
    grad_query = jnp.einsum(
        "hts,sd->thd", grad_scores, keys_all, preferred_element_type=jnp.float32
    )
    grad_keys = jnp.einsum(
        "hts,thd->sd", grad_scores, query_normed, preferred_element_type=jnp.float32
    )
    grad_values = jnp.einsum(
        "hts,thd->sd", probs_cast, grad_heads, preferred_element_type=jnp.float32
    )
    grad_pairs = jnp.concatenate([grad_keys, grad_values], axis=1)
    own_grads = grad_pairs[reach_shards * shard_len :]
    for hop_index in range(1, send_count + 1):
        own_grads = own_grads + passed_along(
            grad_pairs[
                (reach_shards - hop_index) * shard_len : (reach_shards - hop_index + 1) * shard_len
            ].astype(jnp.bfloat16),
            "ctx",
            -hop_index,
        ).astype(jnp.float32)
    query_prenorm_gradient = (
        norm_back(query_heads, query_norm_gain, grad_query)
        .reshape(shard_len, heads_here * head_dim)
        .astype(jnp.bfloat16)
    )
    key_prenorm_gradient = norm_back(
        key_before_norm, key_norm_gain, own_grads[:, :head_dim]
    ).astype(jnp.bfloat16)
    value_prenorm_gradient = own_grads[:, head_dim:].astype(jnp.bfloat16)
    query_up_contribution = adapter_scale * transpose_multiply(middle_query, query_prenorm_gradient)
    key_up_contribution = adapter_scale * transpose_multiply(middle_key, key_prenorm_gradient)
    value_up_contribution = adapter_scale * transpose_multiply(middle_value, value_prenorm_gradient)
    middle_gradients = jnp.concatenate(
        [
            adapter_scale * multiply_by_transpose(query_prenorm_gradient, adapter_query_up),
            adapter_scale * multiply_by_transpose(key_prenorm_gradient, adapter_key_up),
            adapter_scale * multiply_by_transpose(value_prenorm_gradient, adapter_value_up),
        ],
        axis=1,
    ).astype(jnp.bfloat16)
    grad_normed = (
        multiply_by_transpose(query_prenorm_gradient, query_projection)
        + multiply_by_transpose(key_prenorm_gradient, key_projection)
        + multiply_by_transpose(value_prenorm_gradient, value_projection)
        + multiply_by_transpose(middle_gradients, adapter_down_maps)
    )
    grad_normed_rows = tp_sum_scatter(grad_normed.astype(jnp.bfloat16))
    grad_in = norm_back(tok_float, input_norm_gain, grad_normed_rows).astype(jnp.bfloat16)
    down_term = tp_sum_scatter(
        transpose_multiply(normalized_input, middle_gradients).astype(jnp.bfloat16)
    )
    adapter_totals = ctx_sum(
        [
            down_term,
            query_up_contribution,
            key_up_contribution,
            value_up_contribution,
            down_out_term,
            output_up_contribution,
        ]
    )
    return (
        layer_out,
        grad_in,
        adapter_totals[0],
        adapter_totals[1],
        adapter_totals[2],
        adapter_totals[3],
        adapter_totals[4],
        adapter_totals[5],
    )


def solution(mesh):
    in_specs = (
        P(("groups", "ctx", "tp"), None),
        P(("groups", "ctx", "tp"), None),
        P(("groups", "ctx")),
        P(("groups", "ctx")),
        P(),
        P(),
        P(),
        P(),
        P(None, "tp"),
        P(None, "tp"),
        P(None, "tp"),
        P("tp", None),
        P(),
        P(None, "tp"),
        P(None, "tp"),
        P(None, "tp"),
        P("tp", None),
        P(),
    )
    out_specs = (
        P(("groups", "ctx", "tp"), None),
        P(("groups", "ctx", "tp"), None),
        P(("groups", "tp"), None),
        P("groups", "tp"),
        P("groups", "tp"),
        P("groups", "tp"),
        P(("groups", "tp"), None),
        P("groups", "tp"),
    )
    return jax.shard_map(
        on_device, mesh=mesh, in_specs=in_specs, out_specs=out_specs, check_vma=False
    )
```

```python
import jax
import jax.numpy as jnp
from jax import lax
from jax.sharding import PartitionSpec as P

WINDOW = 1024


epsilon = 1e-06
adapter_scale = 2.0
score_scale = 168.0 ** (-0.5)


def passed_along(value, axis, steps):
    count = lax.axis_size(axis)
    leading, last = (max(0, -steps), min(count, count - steps))
    return lax.ppermute(value, axis, [(source, source + steps) for source in range(leading, last)])


def norm_rows(source, gain_vec):
    inverse = lax.rsqrt(jnp.mean(source * source, axis=-1, keepdims=True) + epsilon)
    return source * inverse * gain_vec


def norm_back(source, gain_vec, incoming):
    inverse = lax.rsqrt(jnp.mean(source * source, axis=-1, keepdims=True) + epsilon)
    scaled = source * inverse
    upward = incoming * gain_vec
    return inverse * (upward - scaled * jnp.mean(upward * scaled, axis=-1, keepdims=True))


def matrix_product(first_op, second_op):
    return jnp.dot(first_op, second_op, preferred_element_type=jnp.float32)


def multiply_by_transpose(first_op, second_op):
    return lax.dot_general(
        first_op, second_op, (((1,), (1,)), ((), ())), preferred_element_type=jnp.float32
    )


def transpose_multiply(first_op, second_op):
    return lax.dot_general(
        first_op, second_op, (((0,), (0,)), ((), ())), preferred_element_type=jnp.float32
    )


def window_mask(query_segs, key_codes):
    query_count = query_segs.shape[0]
    key_total = key_codes.shape[0]
    distance = (key_total - query_count + jnp.arange(query_count))[:, None] - jnp.arange(key_total)[
        None, :
    ]
    same_doc = key_codes[None, :] == query_segs[:, None] + 1
    return (distance == 0) | (distance > 0) & (distance < WINDOW) & same_doc


def tp_sum_scatter(value):
    if lax.axis_size("tp") != 2:
        return lax.psum_scatter(value, "tp", scatter_dimension=0, tiled=True).astype(jnp.float32)
    half = value.shape[0] // 2
    tp_index = lax.axis_index("tp")
    mine = lax.dynamic_slice_in_dim(value, tp_index * half, half, 0)
    theirs = lax.dynamic_slice_in_dim(value, (1 - tp_index) * half, half, 0)
    received = lax.ppermute(theirs, "tp", [(0, 1), (1, 0)])
    return mine.astype(jnp.float32) + received.astype(jnp.float32)


def tp_gather(value):
    if lax.axis_size("tp") != 2:
        return lax.all_gather(value, "tp", axis=0, tiled=True)
    received = lax.ppermute(value, "tp", [(0, 1), (1, 0)])
    first = lax.axis_index("tp") == 0
    return jnp.concatenate(
        [jnp.where(first, value, received), jnp.where(first, received, value)], axis=0
    )


def ctx_sum(parts):
    count = lax.axis_size("ctx")
    if count & (count - 1):
        return [lax.psum(p.astype(jnp.bfloat16), "ctx").astype(jnp.float32) for p in parts]
    flat = jnp.concatenate([p.astype(jnp.float32).reshape(-1) for p in parts])
    step = 1
    while step < count:
        sent = flat.astype(jnp.bfloat16)
        received = lax.ppermute(sent, "ctx", [(i, i ^ step) for i in range(count)])
        flat = sent.astype(jnp.float32) + received.astype(jnp.float32)
        step *= 2
    results, offset = [], 0
    for p in parts:
        results.append(flat[offset : offset + p.size].reshape(p.shape))
        offset += p.size
    return results


def on_device(
    tokens,
    output_gradient,
    document_index,
    real_token_count,
    input_norm_gain,
    query_norm_gain,
    key_norm_gain,
    output_norm_gain,
    query_projection,
    key_projection,
    value_projection,
    output_projection,
    adapter_down_maps,
    adapter_query_up,
    adapter_key_up,
    adapter_value_up,
    adapter_output_down,
    adapter_output_up,
):
    row_count, model_width = tokens.shape
    shard_len = document_index.shape[0]
    head_dim = key_projection.shape[1]
    adapter_product = adapter_key_up.shape[0]
    heads_here = query_projection.shape[1] // head_dim
    ctx_size = lax.axis_size("ctx")
    tp_index = lax.axis_index("tp")
    slice_width = model_width // lax.axis_size("tp")
    reach_shards = WINDOW // shard_len
    send_count = min(reach_shards, ctx_size - 1)
    tok_float = tokens.astype(jnp.float32)
    normed_rows = norm_rows(tok_float, input_norm_gain).astype(jnp.bfloat16)
    normalized_input = tp_gather(normed_rows)
    middle_list = matrix_product(normalized_input, adapter_down_maps).astype(jnp.bfloat16)
    middle_query = middle_list[:, :adapter_product]
    middle_key = middle_list[:, adapter_product : 2 * adapter_product]
    middle_value = middle_list[:, 2 * adapter_product :]
    query_before_norm = matrix_product(
        normalized_input, query_projection
    ) + adapter_scale * matrix_product(middle_query, adapter_query_up)
    key_before_norm = matrix_product(
        normalized_input, key_projection
    ) + adapter_scale * matrix_product(middle_key, adapter_key_up)
    value_before_norm = matrix_product(
        normalized_input, value_projection
    ) + adapter_scale * matrix_product(middle_value, adapter_value_up)
    query_heads = query_before_norm.reshape(shard_len, heads_here, head_dim)
    query_normed = norm_rows(query_heads, query_norm_gain).astype(jnp.bfloat16)
    key_normed = norm_rows(key_before_norm, key_norm_gain).astype(jnp.bfloat16)
    value_cast = value_before_norm.astype(jnp.bfloat16)
    positions = jnp.arange(shard_len)
    is_valid = positions < real_token_count[0]
    valid_rows = is_valid.astype(jnp.float32)
    local_codes = jnp.where(is_valid, document_index + 1, 0)
    local_pair = jnp.concatenate([key_normed, value_cast], axis=1)
    code_rows = jnp.zeros((16, local_pair.shape[1]), jnp.bfloat16)
    code_rows = code_rows.at[0, :shard_len].set(local_codes.astype(jnp.bfloat16))
    payload = jnp.concatenate([local_pair, code_rows], axis=0)
    received = []
    for hop_index in range(1, send_count + 1):
        arrived = passed_along(payload, "ctx", hop_index)
        received.append(
            (arrived[:shard_len], arrived[shard_len, :shard_len].astype(jnp.int32))
        )
    missing = reach_shards - send_count
    blank_pair = jnp.zeros_like(local_pair)
    blank_codes = jnp.zeros_like(local_codes)
    earlier = [(blank_pair, blank_codes)] * missing + list(reversed(received))
    key_pairs = jnp.concatenate([entry[0] for entry in earlier] + [local_pair], axis=0)
    key_codes_all = jnp.concatenate([entry[1] for entry in earlier] + [local_codes], axis=0)
    keys_all = key_pairs[:, :head_dim]
    values_all = key_pairs[:, head_dim:]
    allowed = window_mask(document_index, key_codes_all)
    scores = (
        jnp.einsum("thd,sd->hts", query_normed, keys_all, preferred_element_type=jnp.float32)
        * score_scale
    )
    weights = jnp.where(allowed[None], jnp.exp(scores), 0.0)
    attn_probs = weights / jnp.sum(weights, axis=-1, keepdims=True)
    probs_cast = attn_probs.astype(jnp.bfloat16)
    attention_result = jnp.einsum(
        "hts,sd->thd", probs_cast, values_all, preferred_element_type=jnp.float32
    )
    attention_result = (
        (attention_result * valid_rows[:, None, None])
        .astype(jnp.bfloat16)
        .reshape(shard_len, heads_here * head_dim)
    )
    part_out = matrix_product(attention_result, output_projection)
    partial_middle = matrix_product(attention_result, adapter_output_down)
    output_total = tp_sum_scatter(part_out.astype(jnp.bfloat16))
    mid_sum = tp_sum_scatter(partial_middle.astype(jnp.bfloat16))
    middle_output = mid_sum.astype(jnp.bfloat16)
    apply_prenorm = output_total + adapter_scale * matrix_product(middle_output, adapter_output_up)
    layer_out = norm_rows(apply_prenorm, output_norm_gain).astype(jnp.bfloat16)
    prenorm_gradient = norm_back(
        apply_prenorm, output_norm_gain, output_gradient.astype(jnp.float32)
    ).astype(jnp.bfloat16)
    middle_output_gradient = (
        adapter_scale * multiply_by_transpose(prenorm_gradient, adapter_output_up)
    ).astype(jnp.bfloat16)
    complete_gradient = tp_gather(prenorm_gradient)
    middle_pair = tp_gather(jnp.concatenate([middle_output_gradient, middle_output], axis=1))
    middle_complete_gradient = middle_pair[:, :adapter_product]
    middle_complete = middle_pair[:, adapter_product:]
    gradient_portion = lax.dynamic_slice_in_dim(
        complete_gradient, tp_index * slice_width, slice_width, 1
    )
    output_up_contribution = adapter_scale * transpose_multiply(middle_complete, gradient_portion)
    attention_gradient = multiply_by_transpose(
        complete_gradient, output_projection
    ) + multiply_by_transpose(middle_complete_gradient, adapter_output_down)
    attention_gradient = (attention_gradient * valid_rows[:, None]).astype(jnp.bfloat16)
    down_out_term = transpose_multiply(attention_result, middle_complete_gradient)
    grad_heads = attention_gradient.reshape(shard_len, heads_here, head_dim)
    grad_probs = jnp.einsum(
        "thd,sd->hts", grad_heads, values_all, preferred_element_type=jnp.float32
    )
    inner_sum = jnp.sum(attn_probs * grad_probs, axis=-1, keepdims=True)
    grad_scores = (attn_probs * (grad_probs - inner_sum) * score_scale).astype(jnp.bfloat16)
    grad_query = jnp.einsum(
        "hts,sd->thd", grad_scores, keys_all, preferred_element_type=jnp.float32
    )
    grad_keys = jnp.einsum(
        "hts,thd->sd", grad_scores, query_normed, preferred_element_type=jnp.float32
    )
    grad_values = jnp.einsum(
        "hts,thd->sd", probs_cast, grad_heads, preferred_element_type=jnp.float32
    )
    grad_pairs = jnp.concatenate([grad_keys, grad_values], axis=1)
    own_grads = grad_pairs[reach_shards * shard_len :]

    def hop_block(hop_index):
        first_row = (reach_shards - hop_index) * shard_len
        return grad_pairs[first_row : first_row + shard_len]

    if send_count > 0:
        running = hop_block(send_count)
        for hop_index in range(send_count - 1, 0, -1):
            arrived = passed_along(running.astype(jnp.bfloat16), "ctx", -1)
            running = arrived.astype(jnp.float32) + hop_block(hop_index)
        arrived = passed_along(running.astype(jnp.bfloat16), "ctx", -1)
        own_grads = own_grads + arrived.astype(jnp.float32)
    query_prenorm_gradient = (
        norm_back(query_heads, query_norm_gain, grad_query)
        .reshape(shard_len, heads_here * head_dim)
        .astype(jnp.bfloat16)
    )
    key_prenorm_gradient = norm_back(
        key_before_norm, key_norm_gain, own_grads[:, :head_dim]
    ).astype(jnp.bfloat16)
    value_prenorm_gradient = own_grads[:, head_dim:].astype(jnp.bfloat16)
    query_up_contribution = adapter_scale * transpose_multiply(middle_query, query_prenorm_gradient)
    key_up_contribution = adapter_scale * transpose_multiply(middle_key, key_prenorm_gradient)
    value_up_contribution = adapter_scale * transpose_multiply(middle_value, value_prenorm_gradient)
    middle_gradients = jnp.concatenate(
        [
            adapter_scale * multiply_by_transpose(query_prenorm_gradient, adapter_query_up),
            adapter_scale * multiply_by_transpose(key_prenorm_gradient, adapter_key_up),
            adapter_scale * multiply_by_transpose(value_prenorm_gradient, adapter_value_up),
        ],
        axis=1,
    ).astype(jnp.bfloat16)
    grad_normed = (
        multiply_by_transpose(query_prenorm_gradient, query_projection)
        + multiply_by_transpose(key_prenorm_gradient, key_projection)
        + multiply_by_transpose(value_prenorm_gradient, value_projection)
        + multiply_by_transpose(middle_gradients, adapter_down_maps)
    )
    grad_normed_rows = tp_sum_scatter(grad_normed.astype(jnp.bfloat16))
    grad_in = norm_back(tok_float, input_norm_gain, grad_normed_rows).astype(jnp.bfloat16)
    down_term = tp_sum_scatter(
        transpose_multiply(normalized_input, middle_gradients).astype(jnp.bfloat16)
    )
    adapter_totals = ctx_sum(
        [
            down_term,
            query_up_contribution,
            key_up_contribution,
            value_up_contribution,
            down_out_term,
            output_up_contribution,
        ]
    )
    return (
        layer_out,
        grad_in,
        adapter_totals[0],
        adapter_totals[1],
        adapter_totals[2],
        adapter_totals[3],
        adapter_totals[4],
        adapter_totals[5],
    )


def solution(mesh):
    in_specs = (
        P(("groups", "ctx", "tp"), None),
        P(("groups", "ctx", "tp"), None),
        P(("groups", "ctx")),
        P(("groups", "ctx")),
        P(),
        P(),
        P(),
        P(),
        P(None, "tp"),
        P(None, "tp"),
        P(None, "tp"),
        P("tp", None),
        P(),
        P(None, "tp"),
        P(None, "tp"),
        P(None, "tp"),
        P("tp", None),
        P(),
    )
    out_specs = (
        P(("groups", "ctx", "tp"), None),
        P(("groups", "ctx", "tp"), None),
        P(("groups", "tp"), None),
        P("groups", "tp"),
        P("groups", "tp"),
        P("groups", "tp"),
        P(("groups", "tp"), None),
        P("groups", "tp"),
    )
    return jax.shard_map(
        on_device, mesh=mesh, in_specs=in_specs, out_specs=out_specs, check_vma=False
    )
```

```python
import jax
import jax.numpy as jnp
from jax import lax
from jax.sharding import PartitionSpec as P

WINDOW = 1024


epsilon = 1e-06
adapter_scale = 2.0
score_scale = 168.0 ** (-0.5)


def passed_along(value, axis, steps):
    count = lax.axis_size(axis)
    leading, last = (max(0, -steps), min(count, count - steps))
    return lax.ppermute(value, axis, [(source, source + steps) for source in range(leading, last)])


def norm_rows(source, gain_vec):
    inverse = lax.rsqrt(jnp.mean(source * source, axis=-1, keepdims=True) + epsilon)
    return source * inverse * gain_vec


def norm_back(source, gain_vec, incoming):
    inverse = lax.rsqrt(jnp.mean(source * source, axis=-1, keepdims=True) + epsilon)
    scaled = source * inverse
    upward = incoming * gain_vec
    return inverse * (upward - scaled * jnp.mean(upward * scaled, axis=-1, keepdims=True))


def matrix_product(first_op, second_op):
    return jnp.dot(first_op, second_op, preferred_element_type=jnp.float32)


def multiply_by_transpose(first_op, second_op):
    return lax.dot_general(
        first_op, second_op, (((1,), (1,)), ((), ())), preferred_element_type=jnp.float32
    )


def transpose_multiply(first_op, second_op):
    return lax.dot_general(
        first_op, second_op, (((0,), (0,)), ((), ())), preferred_element_type=jnp.float32
    )


def window_mask(query_segs, key_codes):
    query_count = query_segs.shape[0]
    key_total = key_codes.shape[0]
    distance = (key_total - query_count + jnp.arange(query_count))[:, None] - jnp.arange(key_total)[
        None, :
    ]
    same_doc = key_codes[None, :] == query_segs[:, None] + 1
    return (distance == 0) | (distance > 0) & (distance < WINDOW) & same_doc


def tp_sum_scatter(value):
    if lax.axis_size("tp") != 2:
        return lax.psum_scatter(value, "tp", scatter_dimension=0, tiled=True).astype(jnp.float32)
    half = value.shape[0] // 2
    tp_index = lax.axis_index("tp")
    mine = lax.dynamic_slice_in_dim(value, tp_index * half, half, 0)
    theirs = lax.dynamic_slice_in_dim(value, (1 - tp_index) * half, half, 0)
    received = lax.ppermute(theirs, "tp", [(0, 1), (1, 0)])
    return mine.astype(jnp.float32) + received.astype(jnp.float32)


def tp_gather(value):
    if lax.axis_size("tp") != 2:
        return lax.all_gather(value, "tp", axis=0, tiled=True)
    received = lax.ppermute(value, "tp", [(0, 1), (1, 0)])
    first = lax.axis_index("tp") == 0
    return jnp.concatenate(
        [jnp.where(first, value, received), jnp.where(first, received, value)], axis=0
    )


def ctx_sum(parts):
    count = lax.axis_size("ctx")
    if count & (count - 1):
        return [lax.psum(p.astype(jnp.bfloat16), "ctx").astype(jnp.float32) for p in parts]
    flat = jnp.concatenate([p.astype(jnp.float32).reshape(-1) for p in parts])
    step = 1
    while step < count:
        sent = flat.astype(jnp.bfloat16)
        received = lax.ppermute(sent, "ctx", [(i, i ^ step) for i in range(count)])
        flat = sent.astype(jnp.float32) + received.astype(jnp.float32)
        step *= 2
    results, offset = [], 0
    for p in parts:
        results.append(flat[offset : offset + p.size].reshape(p.shape))
        offset += p.size
    return results


def on_device(
    tokens,
    output_gradient,
    document_index,
    real_token_count,
    input_norm_gain,
    query_norm_gain,
    key_norm_gain,
    output_norm_gain,
    query_projection,
    key_projection,
    value_projection,
    output_projection,
    adapter_down_maps,
    adapter_query_up,
    adapter_key_up,
    adapter_value_up,
    adapter_output_down,
    adapter_output_up,
):
    row_count, model_width = tokens.shape
    shard_len = document_index.shape[0]
    head_dim = key_projection.shape[1]
    adapter_product = adapter_key_up.shape[0]
    heads_here = query_projection.shape[1] // head_dim
    ctx_size = lax.axis_size("ctx")
    tp_index = lax.axis_index("tp")
    slice_width = model_width // lax.axis_size("tp")
    reach_shards = WINDOW // shard_len
    send_count = min(reach_shards, ctx_size - 1)
    tok_float = tokens.astype(jnp.float32)
    normed_rows = norm_rows(tok_float, input_norm_gain).astype(jnp.bfloat16)
    normalized_input = tp_gather(normed_rows)
    middle_list = matrix_product(normalized_input, adapter_down_maps).astype(jnp.bfloat16)
    middle_query = middle_list[:, :adapter_product]
    middle_key = middle_list[:, adapter_product : 2 * adapter_product]
    middle_value = middle_list[:, 2 * adapter_product :]
    query_before_norm = matrix_product(
        normalized_input, query_projection
    ) + adapter_scale * matrix_product(middle_query, adapter_query_up)
    key_before_norm = matrix_product(
        normalized_input, key_projection
    ) + adapter_scale * matrix_product(middle_key, adapter_key_up)
    value_before_norm = matrix_product(
        normalized_input, value_projection
    ) + adapter_scale * matrix_product(middle_value, adapter_value_up)
    query_heads = query_before_norm.reshape(shard_len, heads_here, head_dim)
    query_normed = norm_rows(query_heads, query_norm_gain).astype(jnp.bfloat16)
    key_normed = norm_rows(key_before_norm, key_norm_gain).astype(jnp.bfloat16)
    value_cast = value_before_norm.astype(jnp.bfloat16)
    positions = jnp.arange(shard_len)
    is_valid = positions < real_token_count[0]
    valid_rows = is_valid.astype(jnp.float32)
    local_codes = jnp.where(is_valid, document_index + 1, 0)
    local_pair = jnp.concatenate([key_normed, value_cast], axis=1)
    code_rows = jnp.zeros((16, local_pair.shape[1]), jnp.bfloat16)
    code_rows = code_rows.at[0, :shard_len].set(local_codes.astype(jnp.bfloat16))
    payload = jnp.concatenate([local_pair, code_rows], axis=0)
    received = []
    for hop_index in range(1, send_count + 1):
        arrived = passed_along(payload, "ctx", hop_index)
        received.append(
            (arrived[:shard_len], arrived[shard_len, :shard_len].astype(jnp.int32))
        )
    missing = reach_shards - send_count
    blank_pair = jnp.zeros_like(local_pair)
    blank_codes = jnp.zeros_like(local_codes)
    earlier = [(blank_pair, blank_codes)] * missing + list(reversed(received))
    key_pairs = jnp.concatenate([entry[0] for entry in earlier] + [local_pair], axis=0)
    key_codes_all = jnp.concatenate([entry[1] for entry in earlier] + [local_codes], axis=0)
    keys_all = key_pairs[:, :head_dim]
    values_all = key_pairs[:, head_dim:]
    allowed = window_mask(document_index, key_codes_all)
    scores = (
        jnp.einsum("thd,sd->hts", query_normed, keys_all, preferred_element_type=jnp.float32)
        * score_scale
    )
    weights = jnp.where(allowed[None], jnp.exp(scores), 0.0)
    attn_probs = weights / jnp.sum(weights, axis=-1, keepdims=True)
    probs_cast = attn_probs.astype(jnp.bfloat16)
    attention_result = jnp.einsum(
        "hts,sd->thd", probs_cast, values_all, preferred_element_type=jnp.float32
    )
    attention_result = (
        (attention_result * valid_rows[:, None, None])
        .astype(jnp.bfloat16)
        .reshape(shard_len, heads_here * head_dim)
    )
    part_out = matrix_product(attention_result, output_projection)
    partial_middle = matrix_product(attention_result, adapter_output_down)
    output_total = tp_sum_scatter(part_out.astype(jnp.bfloat16))
    mid_sum = tp_sum_scatter(partial_middle.astype(jnp.bfloat16))
    middle_output = mid_sum.astype(jnp.bfloat16)
    apply_prenorm = output_total + adapter_scale * matrix_product(middle_output, adapter_output_up)
    layer_out = norm_rows(apply_prenorm, output_norm_gain).astype(jnp.bfloat16)
    prenorm_gradient = norm_back(
        apply_prenorm, output_norm_gain, output_gradient.astype(jnp.float32)
    ).astype(jnp.bfloat16)
    middle_output_gradient = (
        adapter_scale * multiply_by_transpose(prenorm_gradient, adapter_output_up)
    ).astype(jnp.bfloat16)
    complete_gradient = tp_gather(prenorm_gradient)
    middle_pair = tp_gather(jnp.concatenate([middle_output_gradient, middle_output], axis=1))
    middle_complete_gradient = middle_pair[:, :adapter_product]
    middle_complete = middle_pair[:, adapter_product:]
    gradient_portion = lax.dynamic_slice_in_dim(
        complete_gradient, tp_index * slice_width, slice_width, 1
    )
    output_up_contribution = adapter_scale * transpose_multiply(middle_complete, gradient_portion)
    attention_gradient = multiply_by_transpose(
        complete_gradient, output_projection
    ) + multiply_by_transpose(middle_complete_gradient, adapter_output_down)
    attention_gradient = (attention_gradient * valid_rows[:, None]).astype(jnp.bfloat16)
    down_out_term = transpose_multiply(attention_result, middle_complete_gradient)
    grad_heads = attention_gradient.reshape(shard_len, heads_here, head_dim)
    grad_probs = jnp.einsum(
        "thd,sd->hts", grad_heads, values_all, preferred_element_type=jnp.float32
    )
    inner_sum = jnp.sum(attn_probs * grad_probs, axis=-1, keepdims=True)
    grad_scores = lax.optimization_barrier(
        (attn_probs * (grad_probs - inner_sum) * score_scale).astype(jnp.bfloat16)
    )
    grad_query = jnp.einsum(
        "hts,sd->thd", grad_scores, keys_all, preferred_element_type=jnp.float32
    )
    grad_keys = jnp.einsum(
        "hts,thd->sd", grad_scores, query_normed, preferred_element_type=jnp.float32
    )
    grad_values = jnp.einsum(
        "hts,thd->sd", probs_cast, grad_heads, preferred_element_type=jnp.float32
    )
    grad_pairs = jnp.concatenate([grad_keys, grad_values], axis=1)
    own_grads = grad_pairs[reach_shards * shard_len :]
    for hop_index in range(1, send_count + 1):
        own_grads = own_grads + passed_along(
            grad_pairs[
                (reach_shards - hop_index) * shard_len : (reach_shards - hop_index + 1) * shard_len
            ].astype(jnp.bfloat16),
            "ctx",
            -hop_index,
        ).astype(jnp.float32)
    query_prenorm_gradient = (
        norm_back(query_heads, query_norm_gain, grad_query)
        .reshape(shard_len, heads_here * head_dim)
        .astype(jnp.bfloat16)
    )
    key_prenorm_gradient = norm_back(
        key_before_norm, key_norm_gain, own_grads[:, :head_dim]
    ).astype(jnp.bfloat16)
    value_prenorm_gradient = own_grads[:, head_dim:].astype(jnp.bfloat16)
    query_up_contribution = adapter_scale * transpose_multiply(middle_query, query_prenorm_gradient)
    key_up_contribution = adapter_scale * transpose_multiply(middle_key, key_prenorm_gradient)
    value_up_contribution = adapter_scale * transpose_multiply(middle_value, value_prenorm_gradient)
    middle_gradients = jnp.concatenate(
        [
            adapter_scale * multiply_by_transpose(query_prenorm_gradient, adapter_query_up),
            adapter_scale * multiply_by_transpose(key_prenorm_gradient, adapter_key_up),
            adapter_scale * multiply_by_transpose(value_prenorm_gradient, adapter_value_up),
        ],
        axis=1,
    ).astype(jnp.bfloat16)
    grad_normed = (
        multiply_by_transpose(query_prenorm_gradient, query_projection)
        + multiply_by_transpose(key_prenorm_gradient, key_projection)
        + multiply_by_transpose(value_prenorm_gradient, value_projection)
        + multiply_by_transpose(middle_gradients, adapter_down_maps)
    )
    grad_normed_rows = tp_sum_scatter(grad_normed.astype(jnp.bfloat16))
    grad_in = norm_back(tok_float, input_norm_gain, grad_normed_rows).astype(jnp.bfloat16)
    down_term = tp_sum_scatter(
        transpose_multiply(normalized_input, middle_gradients).astype(jnp.bfloat16)
    )
    adapter_totals = ctx_sum(
        [
            down_term,
            query_up_contribution,
            key_up_contribution,
            value_up_contribution,
            down_out_term,
            output_up_contribution,
        ]
    )
    return (
        layer_out,
        grad_in,
        adapter_totals[0],
        adapter_totals[1],
        adapter_totals[2],
        adapter_totals[3],
        adapter_totals[4],
        adapter_totals[5],
    )


def solution(mesh):
    in_specs = (
        P(("groups", "ctx", "tp"), None),
        P(("groups", "ctx", "tp"), None),
        P(("groups", "ctx")),
        P(("groups", "ctx")),
        P(),
        P(),
        P(),
        P(),
        P(None, "tp"),
        P(None, "tp"),
        P(None, "tp"),
        P("tp", None),
        P(),
        P(None, "tp"),
        P(None, "tp"),
        P(None, "tp"),
        P("tp", None),
        P(),
    )
    out_specs = (
        P(("groups", "ctx", "tp"), None),
        P(("groups", "ctx", "tp"), None),
        P(("groups", "tp"), None),
        P("groups", "tp"),
        P("groups", "tp"),
        P("groups", "tp"),
        P(("groups", "tp"), None),
        P("groups", "tp"),
    )
    return jax.shard_map(
        on_device, mesh=mesh, in_specs=in_specs, out_specs=out_specs, check_vma=False
    )
```

```python
import jax
import jax.numpy as jnp
from jax import lax
from jax.sharding import PartitionSpec as P

WINDOW = 1024


epsilon = 1e-06
adapter_scale = 2.0
score_scale = 168.0 ** (-0.5)


def passed_along(value, axis, steps):
    count = lax.axis_size(axis)
    leading, last = (max(0, -steps), min(count, count - steps))
    return lax.ppermute(value, axis, [(source, source + steps) for source in range(leading, last)])


def norm_rows(source, gain_vec):
    inverse = lax.rsqrt(jnp.mean(source * source, axis=-1, keepdims=True) + epsilon)
    return source * inverse * gain_vec


def norm_back(source, gain_vec, incoming):
    inverse = lax.rsqrt(jnp.mean(source * source, axis=-1, keepdims=True) + epsilon)
    scaled = source * inverse
    upward = incoming * gain_vec
    return inverse * (upward - scaled * jnp.mean(upward * scaled, axis=-1, keepdims=True))


def matrix_product(first_op, second_op):
    return jnp.dot(first_op, second_op, preferred_element_type=jnp.float32)


def multiply_by_transpose(first_op, second_op):
    return lax.dot_general(
        first_op, second_op, (((1,), (1,)), ((), ())), preferred_element_type=jnp.float32
    )


def transpose_multiply(first_op, second_op):
    return lax.dot_general(
        first_op, second_op, (((0,), (0,)), ((), ())), preferred_element_type=jnp.float32
    )


def window_mask(query_segs, key_codes):
    query_count = query_segs.shape[0]
    key_total = key_codes.shape[0]
    distance = (key_total - query_count + jnp.arange(query_count))[:, None] - jnp.arange(key_total)[
        None, :
    ]
    same_doc = key_codes[None, :] == query_segs[:, None] + 1
    return (distance == 0) | (distance > 0) & (distance < WINDOW) & same_doc


def tp_sum_scatter(value):
    if lax.axis_size("tp") != 2:
        return lax.psum_scatter(value, "tp", scatter_dimension=0, tiled=True).astype(jnp.float32)
    half = value.shape[0] // 2
    tp_index = lax.axis_index("tp")
    mine = lax.dynamic_slice_in_dim(value, tp_index * half, half, 0)
    theirs = lax.dynamic_slice_in_dim(value, (1 - tp_index) * half, half, 0)
    received = lax.ppermute(theirs, "tp", [(0, 1), (1, 0)])
    return mine.astype(jnp.float32) + received.astype(jnp.float32)


def tp_gather(value):
    if lax.axis_size("tp") != 2:
        return lax.all_gather(value, "tp", axis=0, tiled=True)
    received = lax.ppermute(value, "tp", [(0, 1), (1, 0)])
    first = lax.axis_index("tp") == 0
    return jnp.concatenate(
        [jnp.where(first, value, received), jnp.where(first, received, value)], axis=0
    )


def ctx_sum(parts):
    count = lax.axis_size("ctx")
    if count & (count - 1):
        return [lax.psum(p.astype(jnp.bfloat16), "ctx").astype(jnp.float32) for p in parts]
    flat = jnp.concatenate([p.astype(jnp.float32).reshape(-1) for p in parts])
    step = 1
    while step < count:
        sent = flat.astype(jnp.bfloat16)
        received = lax.ppermute(sent, "ctx", [(i, i ^ step) for i in range(count)])
        flat = sent.astype(jnp.float32) + received.astype(jnp.float32)
        step *= 2
    results, offset = [], 0
    for p in parts:
        results.append(flat[offset : offset + p.size].reshape(p.shape))
        offset += p.size
    return results


def on_device(
    tokens,
    output_gradient,
    document_index,
    real_token_count,
    input_norm_gain,
    query_norm_gain,
    key_norm_gain,
    output_norm_gain,
    query_projection,
    key_projection,
    value_projection,
    output_projection,
    adapter_down_maps,
    adapter_query_up,
    adapter_key_up,
    adapter_value_up,
    adapter_output_down,
    adapter_output_up,
):
    row_count, model_width = tokens.shape
    shard_len = document_index.shape[0]
    head_dim = key_projection.shape[1]
    adapter_product = adapter_key_up.shape[0]
    heads_here = query_projection.shape[1] // head_dim
    ctx_size = lax.axis_size("ctx")
    tp_index = lax.axis_index("tp")
    slice_width = model_width // lax.axis_size("tp")
    reach_shards = WINDOW // shard_len
    send_count = min(reach_shards, ctx_size - 1)
    tok_float = tokens.astype(jnp.float32)
    normed_rows = norm_rows(tok_float, input_norm_gain).astype(jnp.bfloat16)
    normalized_input = tp_gather(normed_rows)
    query_width = query_projection.shape[1]
    key_end = query_width + head_dim
    value_end = key_end + head_dim
    all_weights = jnp.concatenate(
        [query_projection, key_projection, value_projection, adapter_down_maps], axis=1
    )
    projected = matrix_product(normalized_input, all_weights)
    middle_list = projected[:, value_end:].astype(jnp.bfloat16)
    middle_query = middle_list[:, :adapter_product]
    middle_key = middle_list[:, adapter_product : 2 * adapter_product]
    middle_value = middle_list[:, 2 * adapter_product :]
    query_before_norm = projected[:, :query_width] + adapter_scale * matrix_product(
        middle_query, adapter_query_up
    )
    key_before_norm = projected[:, query_width:key_end] + adapter_scale * matrix_product(
        middle_key, adapter_key_up
    )
    value_before_norm = projected[:, key_end:value_end] + adapter_scale * matrix_product(
        middle_value, adapter_value_up
    )
    query_heads = query_before_norm.reshape(shard_len, heads_here, head_dim)
    query_normed = norm_rows(query_heads, query_norm_gain).astype(jnp.bfloat16)
    key_normed = norm_rows(key_before_norm, key_norm_gain).astype(jnp.bfloat16)
    value_cast = value_before_norm.astype(jnp.bfloat16)
    positions = jnp.arange(shard_len)
    is_valid = positions < real_token_count[0]
    valid_rows = is_valid.astype(jnp.float32)
    local_codes = jnp.where(is_valid, document_index + 1, 0)
    local_pair = jnp.concatenate([key_normed, value_cast], axis=1)
    code_rows = jnp.zeros((16, local_pair.shape[1]), jnp.bfloat16)
    code_rows = code_rows.at[0, :shard_len].set(local_codes.astype(jnp.bfloat16))
    payload = jnp.concatenate([local_pair, code_rows], axis=0)
    received = []
    for hop_index in range(1, send_count + 1):
        arrived = passed_along(payload, "ctx", hop_index)
        received.append(
            (arrived[:shard_len], arrived[shard_len, :shard_len].astype(jnp.int32))
        )
    missing = reach_shards - send_count
    blank_pair = jnp.zeros_like(local_pair)
    blank_codes = jnp.zeros_like(local_codes)
    earlier = [(blank_pair, blank_codes)] * missing + list(reversed(received))
    key_pairs = jnp.concatenate([entry[0] for entry in earlier] + [local_pair], axis=0)
    key_codes_all = jnp.concatenate([entry[1] for entry in earlier] + [local_codes], axis=0)
    keys_all = key_pairs[:, :head_dim]
    values_all = key_pairs[:, head_dim:]
    allowed = window_mask(document_index, key_codes_all)
    scores = (
        jnp.einsum("thd,sd->hts", query_normed, keys_all, preferred_element_type=jnp.float32)
        * score_scale
    )
    weights = jnp.where(allowed[None], jnp.exp(scores), 0.0)
    attn_probs = weights / jnp.sum(weights, axis=-1, keepdims=True)
    probs_cast = attn_probs.astype(jnp.bfloat16)
    attention_result = jnp.einsum(
        "hts,sd->thd", probs_cast, values_all, preferred_element_type=jnp.float32
    )
    attention_result = (
        (attention_result * valid_rows[:, None, None])
        .astype(jnp.bfloat16)
        .reshape(shard_len, heads_here * head_dim)
    )
    part_out = matrix_product(attention_result, output_projection)
    partial_middle = matrix_product(attention_result, adapter_output_down)
    output_total = tp_sum_scatter(part_out.astype(jnp.bfloat16))
    mid_sum = tp_sum_scatter(partial_middle.astype(jnp.bfloat16))
    middle_output = mid_sum.astype(jnp.bfloat16)
    apply_prenorm = output_total + adapter_scale * matrix_product(middle_output, adapter_output_up)
    layer_out = norm_rows(apply_prenorm, output_norm_gain).astype(jnp.bfloat16)
    prenorm_gradient = norm_back(
        apply_prenorm, output_norm_gain, output_gradient.astype(jnp.float32)
    ).astype(jnp.bfloat16)
    middle_output_gradient = (
        adapter_scale * multiply_by_transpose(prenorm_gradient, adapter_output_up)
    ).astype(jnp.bfloat16)
    complete_gradient = tp_gather(prenorm_gradient)
    middle_pair = tp_gather(jnp.concatenate([middle_output_gradient, middle_output], axis=1))
    middle_complete_gradient = middle_pair[:, :adapter_product]
    middle_complete = middle_pair[:, adapter_product:]
    gradient_portion = lax.dynamic_slice_in_dim(
        complete_gradient, tp_index * slice_width, slice_width, 1
    )
    output_up_contribution = adapter_scale * transpose_multiply(middle_complete, gradient_portion)
    attention_gradient = multiply_by_transpose(
        complete_gradient, output_projection
    ) + multiply_by_transpose(middle_complete_gradient, adapter_output_down)
    attention_gradient = (attention_gradient * valid_rows[:, None]).astype(jnp.bfloat16)
    down_out_term = transpose_multiply(attention_result, middle_complete_gradient)
    grad_heads = attention_gradient.reshape(shard_len, heads_here, head_dim)
    grad_probs = jnp.einsum(
        "thd,sd->hts", grad_heads, values_all, preferred_element_type=jnp.float32
    )
    inner_sum = jnp.sum(attn_probs * grad_probs, axis=-1, keepdims=True)
    grad_scores = lax.optimization_barrier(
        (attn_probs * (grad_probs - inner_sum) * score_scale).astype(jnp.bfloat16)
    )
    grad_query = jnp.einsum(
        "hts,sd->thd", grad_scores, keys_all, preferred_element_type=jnp.float32
    )
    grad_keys = jnp.einsum(
        "hts,thd->sd", grad_scores, query_normed, preferred_element_type=jnp.float32
    )
    grad_values = jnp.einsum(
        "hts,thd->sd", probs_cast, grad_heads, preferred_element_type=jnp.float32
    )
    grad_pairs = jnp.concatenate([grad_keys, grad_values], axis=1)
    own_grads = grad_pairs[reach_shards * shard_len :]
    for hop_index in range(1, send_count + 1):
        own_grads = own_grads + passed_along(
            grad_pairs[
                (reach_shards - hop_index) * shard_len : (reach_shards - hop_index + 1) * shard_len
            ].astype(jnp.bfloat16),
            "ctx",
            -hop_index,
        ).astype(jnp.float32)
    query_prenorm_gradient = (
        norm_back(query_heads, query_norm_gain, grad_query)
        .reshape(shard_len, heads_here * head_dim)
        .astype(jnp.bfloat16)
    )
    key_prenorm_gradient = norm_back(
        key_before_norm, key_norm_gain, own_grads[:, :head_dim]
    ).astype(jnp.bfloat16)
    value_prenorm_gradient = own_grads[:, head_dim:].astype(jnp.bfloat16)
    query_up_contribution = adapter_scale * transpose_multiply(middle_query, query_prenorm_gradient)
    key_up_contribution = adapter_scale * transpose_multiply(middle_key, key_prenorm_gradient)
    value_up_contribution = adapter_scale * transpose_multiply(middle_value, value_prenorm_gradient)
    middle_gradients = jnp.concatenate(
        [
            adapter_scale * multiply_by_transpose(query_prenorm_gradient, adapter_query_up),
            adapter_scale * multiply_by_transpose(key_prenorm_gradient, adapter_key_up),
            adapter_scale * multiply_by_transpose(value_prenorm_gradient, adapter_value_up),
        ],
        axis=1,
    ).astype(jnp.bfloat16)
    grad_normed = multiply_by_transpose(
        jnp.concatenate(
            [query_prenorm_gradient, key_prenorm_gradient, value_prenorm_gradient, middle_gradients],
            axis=1,
        ),
        all_weights,
    )
    grad_normed_rows = tp_sum_scatter(grad_normed.astype(jnp.bfloat16))
    grad_in = norm_back(tok_float, input_norm_gain, grad_normed_rows).astype(jnp.bfloat16)
    down_term = tp_sum_scatter(
        transpose_multiply(normalized_input, middle_gradients).astype(jnp.bfloat16)
    )
    adapter_totals = ctx_sum(
        [
            down_term,
            query_up_contribution,
            key_up_contribution,
            value_up_contribution,
            down_out_term,
            output_up_contribution,
        ]
    )
    return (
        layer_out,
        grad_in,
        adapter_totals[0],
        adapter_totals[1],
        adapter_totals[2],
        adapter_totals[3],
        adapter_totals[4],
        adapter_totals[5],
    )


def solution(mesh):
    in_specs = (
        P(("groups", "ctx", "tp"), None),
        P(("groups", "ctx", "tp"), None),
        P(("groups", "ctx")),
        P(("groups", "ctx")),
        P(),
        P(),
        P(),
        P(),
        P(None, "tp"),
        P(None, "tp"),
        P(None, "tp"),
        P("tp", None),
        P(),
        P(None, "tp"),
        P(None, "tp"),
        P(None, "tp"),
        P("tp", None),
        P(),
    )
    out_specs = (
        P(("groups", "ctx", "tp"), None),
        P(("groups", "ctx", "tp"), None),
        P(("groups", "tp"), None),
        P("groups", "tp"),
        P("groups", "tp"),
        P("groups", "tp"),
        P(("groups", "tp"), None),
        P("groups", "tp"),
    )
    return jax.shard_map(
        on_device, mesh=mesh, in_specs=in_specs, out_specs=out_specs, check_vma=False
    )
```

```python
import jax
import jax.numpy as jnp
from jax import lax
from jax.sharding import PartitionSpec as P

WINDOW = 1024


epsilon = 1e-06
adapter_scale = 2.0
score_scale = 168.0 ** (-0.5)


def passed_along(value, axis, steps):
    count = lax.axis_size(axis)
    leading, last = (max(0, -steps), min(count, count - steps))
    return lax.ppermute(value, axis, [(source, source + steps) for source in range(leading, last)])


def norm_rows(source, gain_vec):
    inverse = lax.rsqrt(jnp.mean(source * source, axis=-1, keepdims=True) + epsilon)
    return source * inverse * gain_vec


def norm_back(source, gain_vec, incoming):
    inverse = lax.rsqrt(jnp.mean(source * source, axis=-1, keepdims=True) + epsilon)
    scaled = source * inverse
    upward = incoming * gain_vec
    return inverse * (upward - scaled * jnp.mean(upward * scaled, axis=-1, keepdims=True))


def matrix_product(first_op, second_op):
    return jnp.dot(first_op, second_op, preferred_element_type=jnp.float32)


def multiply_by_transpose(first_op, second_op):
    return lax.dot_general(
        first_op, second_op, (((1,), (1,)), ((), ())), preferred_element_type=jnp.float32
    )


def transpose_multiply(first_op, second_op):
    return lax.dot_general(
        first_op, second_op, (((0,), (0,)), ((), ())), preferred_element_type=jnp.float32
    )


def window_mask(query_segs, key_codes):
    query_count = query_segs.shape[0]
    key_total = key_codes.shape[0]
    distance = (key_total - query_count + jnp.arange(query_count))[:, None] - jnp.arange(key_total)[
        None, :
    ]
    same_doc = key_codes[None, :] == query_segs[:, None] + 1
    return (distance == 0) | (distance > 0) & (distance < WINDOW) & same_doc


def tp_sum_scatter(value):
    if lax.axis_size("tp") != 2:
        return lax.psum_scatter(value, "tp", scatter_dimension=0, tiled=True).astype(jnp.float32)
    half = value.shape[0] // 2
    tp_index = lax.axis_index("tp")
    mine = lax.dynamic_slice_in_dim(value, tp_index * half, half, 0)
    theirs = lax.dynamic_slice_in_dim(value, (1 - tp_index) * half, half, 0)
    received = lax.ppermute(theirs, "tp", [(0, 1), (1, 0)])
    return mine.astype(jnp.float32) + received.astype(jnp.float32)


def tp_gather(value):
    if lax.axis_size("tp") != 2:
        return lax.all_gather(value, "tp", axis=0, tiled=True)
    received = lax.ppermute(value, "tp", [(0, 1), (1, 0)])
    first = lax.axis_index("tp") == 0
    return jnp.concatenate(
        [jnp.where(first, value, received), jnp.where(first, received, value)], axis=0
    )


def ctx_sum(parts):
    count = lax.axis_size("ctx")
    if count & (count - 1):
        return [lax.psum(p.astype(jnp.bfloat16), "ctx").astype(jnp.float32) for p in parts]
    flat = jnp.concatenate([p.astype(jnp.float32).reshape(-1) for p in parts])
    step = 1
    while step < count:
        sent = flat.astype(jnp.bfloat16)
        received = lax.ppermute(sent, "ctx", [(i, i ^ step) for i in range(count)])
        flat = sent.astype(jnp.float32) + received.astype(jnp.float32)
        step *= 2
    results, offset = [], 0
    for p in parts:
        results.append(flat[offset : offset + p.size].reshape(p.shape))
        offset += p.size
    return results


def on_device(
    tokens,
    output_gradient,
    document_index,
    real_token_count,
    input_norm_gain,
    query_norm_gain,
    key_norm_gain,
    output_norm_gain,
    query_projection,
    key_projection,
    value_projection,
    output_projection,
    adapter_down_maps,
    adapter_query_up,
    adapter_key_up,
    adapter_value_up,
    adapter_output_down,
    adapter_output_up,
):
    row_count, model_width = tokens.shape
    shard_len = document_index.shape[0]
    head_dim = key_projection.shape[1]
    adapter_product = adapter_key_up.shape[0]
    heads_here = query_projection.shape[1] // head_dim
    ctx_size = lax.axis_size("ctx")
    tp_index = lax.axis_index("tp")
    slice_width = model_width // lax.axis_size("tp")
    reach_shards = WINDOW // shard_len
    send_count = min(reach_shards, ctx_size - 1)
    tok_float = tokens.astype(jnp.float32)
    normed_rows = norm_rows(tok_float, input_norm_gain).astype(jnp.bfloat16)
    normalized_input = tp_gather(normed_rows)
    query_width = query_projection.shape[1]
    key_end = query_width + head_dim
    value_end = key_end + head_dim
    all_weights = jnp.concatenate(
        [query_projection, key_projection, value_projection, adapter_down_maps], axis=1
    )
    projected = matrix_product(normalized_input, all_weights)
    middle_list = projected[:, value_end:].astype(jnp.bfloat16)
    middle_query = middle_list[:, :adapter_product]
    middle_key = middle_list[:, adapter_product : 2 * adapter_product]
    middle_value = middle_list[:, 2 * adapter_product :]
    query_before_norm = projected[:, :query_width] + adapter_scale * matrix_product(
        middle_query, adapter_query_up
    )
    key_before_norm = projected[:, query_width:key_end] + adapter_scale * matrix_product(
        middle_key, adapter_key_up
    )
    value_before_norm = projected[:, key_end:value_end] + adapter_scale * matrix_product(
        middle_value, adapter_value_up
    )
    query_heads = query_before_norm.reshape(shard_len, heads_here, head_dim)
    query_normed = norm_rows(query_heads, query_norm_gain).astype(jnp.bfloat16)
    key_normed = norm_rows(key_before_norm, key_norm_gain).astype(jnp.bfloat16)
    value_cast = value_before_norm.astype(jnp.bfloat16)
    positions = jnp.arange(shard_len)
    is_valid = positions < real_token_count[0]
    valid_rows = is_valid.astype(jnp.float32)
    local_codes = jnp.where(is_valid, document_index + 1, 0)
    local_pair = jnp.concatenate([key_normed, value_cast], axis=1)
    code_rows = jnp.zeros((16, local_pair.shape[1]), jnp.bfloat16)
    code_rows = code_rows.at[0, :shard_len].set(local_codes.astype(jnp.bfloat16))
    payload = jnp.concatenate([local_pair, code_rows], axis=0)
    received = []
    for hop_index in range(1, send_count + 1):
        arrived = passed_along(payload, "ctx", hop_index)
        received.append(
            (arrived[:shard_len], arrived[shard_len, :shard_len].astype(jnp.int32))
        )
    missing = reach_shards - send_count
    blank_pair = jnp.zeros_like(local_pair)
    blank_codes = jnp.zeros_like(local_codes)
    earlier = [(blank_pair, blank_codes)] * missing + list(reversed(received))
    key_pairs = jnp.concatenate([entry[0] for entry in earlier] + [local_pair], axis=0)
    key_codes_all = jnp.concatenate([entry[1] for entry in earlier] + [local_codes], axis=0)
    keys_all = key_pairs[:, :head_dim]
    values_all = key_pairs[:, head_dim:]
    allowed = window_mask(document_index, key_codes_all)
    scores = (
        jnp.einsum("thd,sd->hts", query_normed, keys_all, preferred_element_type=jnp.float32)
        * score_scale
    )
    weights = jnp.where(allowed[None], jnp.exp(scores), 0.0)
    attn_probs = weights / jnp.sum(weights, axis=-1, keepdims=True)
    probs_cast = attn_probs.astype(jnp.bfloat16)
    attention_result = jnp.einsum(
        "hts,sd->thd", probs_cast, values_all, preferred_element_type=jnp.float32
    )
    attention_result = (
        (attention_result * valid_rows[:, None, None])
        .astype(jnp.bfloat16)
        .reshape(shard_len, heads_here * head_dim)
    )
    part_out = matrix_product(attention_result, output_projection)
    partial_middle = matrix_product(attention_result, adapter_output_down)
    output_total = tp_sum_scatter(part_out.astype(jnp.bfloat16))
    mid_sum = tp_sum_scatter(partial_middle.astype(jnp.bfloat16))
    middle_output = mid_sum.astype(jnp.bfloat16)
    apply_prenorm = output_total + adapter_scale * matrix_product(middle_output, adapter_output_up)
    layer_out = norm_rows(apply_prenorm, output_norm_gain).astype(jnp.bfloat16)
    prenorm_gradient = norm_back(
        apply_prenorm, output_norm_gain, output_gradient.astype(jnp.float32)
    ).astype(jnp.bfloat16)
    middle_output_gradient = (
        adapter_scale * multiply_by_transpose(prenorm_gradient, adapter_output_up)
    ).astype(jnp.bfloat16)
    complete_gradient = tp_gather(prenorm_gradient)
    middle_pair = tp_gather(jnp.concatenate([middle_output_gradient, middle_output], axis=1))
    middle_complete_gradient = middle_pair[:, :adapter_product]
    middle_complete = middle_pair[:, adapter_product:]
    gradient_portion = lax.dynamic_slice_in_dim(
        complete_gradient, tp_index * slice_width, slice_width, 1
    )
    output_up_contribution = adapter_scale * transpose_multiply(middle_complete, gradient_portion)
    attention_gradient = multiply_by_transpose(
        complete_gradient, output_projection
    ) + multiply_by_transpose(middle_complete_gradient, adapter_output_down)
    attention_gradient = (attention_gradient * valid_rows[:, None]).astype(jnp.bfloat16)
    down_out_term = transpose_multiply(attention_result, middle_complete_gradient)
    grad_heads = attention_gradient.reshape(shard_len, heads_here, head_dim)
    grad_probs = jnp.einsum(
        "thd,sd->hts", grad_heads, values_all, preferred_element_type=jnp.float32
    )
    inner_sum = jnp.sum(attn_probs * grad_probs, axis=-1, keepdims=True)
    grad_scores = lax.optimization_barrier(
        (attn_probs * (grad_probs - inner_sum) * score_scale).astype(jnp.bfloat16)
    )
    grad_query = jnp.einsum(
        "hts,sd->thd", grad_scores, keys_all, preferred_element_type=jnp.float32
    )
    grad_keys = jnp.einsum(
        "hts,thd->sd", grad_scores, query_normed, preferred_element_type=jnp.float32
    )
    grad_values = jnp.einsum(
        "hts,thd->sd", probs_cast, grad_heads, preferred_element_type=jnp.float32
    )
    grad_pairs = jnp.concatenate([grad_keys, grad_values], axis=1)
    own_grads = grad_pairs[reach_shards * shard_len :]

    def hop_block(hop_index):
        first_row = (reach_shards - hop_index) * shard_len
        return grad_pairs[first_row : first_row + shard_len]

    if send_count == 4:
        far = passed_along(
            jnp.concatenate([hop_block(3), hop_block(4)], axis=0).astype(jnp.bfloat16), "ctx", -2
        ).astype(jnp.float32)
        near_sum = hop_block(1) + far[:shard_len]
        next_sum = hop_block(2) + far[shard_len:]
        own_grads = (
            own_grads
            + passed_along(near_sum.astype(jnp.bfloat16), "ctx", -1).astype(jnp.float32)
            + passed_along(next_sum.astype(jnp.bfloat16), "ctx", -2).astype(jnp.float32)
        )
    else:
        for hop_index in range(1, send_count + 1):
            own_grads = own_grads + passed_along(
                hop_block(hop_index).astype(jnp.bfloat16), "ctx", -hop_index
            ).astype(jnp.float32)
    query_prenorm_gradient = (
        norm_back(query_heads, query_norm_gain, grad_query)
        .reshape(shard_len, heads_here * head_dim)
        .astype(jnp.bfloat16)
    )
    key_prenorm_gradient = norm_back(
        key_before_norm, key_norm_gain, own_grads[:, :head_dim]
    ).astype(jnp.bfloat16)
    value_prenorm_gradient = own_grads[:, head_dim:].astype(jnp.bfloat16)
    query_up_contribution = adapter_scale * transpose_multiply(middle_query, query_prenorm_gradient)
    key_up_contribution = adapter_scale * transpose_multiply(middle_key, key_prenorm_gradient)
    value_up_contribution = adapter_scale * transpose_multiply(middle_value, value_prenorm_gradient)
    middle_gradients = jnp.concatenate(
        [
            adapter_scale * multiply_by_transpose(query_prenorm_gradient, adapter_query_up),
            adapter_scale * multiply_by_transpose(key_prenorm_gradient, adapter_key_up),
            adapter_scale * multiply_by_transpose(value_prenorm_gradient, adapter_value_up),
        ],
        axis=1,
    ).astype(jnp.bfloat16)
    grad_normed = multiply_by_transpose(
        jnp.concatenate(
            [query_prenorm_gradient, key_prenorm_gradient, value_prenorm_gradient, middle_gradients],
            axis=1,
        ),
        all_weights,
    )
    grad_normed_rows = tp_sum_scatter(grad_normed.astype(jnp.bfloat16))
    grad_in = norm_back(tok_float, input_norm_gain, grad_normed_rows).astype(jnp.bfloat16)
    down_term = tp_sum_scatter(
        transpose_multiply(normalized_input, middle_gradients).astype(jnp.bfloat16)
    )
    adapter_totals = ctx_sum(
        [
            down_term,
            query_up_contribution,
            key_up_contribution,
            value_up_contribution,
            down_out_term,
            output_up_contribution,
        ]
    )
    return (
        layer_out,
        grad_in,
        adapter_totals[0],
        adapter_totals[1],
        adapter_totals[2],
        adapter_totals[3],
        adapter_totals[4],
        adapter_totals[5],
    )


def solution(mesh):
    in_specs = (
        P(("groups", "ctx", "tp"), None),
        P(("groups", "ctx", "tp"), None),
        P(("groups", "ctx")),
        P(("groups", "ctx")),
        P(),
        P(),
        P(),
        P(),
        P(None, "tp"),
        P(None, "tp"),
        P(None, "tp"),
        P("tp", None),
        P(),
        P(None, "tp"),
        P(None, "tp"),
        P(None, "tp"),
        P("tp", None),
        P(),
    )
    out_specs = (
        P(("groups", "ctx", "tp"), None),
        P(("groups", "ctx", "tp"), None),
        P(("groups", "tp"), None),
        P("groups", "tp"),
        P("groups", "tp"),
        P("groups", "tp"),
        P(("groups", "tp"), None),
        P("groups", "tp"),
    )
    return jax.shard_map(
        on_device, mesh=mesh, in_specs=in_specs, out_specs=out_specs, check_vma=False
    )
```

```python
import jax
import jax.numpy as jnp
from jax import lax
from jax.sharding import PartitionSpec as P

WINDOW = 1024


epsilon = 1e-06
adapter_scale = 2.0
score_scale = 168.0 ** (-0.5)


def passed_along(value, axis, steps):
    count = lax.axis_size(axis)
    leading, last = (max(0, -steps), min(count, count - steps))
    return lax.ppermute(value, axis, [(source, source + steps) for source in range(leading, last)])


def norm_rows(source, gain_vec):
    inverse = lax.rsqrt(jnp.mean(source * source, axis=-1, keepdims=True) + epsilon)
    return source * inverse * gain_vec


def norm_back(source, gain_vec, incoming):
    inverse = lax.rsqrt(jnp.mean(source * source, axis=-1, keepdims=True) + epsilon)
    scaled = source * inverse
    upward = incoming * gain_vec
    return inverse * (upward - scaled * jnp.mean(upward * scaled, axis=-1, keepdims=True))


def matrix_product(first_op, second_op):
    return jnp.dot(first_op, second_op, preferred_element_type=jnp.float32)


def multiply_by_transpose(first_op, second_op):
    return lax.dot_general(
        first_op, second_op, (((1,), (1,)), ((), ())), preferred_element_type=jnp.float32
    )


def transpose_multiply(first_op, second_op):
    return lax.dot_general(
        first_op, second_op, (((0,), (0,)), ((), ())), preferred_element_type=jnp.float32
    )


def window_mask(query_segs, key_codes):
    query_count = query_segs.shape[0]
    key_total = key_codes.shape[0]
    distance = (key_total - query_count + jnp.arange(query_count))[:, None] - jnp.arange(key_total)[
        None, :
    ]
    same_doc = key_codes[None, :] == query_segs[:, None] + 1
    return (distance == 0) | (distance > 0) & (distance < WINDOW) & same_doc


def tp_sum_scatter(value):
    if lax.axis_size("tp") != 2:
        return lax.psum_scatter(value, "tp", scatter_dimension=0, tiled=True).astype(jnp.float32)
    half = value.shape[0] // 2
    tp_index = lax.axis_index("tp")
    mine = lax.dynamic_slice_in_dim(value, tp_index * half, half, 0)
    theirs = lax.dynamic_slice_in_dim(value, (1 - tp_index) * half, half, 0)
    received = lax.ppermute(theirs, "tp", [(0, 1), (1, 0)])
    return mine.astype(jnp.float32) + received.astype(jnp.float32)


def tp_gather(value):
    if lax.axis_size("tp") != 2:
        return lax.all_gather(value, "tp", axis=0, tiled=True)
    received = lax.ppermute(value, "tp", [(0, 1), (1, 0)])
    first = lax.axis_index("tp") == 0
    return jnp.concatenate(
        [jnp.where(first, value, received), jnp.where(first, received, value)], axis=0
    )


def ctx_sum(parts):
    count = lax.axis_size("ctx")
    if count & (count - 1):
        return [lax.psum(p.astype(jnp.bfloat16), "ctx").astype(jnp.float32) for p in parts]
    flat = jnp.concatenate([p.astype(jnp.float32).reshape(-1) for p in parts])
    step = 1
    while step < count:
        sent = flat.astype(jnp.bfloat16)
        received = lax.ppermute(sent, "ctx", [(i, i ^ step) for i in range(count)])
        flat = sent.astype(jnp.float32) + received.astype(jnp.float32)
        step *= 2
    results, offset = [], 0
    for p in parts:
        results.append(flat[offset : offset + p.size].reshape(p.shape))
        offset += p.size
    return results


def on_device(
    tokens,
    output_gradient,
    document_index,
    real_token_count,
    input_norm_gain,
    query_norm_gain,
    key_norm_gain,
    output_norm_gain,
    query_projection,
    key_projection,
    value_projection,
    output_projection,
    adapter_down_maps,
    adapter_query_up,
    adapter_key_up,
    adapter_value_up,
    adapter_output_down,
    adapter_output_up,
):
    row_count, model_width = tokens.shape
    shard_len = document_index.shape[0]
    head_dim = key_projection.shape[1]
    adapter_product = adapter_key_up.shape[0]
    heads_here = query_projection.shape[1] // head_dim
    ctx_size = lax.axis_size("ctx")
    tp_index = lax.axis_index("tp")
    slice_width = model_width // lax.axis_size("tp")
    reach_shards = WINDOW // shard_len
    send_count = min(reach_shards, ctx_size - 1)
    tok_float = tokens.astype(jnp.float32)
    normed_rows = norm_rows(tok_float, input_norm_gain).astype(jnp.bfloat16)
    normalized_input = tp_gather(normed_rows)
    query_width = query_projection.shape[1]
    key_end = query_width + head_dim
    value_end = key_end + head_dim
    all_weights = jnp.concatenate(
        [query_projection, key_projection, value_projection, adapter_down_maps], axis=1
    )
    projected = matrix_product(normalized_input, all_weights)
    middle_list = projected[:, value_end:].astype(jnp.bfloat16)
    middle_query = middle_list[:, :adapter_product]
    middle_key = middle_list[:, adapter_product : 2 * adapter_product]
    middle_value = middle_list[:, 2 * adapter_product :]
    query_before_norm = projected[:, :query_width] + adapter_scale * matrix_product(
        middle_query, adapter_query_up
    )
    key_before_norm = projected[:, query_width:key_end] + adapter_scale * matrix_product(
        middle_key, adapter_key_up
    )
    value_before_norm = projected[:, key_end:value_end] + adapter_scale * matrix_product(
        middle_value, adapter_value_up
    )
    query_heads = query_before_norm.reshape(shard_len, heads_here, head_dim)
    query_normed = norm_rows(query_heads, query_norm_gain).astype(jnp.bfloat16)
    key_normed = norm_rows(key_before_norm, key_norm_gain).astype(jnp.bfloat16)
    value_cast = value_before_norm.astype(jnp.bfloat16)
    positions = jnp.arange(shard_len)
    is_valid = positions < real_token_count[0]
    valid_rows = is_valid.astype(jnp.float32)
    local_codes = jnp.where(is_valid, document_index + 1, 0)
    local_pair = jnp.concatenate([key_normed, value_cast], axis=1)
    code_rows = jnp.zeros((16, local_pair.shape[1]), jnp.bfloat16)
    code_rows = code_rows.at[0, :shard_len].set(local_codes.astype(jnp.bfloat16))
    payload = jnp.concatenate([local_pair, code_rows], axis=0)
    payload_rows = payload.shape[0]
    if send_count == 4:
        two_back = passed_along(payload, "ctx", 2)
        odd_back = passed_along(jnp.concatenate([payload, two_back], axis=0), "ctx", 1)
        arrivals = [
            odd_back[:payload_rows],
            two_back,
            odd_back[payload_rows:],
            passed_along(two_back, "ctx", 2),
        ]
    else:
        arrivals = [
            passed_along(payload, "ctx", hop_index) for hop_index in range(1, send_count + 1)
        ]
    received = [
        (arrived[:shard_len], arrived[shard_len, :shard_len].astype(jnp.int32))
        for arrived in arrivals
    ]
    missing = reach_shards - send_count
    blank_pair = jnp.zeros_like(local_pair)
    blank_codes = jnp.zeros_like(local_codes)
    earlier = [(blank_pair, blank_codes)] * missing + list(reversed(received))
    key_pairs = jnp.concatenate([entry[0] for entry in earlier] + [local_pair], axis=0)
    key_codes_all = jnp.concatenate([entry[1] for entry in earlier] + [local_codes], axis=0)
    keys_all = key_pairs[:, :head_dim]
    values_all = key_pairs[:, head_dim:]
    allowed = window_mask(document_index, key_codes_all)
    scores = (
        jnp.einsum("thd,sd->hts", query_normed, keys_all, preferred_element_type=jnp.float32)
        * score_scale
    )
    weights = jnp.where(allowed[None], jnp.exp(scores), 0.0)
    attn_probs = weights / jnp.sum(weights, axis=-1, keepdims=True)
    probs_cast = attn_probs.astype(jnp.bfloat16)
    attention_result = jnp.einsum(
        "hts,sd->thd", probs_cast, values_all, preferred_element_type=jnp.float32
    )
    attention_result = (
        (attention_result * valid_rows[:, None, None])
        .astype(jnp.bfloat16)
        .reshape(shard_len, heads_here * head_dim)
    )
    part_out = matrix_product(attention_result, output_projection)
    partial_middle = matrix_product(attention_result, adapter_output_down)
    output_total = tp_sum_scatter(part_out.astype(jnp.bfloat16))
    mid_sum = tp_sum_scatter(partial_middle.astype(jnp.bfloat16))
    middle_output = mid_sum.astype(jnp.bfloat16)
    apply_prenorm = output_total + adapter_scale * matrix_product(middle_output, adapter_output_up)
    layer_out = norm_rows(apply_prenorm, output_norm_gain).astype(jnp.bfloat16)
    prenorm_gradient = norm_back(
        apply_prenorm, output_norm_gain, output_gradient.astype(jnp.float32)
    ).astype(jnp.bfloat16)
    middle_output_gradient = (
        adapter_scale * multiply_by_transpose(prenorm_gradient, adapter_output_up)
    ).astype(jnp.bfloat16)
    complete_gradient = tp_gather(prenorm_gradient)
    middle_pair = tp_gather(jnp.concatenate([middle_output_gradient, middle_output], axis=1))
    middle_complete_gradient = middle_pair[:, :adapter_product]
    middle_complete = middle_pair[:, adapter_product:]
    gradient_portion = lax.dynamic_slice_in_dim(
        complete_gradient, tp_index * slice_width, slice_width, 1
    )
    output_up_contribution = adapter_scale * transpose_multiply(middle_complete, gradient_portion)
    attention_gradient = multiply_by_transpose(
        complete_gradient, output_projection
    ) + multiply_by_transpose(middle_complete_gradient, adapter_output_down)
    attention_gradient = (attention_gradient * valid_rows[:, None]).astype(jnp.bfloat16)
    down_out_term = transpose_multiply(attention_result, middle_complete_gradient)
    grad_heads = attention_gradient.reshape(shard_len, heads_here, head_dim)
    grad_probs = jnp.einsum(
        "thd,sd->hts", grad_heads, values_all, preferred_element_type=jnp.float32
    )
    inner_sum = jnp.sum(attn_probs * grad_probs, axis=-1, keepdims=True)
    grad_scores = lax.optimization_barrier(
        (attn_probs * (grad_probs - inner_sum) * score_scale).astype(jnp.bfloat16)
    )
    grad_query = jnp.einsum(
        "hts,sd->thd", grad_scores, keys_all, preferred_element_type=jnp.float32
    )
    grad_keys = jnp.einsum(
        "hts,thd->sd", grad_scores, query_normed, preferred_element_type=jnp.float32
    )
    grad_values = jnp.einsum(
        "hts,thd->sd", probs_cast, grad_heads, preferred_element_type=jnp.float32
    )
    grad_pairs = jnp.concatenate([grad_keys, grad_values], axis=1)
    own_grads = grad_pairs[reach_shards * shard_len :]

    def hop_block(hop_index):
        first_row = (reach_shards - hop_index) * shard_len
        return grad_pairs[first_row : first_row + shard_len]

    if send_count == 4:
        far = passed_along(
            jnp.concatenate([hop_block(3), hop_block(4)], axis=0).astype(jnp.bfloat16), "ctx", -2
        ).astype(jnp.float32)
        near_sum = hop_block(1) + far[:shard_len]
        next_sum = hop_block(2) + far[shard_len:]
        own_grads = (
            own_grads
            + passed_along(near_sum.astype(jnp.bfloat16), "ctx", -1).astype(jnp.float32)
            + passed_along(next_sum.astype(jnp.bfloat16), "ctx", -2).astype(jnp.float32)
        )
    else:
        for hop_index in range(1, send_count + 1):
            own_grads = own_grads + passed_along(
                hop_block(hop_index).astype(jnp.bfloat16), "ctx", -hop_index
            ).astype(jnp.float32)
    query_prenorm_gradient = (
        norm_back(query_heads, query_norm_gain, grad_query)
        .reshape(shard_len, heads_here * head_dim)
        .astype(jnp.bfloat16)
    )
    key_prenorm_gradient = norm_back(
        key_before_norm, key_norm_gain, own_grads[:, :head_dim]
    ).astype(jnp.bfloat16)
    value_prenorm_gradient = own_grads[:, head_dim:].astype(jnp.bfloat16)
    query_up_contribution = adapter_scale * transpose_multiply(middle_query, query_prenorm_gradient)
    key_up_contribution = adapter_scale * transpose_multiply(middle_key, key_prenorm_gradient)
    value_up_contribution = adapter_scale * transpose_multiply(middle_value, value_prenorm_gradient)
    middle_gradients = jnp.concatenate(
        [
            adapter_scale * multiply_by_transpose(query_prenorm_gradient, adapter_query_up),
            adapter_scale * multiply_by_transpose(key_prenorm_gradient, adapter_key_up),
            adapter_scale * multiply_by_transpose(value_prenorm_gradient, adapter_value_up),
        ],
        axis=1,
    ).astype(jnp.bfloat16)
    grad_normed = multiply_by_transpose(
        jnp.concatenate(
            [query_prenorm_gradient, key_prenorm_gradient, value_prenorm_gradient, middle_gradients],
            axis=1,
        ),
        all_weights,
    )
    grad_normed_rows = tp_sum_scatter(grad_normed.astype(jnp.bfloat16))
    grad_in = norm_back(tok_float, input_norm_gain, grad_normed_rows).astype(jnp.bfloat16)
    down_term = tp_sum_scatter(
        transpose_multiply(normalized_input, middle_gradients).astype(jnp.bfloat16)
    )
    adapter_totals = ctx_sum(
        [
            down_term,
            query_up_contribution,
            key_up_contribution,
            value_up_contribution,
            down_out_term,
            output_up_contribution,
        ]
    )
    return (
        layer_out,
        grad_in,
        adapter_totals[0],
        adapter_totals[1],
        adapter_totals[2],
        adapter_totals[3],
        adapter_totals[4],
        adapter_totals[5],
    )


def solution(mesh):
    in_specs = (
        P(("groups", "ctx", "tp"), None),
        P(("groups", "ctx", "tp"), None),
        P(("groups", "ctx")),
        P(("groups", "ctx")),
        P(),
        P(),
        P(),
        P(),
        P(None, "tp"),
        P(None, "tp"),
        P(None, "tp"),
        P("tp", None),
        P(),
        P(None, "tp"),
        P(None, "tp"),
        P(None, "tp"),
        P("tp", None),
        P(),
    )
    out_specs = (
        P(("groups", "ctx", "tp"), None),
        P(("groups", "ctx", "tp"), None),
        P(("groups", "tp"), None),
        P("groups", "tp"),
        P("groups", "tp"),
        P("groups", "tp"),
        P(("groups", "tp"), None),
        P("groups", "tp"),
    )
    return jax.shard_map(
        on_device, mesh=mesh, in_specs=in_specs, out_specs=out_specs, check_vma=False
    )
```

```python
import jax
import jax.numpy as jnp
from jax import lax
from jax.sharding import PartitionSpec as P

WINDOW = 1024


epsilon = 1e-06
adapter_scale = 2.0
score_scale = 168.0 ** (-0.5)


def passed_along(value, axis, steps):
    count = lax.axis_size(axis)
    leading, last = (max(0, -steps), min(count, count - steps))
    return lax.ppermute(value, axis, [(source, source + steps) for source in range(leading, last)])


def norm_rows(source, gain_vec):
    inverse = lax.rsqrt(jnp.mean(source * source, axis=-1, keepdims=True) + epsilon)
    return source * inverse * gain_vec


def norm_back(source, gain_vec, incoming):
    inverse = lax.rsqrt(jnp.mean(source * source, axis=-1, keepdims=True) + epsilon)
    scaled = source * inverse
    upward = incoming * gain_vec
    return inverse * (upward - scaled * jnp.mean(upward * scaled, axis=-1, keepdims=True))


def matrix_product(first_op, second_op):
    return jnp.dot(first_op, second_op, preferred_element_type=jnp.float32)


def multiply_by_transpose(first_op, second_op):
    return lax.dot_general(
        first_op, second_op, (((1,), (1,)), ((), ())), preferred_element_type=jnp.float32
    )


def transpose_multiply(first_op, second_op):
    return lax.dot_general(
        first_op, second_op, (((0,), (0,)), ((), ())), preferred_element_type=jnp.float32
    )


def window_mask(query_segs, key_codes):
    query_count = query_segs.shape[0]
    key_total = key_codes.shape[0]
    distance = (key_total - query_count + jnp.arange(query_count))[:, None] - jnp.arange(key_total)[
        None, :
    ]
    same_doc = key_codes[None, :] == query_segs[:, None] + 1
    return (distance == 0) | (distance > 0) & (distance < WINDOW) & same_doc


def tp_sum_scatter(value):
    if lax.axis_size("tp") != 2:
        return lax.psum_scatter(value, "tp", scatter_dimension=0, tiled=True).astype(jnp.float32)
    half = value.shape[0] // 2
    tp_index = lax.axis_index("tp")
    mine = lax.dynamic_slice_in_dim(value, tp_index * half, half, 0)
    theirs = lax.dynamic_slice_in_dim(value, (1 - tp_index) * half, half, 0)
    received = lax.ppermute(theirs, "tp", [(0, 1), (1, 0)])
    return mine.astype(jnp.float32) + received.astype(jnp.float32)


def tp_gather(value):
    if lax.axis_size("tp") != 2:
        return lax.all_gather(value, "tp", axis=0, tiled=True)
    received = lax.ppermute(value, "tp", [(0, 1), (1, 0)])
    first = lax.axis_index("tp") == 0
    return jnp.concatenate(
        [jnp.where(first, value, received), jnp.where(first, received, value)], axis=0
    )


def ctx_sum(parts):
    count = lax.axis_size("ctx")
    if count & (count - 1):
        return [lax.psum(p.astype(jnp.bfloat16), "ctx").astype(jnp.float32) for p in parts]
    flat = jnp.concatenate([p.astype(jnp.float32).reshape(-1) for p in parts])
    step = 1
    while step < count:
        sent = flat.astype(jnp.bfloat16)
        received = lax.ppermute(sent, "ctx", [(i, i ^ step) for i in range(count)])
        flat = sent.astype(jnp.float32) + received.astype(jnp.float32)
        step *= 2
    results, offset = [], 0
    for p in parts:
        results.append(flat[offset : offset + p.size].reshape(p.shape))
        offset += p.size
    return results


def on_device(
    tokens,
    output_gradient,
    document_index,
    real_token_count,
    input_norm_gain,
    query_norm_gain,
    key_norm_gain,
    output_norm_gain,
    query_projection,
    key_projection,
    value_projection,
    output_projection,
    adapter_down_maps,
    adapter_query_up,
    adapter_key_up,
    adapter_value_up,
    adapter_output_down,
    adapter_output_up,
):
    row_count, model_width = tokens.shape
    shard_len = document_index.shape[0]
    head_dim = key_projection.shape[1]
    adapter_product = adapter_key_up.shape[0]
    heads_here = query_projection.shape[1] // head_dim
    ctx_size = lax.axis_size("ctx")
    tp_index = lax.axis_index("tp")
    slice_width = model_width // lax.axis_size("tp")
    reach_shards = WINDOW // shard_len
    send_count = min(reach_shards, ctx_size - 1)
    tok_float = tokens.astype(jnp.float32)
    normed_rows = norm_rows(tok_float, input_norm_gain).astype(jnp.bfloat16)
    normalized_input = tp_gather(normed_rows)
    query_width = query_projection.shape[1]
    key_end = query_width + head_dim
    value_end = key_end + head_dim
    all_weights = jnp.concatenate(
        [query_projection, key_projection, value_projection, adapter_down_maps], axis=1
    )
    projected = matrix_product(normalized_input, all_weights)
    middle_list = projected[:, value_end:].astype(jnp.bfloat16)
    middle_query = middle_list[:, :adapter_product]
    middle_key = middle_list[:, adapter_product : 2 * adapter_product]
    middle_value = middle_list[:, 2 * adapter_product :]
    query_before_norm = projected[:, :query_width] + adapter_scale * matrix_product(
        middle_query, adapter_query_up
    )
    key_before_norm = projected[:, query_width:key_end] + adapter_scale * matrix_product(
        middle_key, adapter_key_up
    )
    value_before_norm = projected[:, key_end:value_end] + adapter_scale * matrix_product(
        middle_value, adapter_value_up
    )
    query_heads = query_before_norm.reshape(shard_len, heads_here, head_dim)
    query_normed = norm_rows(query_heads, query_norm_gain).astype(jnp.bfloat16)
    key_normed = norm_rows(key_before_norm, key_norm_gain).astype(jnp.bfloat16)
    value_cast = value_before_norm.astype(jnp.bfloat16)
    positions = jnp.arange(shard_len)
    is_valid = positions < real_token_count[0]
    valid_rows = is_valid.astype(jnp.float32)
    local_codes = jnp.where(is_valid, document_index + 1, 0)
    local_pair = jnp.concatenate([key_normed, value_cast], axis=1)
    code_rows = jnp.zeros((16, local_pair.shape[1]), jnp.bfloat16)
    code_rows = code_rows.at[0, :shard_len].set(local_codes.astype(jnp.bfloat16))
    payload = jnp.concatenate([local_pair, code_rows], axis=0)
    payload_rows = payload.shape[0]
    if send_count == 4:
        two_back = passed_along(payload, "ctx", 2)
        odd_back = passed_along(jnp.concatenate([payload, two_back], axis=0), "ctx", 1)
        arrivals = [
            odd_back[:payload_rows],
            two_back,
            odd_back[payload_rows:],
            passed_along(two_back, "ctx", 2),
        ]
    else:
        arrivals = [
            passed_along(payload, "ctx", hop_index) for hop_index in range(1, send_count + 1)
        ]
    received = [
        (arrived[:shard_len], arrived[shard_len, :shard_len].astype(jnp.int32))
        for arrived in arrivals
    ]
    missing = reach_shards - send_count
    blank_pair = jnp.zeros_like(local_pair)
    blank_codes = jnp.zeros_like(local_codes)
    earlier = [(blank_pair, blank_codes)] * missing + list(reversed(received))
    key_pairs = jnp.concatenate([entry[0] for entry in earlier] + [local_pair], axis=0)
    key_codes_all = jnp.concatenate([entry[1] for entry in earlier] + [local_codes], axis=0)
    keys_all = key_pairs[:, :head_dim]
    values_all = key_pairs[:, head_dim:]
    allowed = window_mask(document_index, key_codes_all)
    scores = (
        jnp.einsum("thd,sd->hts", query_normed, keys_all, preferred_element_type=jnp.float32)
        * score_scale
    )
    weights = jnp.where(allowed[None], jnp.exp(scores), 0.0)
    attn_probs = weights / jnp.sum(weights, axis=-1, keepdims=True)
    probs_cast = lax.optimization_barrier(attn_probs.astype(jnp.bfloat16))
    attention_result = jnp.einsum(
        "hts,sd->thd", probs_cast, values_all, preferred_element_type=jnp.float32
    )
    attention_result = (
        (attention_result * valid_rows[:, None, None])
        .astype(jnp.bfloat16)
        .reshape(shard_len, heads_here * head_dim)
    )
    part_out = matrix_product(attention_result, output_projection)
    partial_middle = matrix_product(attention_result, adapter_output_down)
    output_total = tp_sum_scatter(part_out.astype(jnp.bfloat16))
    mid_sum = tp_sum_scatter(partial_middle.astype(jnp.bfloat16))
    middle_output = mid_sum.astype(jnp.bfloat16)
    apply_prenorm = output_total + adapter_scale * matrix_product(middle_output, adapter_output_up)
    layer_out = norm_rows(apply_prenorm, output_norm_gain).astype(jnp.bfloat16)
    prenorm_gradient = norm_back(
        apply_prenorm, output_norm_gain, output_gradient.astype(jnp.float32)
    ).astype(jnp.bfloat16)
    middle_output_gradient = (
        adapter_scale * multiply_by_transpose(prenorm_gradient, adapter_output_up)
    ).astype(jnp.bfloat16)
    complete_gradient = tp_gather(prenorm_gradient)
    middle_pair = tp_gather(jnp.concatenate([middle_output_gradient, middle_output], axis=1))
    middle_complete_gradient = middle_pair[:, :adapter_product]
    middle_complete = middle_pair[:, adapter_product:]
    gradient_portion = lax.dynamic_slice_in_dim(
        complete_gradient, tp_index * slice_width, slice_width, 1
    )
    output_up_contribution = adapter_scale * transpose_multiply(middle_complete, gradient_portion)
    attention_gradient = multiply_by_transpose(
        complete_gradient, output_projection
    ) + multiply_by_transpose(middle_complete_gradient, adapter_output_down)
    attention_gradient = (attention_gradient * valid_rows[:, None]).astype(jnp.bfloat16)
    down_out_term = transpose_multiply(attention_result, middle_complete_gradient)
    grad_heads = attention_gradient.reshape(shard_len, heads_here, head_dim)
    grad_probs = jnp.einsum(
        "thd,sd->hts", grad_heads, values_all, preferred_element_type=jnp.float32
    )
    inner_sum = jnp.sum(attn_probs * grad_probs, axis=-1, keepdims=True)
    grad_scores = lax.optimization_barrier(
        (attn_probs * (grad_probs - inner_sum) * score_scale).astype(jnp.bfloat16)
    )
    grad_query = jnp.einsum(
        "hts,sd->thd", grad_scores, keys_all, preferred_element_type=jnp.float32
    )
    grad_keys = jnp.einsum(
        "hts,thd->sd", grad_scores, query_normed, preferred_element_type=jnp.float32
    )
    grad_values = jnp.einsum(
        "hts,thd->sd", probs_cast, grad_heads, preferred_element_type=jnp.float32
    )
    grad_pairs = jnp.concatenate([grad_keys, grad_values], axis=1)
    own_grads = grad_pairs[reach_shards * shard_len :]

    def hop_block(hop_index):
        first_row = (reach_shards - hop_index) * shard_len
        return grad_pairs[first_row : first_row + shard_len]

    if send_count == 4:
        far = passed_along(
            jnp.concatenate([hop_block(3), hop_block(4)], axis=0).astype(jnp.bfloat16), "ctx", -2
        ).astype(jnp.float32)
        near_sum = hop_block(1) + far[:shard_len]
        next_sum = hop_block(2) + far[shard_len:]
        own_grads = (
            own_grads
            + passed_along(near_sum.astype(jnp.bfloat16), "ctx", -1).astype(jnp.float32)
            + passed_along(next_sum.astype(jnp.bfloat16), "ctx", -2).astype(jnp.float32)
        )
    else:
        for hop_index in range(1, send_count + 1):
            own_grads = own_grads + passed_along(
                hop_block(hop_index).astype(jnp.bfloat16), "ctx", -hop_index
            ).astype(jnp.float32)
    query_prenorm_gradient = (
        norm_back(query_heads, query_norm_gain, grad_query)
        .reshape(shard_len, heads_here * head_dim)
        .astype(jnp.bfloat16)
    )
    key_prenorm_gradient = norm_back(
        key_before_norm, key_norm_gain, own_grads[:, :head_dim]
    ).astype(jnp.bfloat16)
    value_prenorm_gradient = own_grads[:, head_dim:].astype(jnp.bfloat16)
    query_up_contribution = adapter_scale * transpose_multiply(middle_query, query_prenorm_gradient)
    key_up_contribution = adapter_scale * transpose_multiply(middle_key, key_prenorm_gradient)
    value_up_contribution = adapter_scale * transpose_multiply(middle_value, value_prenorm_gradient)
    middle_gradients = jnp.concatenate(
        [
            adapter_scale * multiply_by_transpose(query_prenorm_gradient, adapter_query_up),
            adapter_scale * multiply_by_transpose(key_prenorm_gradient, adapter_key_up),
            adapter_scale * multiply_by_transpose(value_prenorm_gradient, adapter_value_up),
        ],
        axis=1,
    ).astype(jnp.bfloat16)
    grad_normed = multiply_by_transpose(
        jnp.concatenate(
            [query_prenorm_gradient, key_prenorm_gradient, value_prenorm_gradient, middle_gradients],
            axis=1,
        ),
        all_weights,
    )
    grad_normed_rows = tp_sum_scatter(grad_normed.astype(jnp.bfloat16))
    grad_in = norm_back(tok_float, input_norm_gain, grad_normed_rows).astype(jnp.bfloat16)
    down_term = tp_sum_scatter(
        transpose_multiply(normalized_input, middle_gradients).astype(jnp.bfloat16)
    )
    adapter_totals = ctx_sum(
        [
            down_term,
            query_up_contribution,
            key_up_contribution,
            value_up_contribution,
            down_out_term,
            output_up_contribution,
        ]
    )
    return (
        layer_out,
        grad_in,
        adapter_totals[0],
        adapter_totals[1],
        adapter_totals[2],
        adapter_totals[3],
        adapter_totals[4],
        adapter_totals[5],
    )


def solution(mesh):
    in_specs = (
        P(("groups", "ctx", "tp"), None),
        P(("groups", "ctx", "tp"), None),
        P(("groups", "ctx")),
        P(("groups", "ctx")),
        P(),
        P(),
        P(),
        P(),
        P(None, "tp"),
        P(None, "tp"),
        P(None, "tp"),
        P("tp", None),
        P(),
        P(None, "tp"),
        P(None, "tp"),
        P(None, "tp"),
        P("tp", None),
        P(),
    )
    out_specs = (
        P(("groups", "ctx", "tp"), None),
        P(("groups", "ctx", "tp"), None),
        P(("groups", "tp"), None),
        P("groups", "tp"),
        P("groups", "tp"),
        P("groups", "tp"),
        P(("groups", "tp"), None),
        P("groups", "tp"),
    )
    return jax.shard_map(
        on_device, mesh=mesh, in_specs=in_specs, out_specs=out_specs, check_vma=False
    )
```

```python
import jax
import jax.numpy as jnp
from jax import lax
from jax.sharding import PartitionSpec as P

WINDOW = 1024


epsilon = 1e-06
adapter_scale = 2.0
score_scale = 168.0 ** (-0.5)


def passed_along(value, axis, steps):
    count = lax.axis_size(axis)
    leading, last = (max(0, -steps), min(count, count - steps))
    return lax.ppermute(value, axis, [(source, source + steps) for source in range(leading, last)])


def norm_rows(source, gain_vec):
    inverse = lax.rsqrt(jnp.mean(source * source, axis=-1, keepdims=True) + epsilon)
    return source * inverse * gain_vec


def norm_back(source, gain_vec, incoming):
    inverse = lax.rsqrt(jnp.mean(source * source, axis=-1, keepdims=True) + epsilon)
    scaled = source * inverse
    upward = incoming * gain_vec
    return inverse * (upward - scaled * jnp.mean(upward * scaled, axis=-1, keepdims=True))


def matrix_product(first_op, second_op):
    return jnp.dot(first_op, second_op, preferred_element_type=jnp.float32)


def multiply_by_transpose(first_op, second_op):
    return lax.dot_general(
        first_op, second_op, (((1,), (1,)), ((), ())), preferred_element_type=jnp.float32
    )


def transpose_multiply(first_op, second_op):
    return lax.dot_general(
        first_op, second_op, (((0,), (0,)), ((), ())), preferred_element_type=jnp.float32
    )


def window_mask(query_segs, key_codes):
    query_count = query_segs.shape[0]
    key_total = key_codes.shape[0]
    distance = (key_total - query_count + jnp.arange(query_count))[:, None] - jnp.arange(key_total)[
        None, :
    ]
    same_doc = key_codes[None, :] == query_segs[:, None] + 1
    return (distance == 0) | (distance > 0) & (distance < WINDOW) & same_doc


def tp_sum_scatter(value):
    if lax.axis_size("tp") != 2:
        return lax.psum_scatter(value, "tp", scatter_dimension=0, tiled=True).astype(jnp.float32)
    half = value.shape[0] // 2
    tp_index = lax.axis_index("tp")
    mine = lax.dynamic_slice_in_dim(value, tp_index * half, half, 0)
    theirs = lax.dynamic_slice_in_dim(value, (1 - tp_index) * half, half, 0)
    received = lax.ppermute(theirs, "tp", [(0, 1), (1, 0)])
    return mine.astype(jnp.float32) + received.astype(jnp.float32)


def tp_gather(value):
    if lax.axis_size("tp") != 2:
        return lax.all_gather(value, "tp", axis=0, tiled=True)
    received = lax.ppermute(value, "tp", [(0, 1), (1, 0)])
    first = lax.axis_index("tp") == 0
    return jnp.concatenate(
        [jnp.where(first, value, received), jnp.where(first, received, value)], axis=0
    )


def ctx_sum(parts):
    count = lax.axis_size("ctx")
    if count & (count - 1):
        return [lax.psum(p.astype(jnp.bfloat16), "ctx").astype(jnp.float32) for p in parts]
    flat = jnp.concatenate([p.astype(jnp.float32).reshape(-1) for p in parts])
    step = 1
    while step < count:
        sent = flat.astype(jnp.bfloat16)
        received = lax.ppermute(sent, "ctx", [(i, i ^ step) for i in range(count)])
        flat = sent.astype(jnp.float32) + received.astype(jnp.float32)
        step *= 2
    results, offset = [], 0
    for p in parts:
        results.append(flat[offset : offset + p.size].reshape(p.shape))
        offset += p.size
    return results


def on_device(
    tokens,
    output_gradient,
    document_index,
    real_token_count,
    input_norm_gain,
    query_norm_gain,
    key_norm_gain,
    output_norm_gain,
    query_projection,
    key_projection,
    value_projection,
    output_projection,
    adapter_down_maps,
    adapter_query_up,
    adapter_key_up,
    adapter_value_up,
    adapter_output_down,
    adapter_output_up,
):
    row_count, model_width = tokens.shape
    shard_len = document_index.shape[0]
    head_dim = key_projection.shape[1]
    adapter_product = adapter_key_up.shape[0]
    heads_here = query_projection.shape[1] // head_dim
    ctx_size = lax.axis_size("ctx")
    tp_index = lax.axis_index("tp")
    slice_width = model_width // lax.axis_size("tp")
    reach_shards = WINDOW // shard_len
    send_count = min(reach_shards, ctx_size - 1)
    tok_float = tokens.astype(jnp.float32)
    normed_rows = norm_rows(tok_float, input_norm_gain).astype(jnp.bfloat16)
    normalized_input = tp_gather(normed_rows)
    query_width = query_projection.shape[1]
    key_end = query_width + head_dim
    value_end = key_end + head_dim
    all_weights = jnp.concatenate(
        [query_projection, key_projection, value_projection, adapter_down_maps], axis=1
    )
    projected = matrix_product(normalized_input, all_weights)
    middle_list = projected[:, value_end:].astype(jnp.bfloat16)
    middle_query = middle_list[:, :adapter_product]
    middle_key = middle_list[:, adapter_product : 2 * adapter_product]
    middle_value = middle_list[:, 2 * adapter_product :]
    query_before_norm = projected[:, :query_width] + adapter_scale * matrix_product(
        middle_query, adapter_query_up
    )
    key_before_norm = projected[:, query_width:key_end] + adapter_scale * matrix_product(
        middle_key, adapter_key_up
    )
    value_before_norm = projected[:, key_end:value_end] + adapter_scale * matrix_product(
        middle_value, adapter_value_up
    )
    query_heads = query_before_norm.reshape(shard_len, heads_here, head_dim)
    query_normed = norm_rows(query_heads, query_norm_gain).astype(jnp.bfloat16)
    key_normed = norm_rows(key_before_norm, key_norm_gain).astype(jnp.bfloat16)
    value_cast = value_before_norm.astype(jnp.bfloat16)
    positions = jnp.arange(shard_len)
    is_valid = positions < real_token_count[0]
    valid_rows = is_valid.astype(jnp.float32)
    local_codes = jnp.where(is_valid, document_index + 1, 0)
    local_pair = jnp.concatenate([key_normed, value_cast], axis=1)
    code_rows = jnp.zeros((16, local_pair.shape[1]), jnp.bfloat16)
    code_rows = code_rows.at[0, :shard_len].set(local_codes.astype(jnp.bfloat16))
    payload = jnp.concatenate([local_pair, code_rows], axis=0)
    payload_rows = payload.shape[0]
    if send_count == 4:
        two_back = passed_along(payload, "ctx", 2)
        odd_back = passed_along(jnp.concatenate([payload, two_back], axis=0), "ctx", 1)
        arrivals = [
            odd_back[:payload_rows],
            two_back,
            odd_back[payload_rows:],
            passed_along(two_back, "ctx", 2),
        ]
    else:
        arrivals = [
            passed_along(payload, "ctx", hop_index) for hop_index in range(1, send_count + 1)
        ]
    received = [
        (arrived[:shard_len], arrived[shard_len, :shard_len].astype(jnp.int32))
        for arrived in arrivals
    ]
    missing = reach_shards - send_count
    blank_pair = jnp.zeros_like(local_pair)
    blank_codes = jnp.zeros_like(local_codes)
    earlier = [(blank_pair, blank_codes)] * missing + list(reversed(received))
    key_pairs = jnp.concatenate([entry[0] for entry in earlier] + [local_pair], axis=0)
    key_codes_all = jnp.concatenate([entry[1] for entry in earlier] + [local_codes], axis=0)
    keys_all = key_pairs[:, :head_dim]
    values_all = key_pairs[:, head_dim:]
    allowed = window_mask(document_index, key_codes_all)
    scores = (
        jnp.einsum("thd,sd->hts", query_normed, keys_all, preferred_element_type=jnp.float32)
        * score_scale
    )
    weights = jnp.where(allowed[None], jnp.exp(scores), 0.0)
    attn_probs = weights / jnp.sum(weights, axis=-1, keepdims=True)
    probs_cast = attn_probs.astype(jnp.bfloat16)
    attention_result = jnp.einsum(
        "hts,sd->thd", probs_cast, values_all, preferred_element_type=jnp.float32
    )
    attention_result = (
        (attention_result * valid_rows[:, None, None])
        .astype(jnp.bfloat16)
        .reshape(shard_len, heads_here * head_dim)
    )
    out_parts = matrix_product(
        attention_result, jnp.concatenate([output_projection, adapter_output_down], axis=1)
    )
    summed_parts = tp_sum_scatter(out_parts.astype(jnp.bfloat16))
    output_total = summed_parts[:, :model_width]
    mid_sum = summed_parts[:, model_width:]
    middle_output = mid_sum.astype(jnp.bfloat16)
    apply_prenorm = output_total + adapter_scale * matrix_product(middle_output, adapter_output_up)
    layer_out = norm_rows(apply_prenorm, output_norm_gain).astype(jnp.bfloat16)
    prenorm_gradient = norm_back(
        apply_prenorm, output_norm_gain, output_gradient.astype(jnp.float32)
    ).astype(jnp.bfloat16)
    middle_output_gradient = (
        adapter_scale * multiply_by_transpose(prenorm_gradient, adapter_output_up)
    ).astype(jnp.bfloat16)
    complete_gradient = tp_gather(prenorm_gradient)
    middle_pair = tp_gather(jnp.concatenate([middle_output_gradient, middle_output], axis=1))
    middle_complete_gradient = middle_pair[:, :adapter_product]
    middle_complete = middle_pair[:, adapter_product:]
    gradient_portion = lax.dynamic_slice_in_dim(
        complete_gradient, tp_index * slice_width, slice_width, 1
    )
    output_up_contribution = adapter_scale * transpose_multiply(middle_complete, gradient_portion)
    attention_gradient = multiply_by_transpose(
        complete_gradient, output_projection
    ) + multiply_by_transpose(middle_complete_gradient, adapter_output_down)
    attention_gradient = (attention_gradient * valid_rows[:, None]).astype(jnp.bfloat16)
    down_out_term = transpose_multiply(attention_result, middle_complete_gradient)
    grad_heads = attention_gradient.reshape(shard_len, heads_here, head_dim)
    grad_probs = jnp.einsum(
        "thd,sd->hts", grad_heads, values_all, preferred_element_type=jnp.float32
    )
    inner_sum = jnp.sum(attn_probs * grad_probs, axis=-1, keepdims=True)
    grad_scores = lax.optimization_barrier(
        (attn_probs * (grad_probs - inner_sum) * score_scale).astype(jnp.bfloat16)
    )
    grad_query = jnp.einsum(
        "hts,sd->thd", grad_scores, keys_all, preferred_element_type=jnp.float32
    )
    grad_keys = jnp.einsum(
        "hts,thd->sd", grad_scores, query_normed, preferred_element_type=jnp.float32
    )
    grad_values = jnp.einsum(
        "hts,thd->sd", probs_cast, grad_heads, preferred_element_type=jnp.float32
    )
    grad_pairs = jnp.concatenate([grad_keys, grad_values], axis=1)
    own_grads = grad_pairs[reach_shards * shard_len :]

    def hop_block(hop_index):
        first_row = (reach_shards - hop_index) * shard_len
        return grad_pairs[first_row : first_row + shard_len]

    if send_count == 4:
        far = passed_along(
            jnp.concatenate([hop_block(3), hop_block(4)], axis=0).astype(jnp.bfloat16), "ctx", -2
        ).astype(jnp.float32)
        near_sum = hop_block(1) + far[:shard_len]
        next_sum = hop_block(2) + far[shard_len:]
        own_grads = (
            own_grads
            + passed_along(near_sum.astype(jnp.bfloat16), "ctx", -1).astype(jnp.float32)
            + passed_along(next_sum.astype(jnp.bfloat16), "ctx", -2).astype(jnp.float32)
        )
    else:
        for hop_index in range(1, send_count + 1):
            own_grads = own_grads + passed_along(
                hop_block(hop_index).astype(jnp.bfloat16), "ctx", -hop_index
            ).astype(jnp.float32)
    query_prenorm_gradient = (
        norm_back(query_heads, query_norm_gain, grad_query)
        .reshape(shard_len, heads_here * head_dim)
        .astype(jnp.bfloat16)
    )
    key_prenorm_gradient = norm_back(
        key_before_norm, key_norm_gain, own_grads[:, :head_dim]
    ).astype(jnp.bfloat16)
    value_prenorm_gradient = own_grads[:, head_dim:].astype(jnp.bfloat16)
    query_up_contribution = adapter_scale * transpose_multiply(middle_query, query_prenorm_gradient)
    key_up_contribution = adapter_scale * transpose_multiply(middle_key, key_prenorm_gradient)
    value_up_contribution = adapter_scale * transpose_multiply(middle_value, value_prenorm_gradient)
    middle_gradients = jnp.concatenate(
        [
            adapter_scale * multiply_by_transpose(query_prenorm_gradient, adapter_query_up),
            adapter_scale * multiply_by_transpose(key_prenorm_gradient, adapter_key_up),
            adapter_scale * multiply_by_transpose(value_prenorm_gradient, adapter_value_up),
        ],
        axis=1,
    ).astype(jnp.bfloat16)
    grad_normed = multiply_by_transpose(
        jnp.concatenate(
            [query_prenorm_gradient, key_prenorm_gradient, value_prenorm_gradient, middle_gradients],
            axis=1,
        ),
        all_weights,
    )
    grad_normed_rows = tp_sum_scatter(grad_normed.astype(jnp.bfloat16))
    grad_in = norm_back(tok_float, input_norm_gain, grad_normed_rows).astype(jnp.bfloat16)
    down_term = tp_sum_scatter(
        transpose_multiply(normalized_input, middle_gradients).astype(jnp.bfloat16)
    )
    adapter_totals = ctx_sum(
        [
            down_term,
            query_up_contribution,
            key_up_contribution,
            value_up_contribution,
            down_out_term,
            output_up_contribution,
        ]
    )
    return (
        layer_out,
        grad_in,
        adapter_totals[0],
        adapter_totals[1],
        adapter_totals[2],
        adapter_totals[3],
        adapter_totals[4],
        adapter_totals[5],
    )


def solution(mesh):
    in_specs = (
        P(("groups", "ctx", "tp"), None),
        P(("groups", "ctx", "tp"), None),
        P(("groups", "ctx")),
        P(("groups", "ctx")),
        P(),
        P(),
        P(),
        P(),
        P(None, "tp"),
        P(None, "tp"),
        P(None, "tp"),
        P("tp", None),
        P(),
        P(None, "tp"),
        P(None, "tp"),
        P(None, "tp"),
        P("tp", None),
        P(),
    )
    out_specs = (
        P(("groups", "ctx", "tp"), None),
        P(("groups", "ctx", "tp"), None),
        P(("groups", "tp"), None),
        P("groups", "tp"),
        P("groups", "tp"),
        P("groups", "tp"),
        P(("groups", "tp"), None),
        P("groups", "tp"),
    )
    return jax.shard_map(
        on_device, mesh=mesh, in_specs=in_specs, out_specs=out_specs, check_vma=False
    )
```

```python
import jax
import jax.numpy as jnp
from jax import lax
from jax.sharding import PartitionSpec as P

WINDOW = 1024


epsilon = 1e-06
adapter_scale = 2.0
score_scale = 168.0 ** (-0.5)


def passed_along(value, axis, steps):
    count = lax.axis_size(axis)
    leading, last = (max(0, -steps), min(count, count - steps))
    return lax.ppermute(value, axis, [(source, source + steps) for source in range(leading, last)])


def norm_rows(source, gain_vec):
    inverse = lax.rsqrt(jnp.mean(source * source, axis=-1, keepdims=True) + epsilon)
    return source * inverse * gain_vec


def norm_back(source, gain_vec, incoming):
    inverse = lax.rsqrt(jnp.mean(source * source, axis=-1, keepdims=True) + epsilon)
    scaled = source * inverse
    upward = incoming * gain_vec
    return inverse * (upward - scaled * jnp.mean(upward * scaled, axis=-1, keepdims=True))


def matrix_product(first_op, second_op):
    return jnp.dot(first_op, second_op, preferred_element_type=jnp.float32)


def multiply_by_transpose(first_op, second_op):
    return lax.dot_general(
        first_op, second_op, (((1,), (1,)), ((), ())), preferred_element_type=jnp.float32
    )


def transpose_multiply(first_op, second_op):
    return lax.dot_general(
        first_op, second_op, (((0,), (0,)), ((), ())), preferred_element_type=jnp.float32
    )


def window_mask(query_segs, key_codes):
    query_count = query_segs.shape[0]
    key_total = key_codes.shape[0]
    distance = (key_total - query_count + jnp.arange(query_count))[:, None] - jnp.arange(key_total)[
        None, :
    ]
    same_doc = key_codes[None, :] == query_segs[:, None] + 1
    return (distance == 0) | (distance > 0) & (distance < WINDOW) & same_doc


def tp_sum_scatter(value):
    if lax.axis_size("tp") != 2:
        return lax.psum_scatter(value, "tp", scatter_dimension=0, tiled=True).astype(jnp.float32)
    half = value.shape[0] // 2
    tp_index = lax.axis_index("tp")
    mine = lax.dynamic_slice_in_dim(value, tp_index * half, half, 0)
    theirs = lax.dynamic_slice_in_dim(value, (1 - tp_index) * half, half, 0)
    received = lax.ppermute(theirs, "tp", [(0, 1), (1, 0)])
    return mine.astype(jnp.float32) + received.astype(jnp.float32)


def tp_gather(value):
    if lax.axis_size("tp") != 2:
        return lax.all_gather(value, "tp", axis=0, tiled=True)
    received = lax.ppermute(value, "tp", [(0, 1), (1, 0)])
    first = lax.axis_index("tp") == 0
    return jnp.concatenate(
        [jnp.where(first, value, received), jnp.where(first, received, value)], axis=0
    )


def ctx_sum(parts):
    count = lax.axis_size("ctx")
    if count & (count - 1):
        return [lax.psum(p.astype(jnp.bfloat16), "ctx").astype(jnp.float32) for p in parts]
    flat = jnp.concatenate([p.astype(jnp.float32).reshape(-1) for p in parts])
    step = 1
    while step < count:
        sent = flat.astype(jnp.bfloat16)
        received = lax.ppermute(sent, "ctx", [(i, i ^ step) for i in range(count)])
        flat = sent.astype(jnp.float32) + received.astype(jnp.float32)
        step *= 2
    results, offset = [], 0
    for p in parts:
        results.append(flat[offset : offset + p.size].reshape(p.shape))
        offset += p.size
    return results


def on_device(
    tokens,
    output_gradient,
    document_index,
    real_token_count,
    input_norm_gain,
    query_norm_gain,
    key_norm_gain,
    output_norm_gain,
    query_projection,
    key_projection,
    value_projection,
    output_projection,
    adapter_down_maps,
    adapter_query_up,
    adapter_key_up,
    adapter_value_up,
    adapter_output_down,
    adapter_output_up,
):
    row_count, model_width = tokens.shape
    shard_len = document_index.shape[0]
    head_dim = key_projection.shape[1]
    adapter_product = adapter_key_up.shape[0]
    heads_here = query_projection.shape[1] // head_dim
    ctx_size = lax.axis_size("ctx")
    tp_index = lax.axis_index("tp")
    slice_width = model_width // lax.axis_size("tp")
    reach_shards = WINDOW // shard_len
    send_count = min(reach_shards, ctx_size - 1)
    tok_float = tokens.astype(jnp.float32)
    normed_rows = norm_rows(tok_float, input_norm_gain).astype(jnp.bfloat16)
    normalized_input = tp_gather(normed_rows)
    query_width = query_projection.shape[1]
    key_end = query_width + head_dim
    value_end = key_end + head_dim
    all_weights = jnp.concatenate(
        [query_projection, key_projection, value_projection, adapter_down_maps], axis=1
    )
    projected = matrix_product(normalized_input, all_weights)
    middle_list = projected[:, value_end:].astype(jnp.bfloat16)
    middle_query = middle_list[:, :adapter_product]
    middle_key = middle_list[:, adapter_product : 2 * adapter_product]
    middle_value = middle_list[:, 2 * adapter_product :]
    query_before_norm = projected[:, :query_width] + adapter_scale * matrix_product(
        middle_query, adapter_query_up
    )
    key_before_norm = projected[:, query_width:key_end] + adapter_scale * matrix_product(
        middle_key, adapter_key_up
    )
    value_before_norm = projected[:, key_end:value_end] + adapter_scale * matrix_product(
        middle_value, adapter_value_up
    )
    query_heads = query_before_norm.reshape(shard_len, heads_here, head_dim)
    query_normed = norm_rows(query_heads, query_norm_gain).astype(jnp.bfloat16)
    key_normed = norm_rows(key_before_norm, key_norm_gain).astype(jnp.bfloat16)
    value_cast = value_before_norm.astype(jnp.bfloat16)
    positions = jnp.arange(shard_len)
    is_valid = positions < real_token_count[0]
    valid_rows = is_valid.astype(jnp.float32)
    local_codes = jnp.where(is_valid, document_index + 1, 0)
    local_pair = jnp.concatenate([key_normed, value_cast], axis=1)
    code_rows = jnp.zeros((16, local_pair.shape[1]), jnp.bfloat16)
    code_rows = code_rows.at[0, :shard_len].set(local_codes.astype(jnp.bfloat16))
    payload = jnp.concatenate([local_pair, code_rows], axis=0)
    payload_rows = payload.shape[0]
    if send_count == 4:
        two_back = passed_along(payload, "ctx", 2)
        odd_back = passed_along(jnp.concatenate([payload, two_back], axis=0), "ctx", 1)
        arrivals = [
            odd_back[:payload_rows],
            two_back,
            odd_back[payload_rows:],
            passed_along(two_back, "ctx", 2),
        ]
    else:
        arrivals = [
            passed_along(payload, "ctx", hop_index) for hop_index in range(1, send_count + 1)
        ]
    received = [
        (arrived[:shard_len], arrived[shard_len, :shard_len].astype(jnp.int32))
        for arrived in arrivals
    ]
    missing = reach_shards - send_count
    blank_pair = jnp.zeros_like(local_pair)
    blank_codes = jnp.zeros_like(local_codes)
    earlier = [(blank_pair, blank_codes)] * missing + list(reversed(received))
    key_pairs = jnp.concatenate([entry[0] for entry in earlier] + [local_pair], axis=0)
    key_codes_all = jnp.concatenate([entry[1] for entry in earlier] + [local_codes], axis=0)
    keys_all = key_pairs[:, :head_dim]
    values_all = key_pairs[:, head_dim:]
    allowed = window_mask(document_index, key_codes_all)
    scores = (
        jnp.einsum("thd,sd->hts", query_normed, keys_all, preferred_element_type=jnp.float32)
        * score_scale
    )
    weights = jnp.where(allowed[None], jnp.exp(scores), 0.0)
    attn_probs = weights / jnp.sum(weights, axis=-1, keepdims=True)
    probs_cast = attn_probs.astype(jnp.bfloat16)
    attention_result = jnp.einsum(
        "hts,sd->thd", probs_cast, values_all, preferred_element_type=jnp.float32
    )
    attention_result = (
        (attention_result * valid_rows[:, None, None])
        .astype(jnp.bfloat16)
        .reshape(shard_len, heads_here * head_dim)
    )
    part_out = matrix_product(attention_result, output_projection)
    partial_middle = matrix_product(attention_result, adapter_output_down)
    output_total = tp_sum_scatter(part_out.astype(jnp.bfloat16))
    mid_sum = tp_sum_scatter(partial_middle.astype(jnp.bfloat16))
    middle_output = mid_sum.astype(jnp.bfloat16)
    apply_prenorm = output_total + adapter_scale * matrix_product(middle_output, adapter_output_up)
    layer_out = norm_rows(apply_prenorm, output_norm_gain).astype(jnp.bfloat16)
    prenorm_gradient = norm_back(
        apply_prenorm, output_norm_gain, output_gradient.astype(jnp.float32)
    ).astype(jnp.bfloat16)
    middle_output_gradient = (
        adapter_scale * multiply_by_transpose(prenorm_gradient, adapter_output_up)
    ).astype(jnp.bfloat16)
    complete_gradient = tp_gather(prenorm_gradient)
    middle_pair = tp_gather(jnp.concatenate([middle_output_gradient, middle_output], axis=1))
    middle_complete_gradient = middle_pair[:, :adapter_product]
    middle_complete = middle_pair[:, adapter_product:]
    gradient_portion = lax.dynamic_slice_in_dim(
        complete_gradient, tp_index * slice_width, slice_width, 1
    )
    output_up_contribution = adapter_scale * transpose_multiply(middle_complete, gradient_portion)
    attention_gradient = multiply_by_transpose(
        complete_gradient, output_projection
    ) + multiply_by_transpose(middle_complete_gradient, adapter_output_down)
    attention_gradient = (attention_gradient * valid_rows[:, None]).astype(jnp.bfloat16)
    down_out_term = transpose_multiply(attention_result, middle_complete_gradient)
    grad_heads = attention_gradient.reshape(shard_len, heads_here, head_dim)
    grad_probs = jnp.einsum(
        "thd,sd->hts", grad_heads, values_all, preferred_element_type=jnp.float32
    )
    inner_sum = jnp.sum(attn_probs * grad_probs, axis=-1, keepdims=True)
    grad_scores = lax.optimization_barrier(
        (attn_probs * (grad_probs - inner_sum) * score_scale).astype(jnp.bfloat16)
    )
    grad_query = jnp.einsum(
        "hts,sd->thd", grad_scores, keys_all, preferred_element_type=jnp.float32
    )
    grad_keys = jnp.einsum(
        "hts,thd->sd", grad_scores, query_normed, preferred_element_type=jnp.float32
    )
    grad_values = jnp.einsum(
        "hts,thd->sd", probs_cast, grad_heads, preferred_element_type=jnp.float32
    )
    grad_pairs = jnp.concatenate([grad_keys, grad_values], axis=1)
    own_grads = grad_pairs[reach_shards * shard_len :]

    def hop_block(hop_index):
        first_row = (reach_shards - hop_index) * shard_len
        return grad_pairs[first_row : first_row + shard_len]

    if send_count == 4:
        one_down = passed_along(
            jnp.concatenate([hop_block(1), hop_block(3)], axis=0).astype(jnp.bfloat16), "ctx", -1
        ).astype(jnp.float32)
        two_down = passed_along(hop_block(4).astype(jnp.bfloat16), "ctx", -2).astype(jnp.float32)
        pending = hop_block(2) + one_down[shard_len:] + two_down
        own_grads = (
            own_grads
            + one_down[:shard_len]
            + passed_along(pending.astype(jnp.bfloat16), "ctx", -2).astype(jnp.float32)
        )
    else:
        for hop_index in range(1, send_count + 1):
            own_grads = own_grads + passed_along(
                hop_block(hop_index).astype(jnp.bfloat16), "ctx", -hop_index
            ).astype(jnp.float32)
    query_prenorm_gradient = (
        norm_back(query_heads, query_norm_gain, grad_query)
        .reshape(shard_len, heads_here * head_dim)
        .astype(jnp.bfloat16)
    )
    key_prenorm_gradient = norm_back(
        key_before_norm, key_norm_gain, own_grads[:, :head_dim]
    ).astype(jnp.bfloat16)
    value_prenorm_gradient = own_grads[:, head_dim:].astype(jnp.bfloat16)
    query_up_contribution = adapter_scale * transpose_multiply(middle_query, query_prenorm_gradient)
    key_up_contribution = adapter_scale * transpose_multiply(middle_key, key_prenorm_gradient)
    value_up_contribution = adapter_scale * transpose_multiply(middle_value, value_prenorm_gradient)
    middle_gradients = jnp.concatenate(
        [
            adapter_scale * multiply_by_transpose(query_prenorm_gradient, adapter_query_up),
            adapter_scale * multiply_by_transpose(key_prenorm_gradient, adapter_key_up),
            adapter_scale * multiply_by_transpose(value_prenorm_gradient, adapter_value_up),
        ],
        axis=1,
    ).astype(jnp.bfloat16)
    grad_normed = multiply_by_transpose(
        jnp.concatenate(
            [query_prenorm_gradient, key_prenorm_gradient, value_prenorm_gradient, middle_gradients],
            axis=1,
        ),
        all_weights,
    )
    grad_normed_rows = tp_sum_scatter(grad_normed.astype(jnp.bfloat16))
    grad_in = norm_back(tok_float, input_norm_gain, grad_normed_rows).astype(jnp.bfloat16)
    down_term = tp_sum_scatter(
        transpose_multiply(normalized_input, middle_gradients).astype(jnp.bfloat16)
    )
    adapter_totals = ctx_sum(
        [
            down_term,
            query_up_contribution,
            key_up_contribution,
            value_up_contribution,
            down_out_term,
            output_up_contribution,
        ]
    )
    return (
        layer_out,
        grad_in,
        adapter_totals[0],
        adapter_totals[1],
        adapter_totals[2],
        adapter_totals[3],
        adapter_totals[4],
        adapter_totals[5],
    )


def solution(mesh):
    in_specs = (
        P(("groups", "ctx", "tp"), None),
        P(("groups", "ctx", "tp"), None),
        P(("groups", "ctx")),
        P(("groups", "ctx")),
        P(),
        P(),
        P(),
        P(),
        P(None, "tp"),
        P(None, "tp"),
        P(None, "tp"),
        P("tp", None),
        P(),
        P(None, "tp"),
        P(None, "tp"),
        P(None, "tp"),
        P("tp", None),
        P(),
    )
    out_specs = (
        P(("groups", "ctx", "tp"), None),
        P(("groups", "ctx", "tp"), None),
        P(("groups", "tp"), None),
        P("groups", "tp"),
        P("groups", "tp"),
        P("groups", "tp"),
        P(("groups", "tp"), None),
        P("groups", "tp"),
    )
    return jax.shard_map(
        on_device, mesh=mesh, in_specs=in_specs, out_specs=out_specs, check_vma=False
    )
```

```python
import jax
import jax.numpy as jnp
from jax import lax
from jax.sharding import PartitionSpec as P

WINDOW = 1024


epsilon = 1e-06
adapter_scale = 2.0
score_scale = 168.0 ** (-0.5)


def passed_along(value, axis, steps):
    count = lax.axis_size(axis)
    leading, last = (max(0, -steps), min(count, count - steps))
    return lax.ppermute(value, axis, [(source, source + steps) for source in range(leading, last)])


def norm_rows(source, gain_vec):
    inverse = lax.rsqrt(jnp.mean(source * source, axis=-1, keepdims=True) + epsilon)
    return source * inverse * gain_vec


def norm_back(source, gain_vec, incoming):
    inverse = lax.rsqrt(jnp.mean(source * source, axis=-1, keepdims=True) + epsilon)
    scaled = source * inverse
    upward = incoming * gain_vec
    return inverse * (upward - scaled * jnp.mean(upward * scaled, axis=-1, keepdims=True))


def matrix_product(first_op, second_op):
    return jnp.dot(first_op, second_op, preferred_element_type=jnp.float32)


def multiply_by_transpose(first_op, second_op):
    return lax.dot_general(
        first_op, second_op, (((1,), (1,)), ((), ())), preferred_element_type=jnp.float32
    )


def transpose_multiply(first_op, second_op):
    return lax.dot_general(
        first_op, second_op, (((0,), (0,)), ((), ())), preferred_element_type=jnp.float32
    )


def window_mask(query_segs, key_codes):
    query_count = query_segs.shape[0]
    key_total = key_codes.shape[0]
    distance = (key_total - query_count + jnp.arange(query_count))[:, None] - jnp.arange(key_total)[
        None, :
    ]
    same_doc = key_codes[None, :] == query_segs[:, None] + 1
    return (distance == 0) | (distance > 0) & (distance < WINDOW) & same_doc


def tp_sum_scatter(value):
    if lax.axis_size("tp") != 2:
        return lax.psum_scatter(value, "tp", scatter_dimension=0, tiled=True).astype(jnp.float32)
    half = value.shape[0] // 2
    tp_index = lax.axis_index("tp")
    mine = lax.dynamic_slice_in_dim(value, tp_index * half, half, 0)
    theirs = lax.dynamic_slice_in_dim(value, (1 - tp_index) * half, half, 0)
    received = lax.ppermute(theirs, "tp", [(0, 1), (1, 0)])
    return mine.astype(jnp.float32) + received.astype(jnp.float32)


def tp_gather(value):
    if lax.axis_size("tp") != 2:
        return lax.all_gather(value, "tp", axis=0, tiled=True)
    received = lax.ppermute(value, "tp", [(0, 1), (1, 0)])
    first = lax.axis_index("tp") == 0
    return jnp.concatenate(
        [jnp.where(first, value, received), jnp.where(first, received, value)], axis=0
    )


def ctx_sum(parts):
    count = lax.axis_size("ctx")
    if count & (count - 1):
        return [lax.psum(p.astype(jnp.bfloat16), "ctx").astype(jnp.float32) for p in parts]
    flat = jnp.concatenate([p.astype(jnp.float32).reshape(-1) for p in parts])
    step = count // 2
    while step >= 1:
        sent = flat.astype(jnp.bfloat16)
        received = lax.ppermute(sent, "ctx", [(i, i ^ step) for i in range(count)])
        flat = sent.astype(jnp.float32) + received.astype(jnp.float32)
        step //= 2
    results, offset = [], 0
    for p in parts:
        results.append(flat[offset : offset + p.size].reshape(p.shape))
        offset += p.size
    return results


def on_device(
    tokens,
    output_gradient,
    document_index,
    real_token_count,
    input_norm_gain,
    query_norm_gain,
    key_norm_gain,
    output_norm_gain,
    query_projection,
    key_projection,
    value_projection,
    output_projection,
    adapter_down_maps,
    adapter_query_up,
    adapter_key_up,
    adapter_value_up,
    adapter_output_down,
    adapter_output_up,
):
    row_count, model_width = tokens.shape
    shard_len = document_index.shape[0]
    head_dim = key_projection.shape[1]
    adapter_product = adapter_key_up.shape[0]
    heads_here = query_projection.shape[1] // head_dim
    ctx_size = lax.axis_size("ctx")
    tp_index = lax.axis_index("tp")
    slice_width = model_width // lax.axis_size("tp")
    reach_shards = WINDOW // shard_len
    send_count = min(reach_shards, ctx_size - 1)
    tok_float = tokens.astype(jnp.float32)
    normed_rows = norm_rows(tok_float, input_norm_gain).astype(jnp.bfloat16)
    normalized_input = tp_gather(normed_rows)
    query_width = query_projection.shape[1]
    key_end = query_width + head_dim
    value_end = key_end + head_dim
    all_weights = jnp.concatenate(
        [query_projection, key_projection, value_projection, adapter_down_maps], axis=1
    )
    projected = matrix_product(normalized_input, all_weights)
    middle_list = projected[:, value_end:].astype(jnp.bfloat16)
    middle_query = middle_list[:, :adapter_product]
    middle_key = middle_list[:, adapter_product : 2 * adapter_product]
    middle_value = middle_list[:, 2 * adapter_product :]
    query_before_norm = projected[:, :query_width] + adapter_scale * matrix_product(
        middle_query, adapter_query_up
    )
    key_before_norm = projected[:, query_width:key_end] + adapter_scale * matrix_product(
        middle_key, adapter_key_up
    )
    value_before_norm = projected[:, key_end:value_end] + adapter_scale * matrix_product(
        middle_value, adapter_value_up
    )
    query_heads = query_before_norm.reshape(shard_len, heads_here, head_dim)
    query_normed = norm_rows(query_heads, query_norm_gain).astype(jnp.bfloat16)
    key_normed = norm_rows(key_before_norm, key_norm_gain).astype(jnp.bfloat16)
    value_cast = value_before_norm.astype(jnp.bfloat16)
    positions = jnp.arange(shard_len)
    is_valid = positions < real_token_count[0]
    valid_rows = is_valid.astype(jnp.float32)
    local_codes = jnp.where(is_valid, document_index + 1, 0)
    local_pair = jnp.concatenate([key_normed, value_cast], axis=1)
    code_rows = jnp.zeros((16, local_pair.shape[1]), jnp.bfloat16)
    code_rows = code_rows.at[0, :shard_len].set(local_codes.astype(jnp.bfloat16))
    payload = jnp.concatenate([local_pair, code_rows], axis=0)
    payload_rows = payload.shape[0]
    if send_count == 4:
        two_back = passed_along(payload, "ctx", 2)
        odd_back = passed_along(jnp.concatenate([payload, two_back], axis=0), "ctx", 1)
        arrivals = [
            odd_back[:payload_rows],
            two_back,
            odd_back[payload_rows:],
            passed_along(two_back, "ctx", 2),
        ]
    else:
        arrivals = [
            passed_along(payload, "ctx", hop_index) for hop_index in range(1, send_count + 1)
        ]
    received = [
        (arrived[:shard_len], arrived[shard_len, :shard_len].astype(jnp.int32))
        for arrived in arrivals
    ]
    missing = reach_shards - send_count
    blank_pair = jnp.zeros_like(local_pair)
    blank_codes = jnp.zeros_like(local_codes)
    earlier = [(blank_pair, blank_codes)] * missing + list(reversed(received))
    key_pairs = jnp.concatenate([entry[0] for entry in earlier] + [local_pair], axis=0)
    key_codes_all = jnp.concatenate([entry[1] for entry in earlier] + [local_codes], axis=0)
    keys_all = key_pairs[:, :head_dim]
    values_all = key_pairs[:, head_dim:]
    allowed = window_mask(document_index, key_codes_all)
    scores = (
        jnp.einsum("thd,sd->hts", query_normed, keys_all, preferred_element_type=jnp.float32)
        * score_scale
    )
    weights = jnp.where(allowed[None], jnp.exp(scores), 0.0)
    attn_probs = weights / jnp.sum(weights, axis=-1, keepdims=True)
    probs_cast = attn_probs.astype(jnp.bfloat16)
    attention_result = jnp.einsum(
        "hts,sd->thd", probs_cast, values_all, preferred_element_type=jnp.float32
    )
    attention_result = (
        (attention_result * valid_rows[:, None, None])
        .astype(jnp.bfloat16)
        .reshape(shard_len, heads_here * head_dim)
    )
    part_out = matrix_product(attention_result, output_projection)
    partial_middle = matrix_product(attention_result, adapter_output_down)
    output_total = tp_sum_scatter(part_out.astype(jnp.bfloat16))
    mid_sum = tp_sum_scatter(partial_middle.astype(jnp.bfloat16))
    middle_output = mid_sum.astype(jnp.bfloat16)
    apply_prenorm = output_total + adapter_scale * matrix_product(middle_output, adapter_output_up)
    layer_out = norm_rows(apply_prenorm, output_norm_gain).astype(jnp.bfloat16)
    prenorm_gradient = norm_back(
        apply_prenorm, output_norm_gain, output_gradient.astype(jnp.float32)
    ).astype(jnp.bfloat16)
    middle_output_gradient = (
        adapter_scale * multiply_by_transpose(prenorm_gradient, adapter_output_up)
    ).astype(jnp.bfloat16)
    complete_gradient = tp_gather(prenorm_gradient)
    middle_pair = tp_gather(jnp.concatenate([middle_output_gradient, middle_output], axis=1))
    middle_complete_gradient = middle_pair[:, :adapter_product]
    middle_complete = middle_pair[:, adapter_product:]
    gradient_portion = lax.dynamic_slice_in_dim(
        complete_gradient, tp_index * slice_width, slice_width, 1
    )
    output_up_contribution = adapter_scale * transpose_multiply(middle_complete, gradient_portion)
    attention_gradient = multiply_by_transpose(
        complete_gradient, output_projection
    ) + multiply_by_transpose(middle_complete_gradient, adapter_output_down)
    attention_gradient = (attention_gradient * valid_rows[:, None]).astype(jnp.bfloat16)
    down_out_term = transpose_multiply(attention_result, middle_complete_gradient)
    grad_heads = attention_gradient.reshape(shard_len, heads_here, head_dim)
    grad_probs = jnp.einsum(
        "thd,sd->hts", grad_heads, values_all, preferred_element_type=jnp.float32
    )
    inner_sum = jnp.sum(attn_probs * grad_probs, axis=-1, keepdims=True)
    grad_scores = lax.optimization_barrier(
        (attn_probs * (grad_probs - inner_sum) * score_scale).astype(jnp.bfloat16)
    )
    grad_query = jnp.einsum(
        "hts,sd->thd", grad_scores, keys_all, preferred_element_type=jnp.float32
    )
    grad_keys = jnp.einsum(
        "hts,thd->sd", grad_scores, query_normed, preferred_element_type=jnp.float32
    )
    grad_values = jnp.einsum(
        "hts,thd->sd", probs_cast, grad_heads, preferred_element_type=jnp.float32
    )
    grad_pairs = jnp.concatenate([grad_keys, grad_values], axis=1)
    own_grads = grad_pairs[reach_shards * shard_len :]

    def hop_block(hop_index):
        first_row = (reach_shards - hop_index) * shard_len
        return grad_pairs[first_row : first_row + shard_len]

    if send_count == 4:
        far = passed_along(
            jnp.concatenate([hop_block(3), hop_block(4)], axis=0).astype(jnp.bfloat16), "ctx", -2
        ).astype(jnp.float32)
        near_sum = hop_block(1) + far[:shard_len]
        next_sum = hop_block(2) + far[shard_len:]
        own_grads = (
            own_grads
            + passed_along(near_sum.astype(jnp.bfloat16), "ctx", -1).astype(jnp.float32)
            + passed_along(next_sum.astype(jnp.bfloat16), "ctx", -2).astype(jnp.float32)
        )
    else:
        for hop_index in range(1, send_count + 1):
            own_grads = own_grads + passed_along(
                hop_block(hop_index).astype(jnp.bfloat16), "ctx", -hop_index
            ).astype(jnp.float32)
    query_prenorm_gradient = (
        norm_back(query_heads, query_norm_gain, grad_query)
        .reshape(shard_len, heads_here * head_dim)
        .astype(jnp.bfloat16)
    )
    key_prenorm_gradient = norm_back(
        key_before_norm, key_norm_gain, own_grads[:, :head_dim]
    ).astype(jnp.bfloat16)
    value_prenorm_gradient = own_grads[:, head_dim:].astype(jnp.bfloat16)
    query_up_contribution = adapter_scale * transpose_multiply(middle_query, query_prenorm_gradient)
    key_up_contribution = adapter_scale * transpose_multiply(middle_key, key_prenorm_gradient)
    value_up_contribution = adapter_scale * transpose_multiply(middle_value, value_prenorm_gradient)
    middle_gradients = jnp.concatenate(
        [
            adapter_scale * multiply_by_transpose(query_prenorm_gradient, adapter_query_up),
            adapter_scale * multiply_by_transpose(key_prenorm_gradient, adapter_key_up),
            adapter_scale * multiply_by_transpose(value_prenorm_gradient, adapter_value_up),
        ],
        axis=1,
    ).astype(jnp.bfloat16)
    grad_normed = multiply_by_transpose(
        jnp.concatenate(
            [query_prenorm_gradient, key_prenorm_gradient, value_prenorm_gradient, middle_gradients],
            axis=1,
        ),
        all_weights,
    )
    grad_normed_rows = tp_sum_scatter(grad_normed.astype(jnp.bfloat16))
    grad_in = norm_back(tok_float, input_norm_gain, grad_normed_rows).astype(jnp.bfloat16)
    down_term = tp_sum_scatter(
        transpose_multiply(normalized_input, middle_gradients).astype(jnp.bfloat16)
    )
    adapter_totals = ctx_sum(
        [
            down_term,
            query_up_contribution,
            key_up_contribution,
            value_up_contribution,
            down_out_term,
            output_up_contribution,
        ]
    )
    return (
        layer_out,
        grad_in,
        adapter_totals[0],
        adapter_totals[1],
        adapter_totals[2],
        adapter_totals[3],
        adapter_totals[4],
        adapter_totals[5],
    )


def solution(mesh):
    in_specs = (
        P(("groups", "ctx", "tp"), None),
        P(("groups", "ctx", "tp"), None),
        P(("groups", "ctx")),
        P(("groups", "ctx")),
        P(),
        P(),
        P(),
        P(),
        P(None, "tp"),
        P(None, "tp"),
        P(None, "tp"),
        P("tp", None),
        P(),
        P(None, "tp"),
        P(None, "tp"),
        P(None, "tp"),
        P("tp", None),
        P(),
    )
    out_specs = (
        P(("groups", "ctx", "tp"), None),
        P(("groups", "ctx", "tp"), None),
        P(("groups", "tp"), None),
        P("groups", "tp"),
        P("groups", "tp"),
        P("groups", "tp"),
        P(("groups", "tp"), None),
        P("groups", "tp"),
    )
    return jax.shard_map(
        on_device, mesh=mesh, in_specs=in_specs, out_specs=out_specs, check_vma=False
    )
```

```python
import jax
import jax.numpy as jnp
from jax import lax
from jax.sharding import PartitionSpec as P

WINDOW = 1024


epsilon = 1e-06
adapter_scale = 2.0
score_scale = 168.0 ** (-0.5)


def passed_along(value, axis, steps):
    count = lax.axis_size(axis)
    leading, last = (max(0, -steps), min(count, count - steps))
    return lax.ppermute(value, axis, [(source, source + steps) for source in range(leading, last)])


def norm_rows(source, gain_vec):
    inverse = lax.rsqrt(jnp.mean(source * source, axis=-1, keepdims=True) + epsilon)
    return source * inverse * gain_vec


def norm_back(source, gain_vec, incoming):
    inverse = lax.rsqrt(jnp.mean(source * source, axis=-1, keepdims=True) + epsilon)
    scaled = source * inverse
    upward = incoming * gain_vec
    return inverse * (upward - scaled * jnp.mean(upward * scaled, axis=-1, keepdims=True))


def matrix_product(first_op, second_op):
    return jnp.dot(first_op, second_op, preferred_element_type=jnp.float32)


def multiply_by_transpose(first_op, second_op):
    return lax.dot_general(
        first_op, second_op, (((1,), (1,)), ((), ())), preferred_element_type=jnp.float32
    )


def transpose_multiply(first_op, second_op):
    return lax.dot_general(
        first_op, second_op, (((0,), (0,)), ((), ())), preferred_element_type=jnp.float32
    )


def window_mask(query_segs, key_codes):
    query_count = query_segs.shape[0]
    key_total = key_codes.shape[0]
    distance = (key_total - query_count + jnp.arange(query_count))[:, None] - jnp.arange(key_total)[
        None, :
    ]
    same_doc = key_codes[None, :] == query_segs[:, None] + 1
    return (distance == 0) | (distance > 0) & (distance < WINDOW) & same_doc


def tp_sum_scatter(value):
    if lax.axis_size("tp") != 2:
        return lax.psum_scatter(value, "tp", scatter_dimension=0, tiled=True).astype(jnp.float32)
    half = value.shape[0] // 2
    tp_index = lax.axis_index("tp")
    mine = lax.dynamic_slice_in_dim(value, tp_index * half, half, 0)
    theirs = lax.dynamic_slice_in_dim(value, (1 - tp_index) * half, half, 0)
    received = lax.ppermute(theirs, "tp", [(0, 1), (1, 0)])
    return mine.astype(jnp.float32) + received.astype(jnp.float32)


def tp_gather(value):
    if lax.axis_size("tp") != 2:
        return lax.all_gather(value, "tp", axis=0, tiled=True)
    received = lax.ppermute(value, "tp", [(0, 1), (1, 0)])
    first = lax.axis_index("tp") == 0
    return jnp.concatenate(
        [jnp.where(first, value, received), jnp.where(first, received, value)], axis=0
    )


def ctx_sum(parts):
    count = lax.axis_size("ctx")
    if count & (count - 1):
        return [lax.psum(p.astype(jnp.bfloat16), "ctx").astype(jnp.float32) for p in parts]
    flat = jnp.concatenate([p.astype(jnp.float32).reshape(-1) for p in parts])
    step = 1
    while step < count:
        sent = flat.astype(jnp.bfloat16)
        received = lax.ppermute(sent, "ctx", [(i, i ^ step) for i in range(count)])
        flat = sent.astype(jnp.float32) + received.astype(jnp.float32)
        step *= 2
    results, offset = [], 0
    for p in parts:
        results.append(flat[offset : offset + p.size].reshape(p.shape))
        offset += p.size
    return results


def on_device(
    tokens,
    output_gradient,
    document_index,
    real_token_count,
    input_norm_gain,
    query_norm_gain,
    key_norm_gain,
    output_norm_gain,
    query_projection,
    key_projection,
    value_projection,
    output_projection,
    adapter_down_maps,
    adapter_query_up,
    adapter_key_up,
    adapter_value_up,
    adapter_output_down,
    adapter_output_up,
):
    row_count, model_width = tokens.shape
    shard_len = document_index.shape[0]
    head_dim = key_projection.shape[1]
    adapter_product = adapter_key_up.shape[0]
    heads_here = query_projection.shape[1] // head_dim
    ctx_size = lax.axis_size("ctx")
    tp_index = lax.axis_index("tp")
    slice_width = model_width // lax.axis_size("tp")
    reach_shards = WINDOW // shard_len
    send_count = min(reach_shards, ctx_size - 1)
    tok_float = tokens.astype(jnp.float32)
    normed_rows = norm_rows(tok_float, input_norm_gain).astype(jnp.bfloat16)
    normalized_input = tp_gather(normed_rows)
    query_width = query_projection.shape[1]
    key_end = query_width + head_dim
    value_end = key_end + head_dim
    all_weights = jnp.concatenate(
        [query_projection, key_projection, value_projection, adapter_down_maps], axis=1
    )
    projected = matrix_product(normalized_input, all_weights)
    middle_list = projected[:, value_end:].astype(jnp.bfloat16)
    middle_query = middle_list[:, :adapter_product]
    middle_key = middle_list[:, adapter_product : 2 * adapter_product]
    middle_value = middle_list[:, 2 * adapter_product :]
    query_before_norm = projected[:, :query_width] + adapter_scale * matrix_product(
        middle_query, adapter_query_up
    )
    key_before_norm = projected[:, query_width:key_end] + adapter_scale * matrix_product(
        middle_key, adapter_key_up
    )
    value_before_norm = projected[:, key_end:value_end] + adapter_scale * matrix_product(
        middle_value, adapter_value_up
    )
    query_heads = query_before_norm.reshape(shard_len, heads_here, head_dim)
    query_normed = norm_rows(query_heads, query_norm_gain).astype(jnp.bfloat16)
    key_normed = norm_rows(key_before_norm, key_norm_gain).astype(jnp.bfloat16)
    value_cast = value_before_norm.astype(jnp.bfloat16)
    positions = jnp.arange(shard_len)
    is_valid = positions < real_token_count[0]
    valid_rows = is_valid.astype(jnp.float32)
    local_codes = jnp.where(is_valid, document_index + 1, 0)
    local_pair = jnp.concatenate([key_normed, value_cast], axis=1)
    code_rows = jnp.zeros((16, local_pair.shape[1]), jnp.bfloat16)
    code_rows = code_rows.at[0, :shard_len].set(local_codes.astype(jnp.bfloat16))
    payload = jnp.concatenate([local_pair, code_rows], axis=0)
    payload_rows = payload.shape[0]
    if send_count == 4:
        two_back = passed_along(payload, "ctx", 2)
        odd_back = passed_along(jnp.concatenate([payload, two_back], axis=0), "ctx", 1)
        arrivals = [
            odd_back[:payload_rows],
            two_back,
            odd_back[payload_rows:],
            passed_along(two_back, "ctx", 2),
        ]
    else:
        arrivals = [
            passed_along(payload, "ctx", hop_index) for hop_index in range(1, send_count + 1)
        ]
    received = [
        (arrived[:shard_len], arrived[shard_len, :shard_len].astype(jnp.int32))
        for arrived in arrivals
    ]
    missing = reach_shards - send_count
    blank_pair = jnp.zeros_like(local_pair)
    blank_codes = jnp.zeros_like(local_codes)
    earlier = [(blank_pair, blank_codes)] * missing + list(reversed(received))
    key_pairs = jnp.concatenate([entry[0] for entry in earlier] + [local_pair], axis=0)
    key_codes_all = jnp.concatenate([entry[1] for entry in earlier] + [local_codes], axis=0)
    keys_all = key_pairs[:, :head_dim]
    values_all = key_pairs[:, head_dim:]
    allowed = window_mask(document_index, key_codes_all)
    scores = (
        jnp.einsum("thd,sd->hts", query_normed, keys_all, preferred_element_type=jnp.float32)
        * score_scale
    )
    weights = jnp.where(allowed[None], jnp.exp(scores), 0.0)
    attn_probs = weights / jnp.sum(weights, axis=-1, keepdims=True)
    probs_cast = attn_probs.astype(jnp.bfloat16)
    attention_result = jnp.einsum(
        "hts,sd->thd", probs_cast, values_all, preferred_element_type=jnp.float32
    )
    attention_result = (
        (attention_result * valid_rows[:, None, None])
        .astype(jnp.bfloat16)
        .reshape(shard_len, heads_here * head_dim)
    )
    part_out = matrix_product(attention_result, output_projection)
    partial_middle = matrix_product(attention_result, adapter_output_down)
    output_total = tp_sum_scatter(part_out.astype(jnp.bfloat16))
    mid_sum = tp_sum_scatter(partial_middle.astype(jnp.bfloat16))
    middle_output = mid_sum.astype(jnp.bfloat16)
    apply_prenorm = output_total + adapter_scale * matrix_product(middle_output, adapter_output_up)
    layer_out = norm_rows(apply_prenorm, output_norm_gain).astype(jnp.bfloat16)
    prenorm_gradient = norm_back(
        apply_prenorm, output_norm_gain, output_gradient.astype(jnp.float32)
    ).astype(jnp.bfloat16)
    middle_output_gradient = (
        adapter_scale * multiply_by_transpose(prenorm_gradient, adapter_output_up)
    ).astype(jnp.bfloat16)
    middle_pair = tp_gather(jnp.concatenate([middle_output_gradient, middle_output], axis=1))
    middle_complete_gradient = middle_pair[:, :adapter_product]
    middle_complete = middle_pair[:, adapter_product:]
    middle_part = multiply_by_transpose(middle_complete_gradient, adapter_output_down)
    if lax.axis_size("tp") == 2:
        partner_gradient = lax.ppermute(prenorm_gradient, "tp", [(0, 1), (1, 0)])
        partner_middle = lax.ppermute(middle_output, "tp", [(0, 1), (1, 0)])
        own_portion = lax.dynamic_slice_in_dim(
            prenorm_gradient, tp_index * slice_width, slice_width, 1
        )
        partner_portion = lax.dynamic_slice_in_dim(
            partner_gradient, tp_index * slice_width, slice_width, 1
        )
        output_up_contribution = adapter_scale * (
            transpose_multiply(middle_output, own_portion)
            + transpose_multiply(partner_middle, partner_portion)
        )
        own_rows = multiply_by_transpose(prenorm_gradient, output_projection)
        partner_rows = multiply_by_transpose(partner_gradient, output_projection)
        first = tp_index == 0
        attention_gradient = (
            jnp.concatenate(
                [jnp.where(first, own_rows, partner_rows), jnp.where(first, partner_rows, own_rows)],
                axis=0,
            )
            + middle_part
        )
    else:
        complete_gradient = tp_gather(prenorm_gradient)
        gradient_portion = lax.dynamic_slice_in_dim(
            complete_gradient, tp_index * slice_width, slice_width, 1
        )
        output_up_contribution = adapter_scale * transpose_multiply(
            middle_complete, gradient_portion
        )
        attention_gradient = (
            multiply_by_transpose(complete_gradient, output_projection) + middle_part
        )
    attention_gradient = (attention_gradient * valid_rows[:, None]).astype(jnp.bfloat16)
    down_out_term = transpose_multiply(attention_result, middle_complete_gradient)
    grad_heads = attention_gradient.reshape(shard_len, heads_here, head_dim)
    grad_probs = jnp.einsum(
        "thd,sd->hts", grad_heads, values_all, preferred_element_type=jnp.float32
    )
    inner_sum = jnp.sum(attn_probs * grad_probs, axis=-1, keepdims=True)
    grad_scores = lax.optimization_barrier(
        (attn_probs * (grad_probs - inner_sum) * score_scale).astype(jnp.bfloat16)
    )
    grad_query = jnp.einsum(
        "hts,sd->thd", grad_scores, keys_all, preferred_element_type=jnp.float32
    )
    grad_keys = jnp.einsum(
        "hts,thd->sd", grad_scores, query_normed, preferred_element_type=jnp.float32
    )
    grad_values = jnp.einsum(
        "hts,thd->sd", probs_cast, grad_heads, preferred_element_type=jnp.float32
    )
    grad_pairs = jnp.concatenate([grad_keys, grad_values], axis=1)
    own_grads = grad_pairs[reach_shards * shard_len :]

    def hop_block(hop_index):
        first_row = (reach_shards - hop_index) * shard_len
        return grad_pairs[first_row : first_row + shard_len]

    if send_count == 4:
        far = passed_along(
            jnp.concatenate([hop_block(3), hop_block(4)], axis=0).astype(jnp.bfloat16), "ctx", -2
        ).astype(jnp.float32)
        near_sum = hop_block(1) + far[:shard_len]
        next_sum = hop_block(2) + far[shard_len:]
        own_grads = (
            own_grads
            + passed_along(near_sum.astype(jnp.bfloat16), "ctx", -1).astype(jnp.float32)
            + passed_along(next_sum.astype(jnp.bfloat16), "ctx", -2).astype(jnp.float32)
        )
    else:
        for hop_index in range(1, send_count + 1):
            own_grads = own_grads + passed_along(
                hop_block(hop_index).astype(jnp.bfloat16), "ctx", -hop_index
            ).astype(jnp.float32)
    query_prenorm_gradient = (
        norm_back(query_heads, query_norm_gain, grad_query)
        .reshape(shard_len, heads_here * head_dim)
        .astype(jnp.bfloat16)
    )
    key_prenorm_gradient = norm_back(
        key_before_norm, key_norm_gain, own_grads[:, :head_dim]
    ).astype(jnp.bfloat16)
    value_prenorm_gradient = own_grads[:, head_dim:].astype(jnp.bfloat16)
    query_up_contribution = adapter_scale * transpose_multiply(middle_query, query_prenorm_gradient)
    key_up_contribution = adapter_scale * transpose_multiply(middle_key, key_prenorm_gradient)
    value_up_contribution = adapter_scale * transpose_multiply(middle_value, value_prenorm_gradient)
    middle_gradients = jnp.concatenate(
        [
            adapter_scale * multiply_by_transpose(query_prenorm_gradient, adapter_query_up),
            adapter_scale * multiply_by_transpose(key_prenorm_gradient, adapter_key_up),
            adapter_scale * multiply_by_transpose(value_prenorm_gradient, adapter_value_up),
        ],
        axis=1,
    ).astype(jnp.bfloat16)
    grad_normed = multiply_by_transpose(
        jnp.concatenate(
            [query_prenorm_gradient, key_prenorm_gradient, value_prenorm_gradient, middle_gradients],
            axis=1,
        ),
        all_weights,
    )
    grad_normed_rows = tp_sum_scatter(grad_normed.astype(jnp.bfloat16))
    grad_in = norm_back(tok_float, input_norm_gain, grad_normed_rows).astype(jnp.bfloat16)
    down_term = tp_sum_scatter(
        transpose_multiply(normalized_input, middle_gradients).astype(jnp.bfloat16)
    )
    adapter_totals = ctx_sum(
        [
            down_term,
            query_up_contribution,
            key_up_contribution,
            value_up_contribution,
            down_out_term,
            output_up_contribution,
        ]
    )
    return (
        layer_out,
        grad_in,
        adapter_totals[0],
        adapter_totals[1],
        adapter_totals[2],
        adapter_totals[3],
        adapter_totals[4],
        adapter_totals[5],
    )


def solution(mesh):
    in_specs = (
        P(("groups", "ctx", "tp"), None),
        P(("groups", "ctx", "tp"), None),
        P(("groups", "ctx")),
        P(("groups", "ctx")),
        P(),
        P(),
        P(),
        P(),
        P(None, "tp"),
        P(None, "tp"),
        P(None, "tp"),
        P("tp", None),
        P(),
        P(None, "tp"),
        P(None, "tp"),
        P(None, "tp"),
        P("tp", None),
        P(),
    )
    out_specs = (
        P(("groups", "ctx", "tp"), None),
        P(("groups", "ctx", "tp"), None),
        P(("groups", "tp"), None),
        P("groups", "tp"),
        P("groups", "tp"),
        P("groups", "tp"),
        P(("groups", "tp"), None),
        P("groups", "tp"),
    )
    return jax.shard_map(
        on_device, mesh=mesh, in_specs=in_specs, out_specs=out_specs, check_vma=False
    )
```

```python
import jax
import jax.numpy as jnp
from jax import lax
from jax.sharding import PartitionSpec as P

WINDOW = 1024


epsilon = 1e-06
adapter_scale = 2.0
score_scale = 168.0 ** (-0.5)


def passed_along(value, axis, steps):
    count = lax.axis_size(axis)
    leading, last = (max(0, -steps), min(count, count - steps))
    return lax.ppermute(value, axis, [(source, source + steps) for source in range(leading, last)])


def norm_rows(source, gain_vec):
    inverse = lax.rsqrt(jnp.mean(source * source, axis=-1, keepdims=True) + epsilon)
    return source * inverse * gain_vec


def norm_back(source, gain_vec, incoming):
    inverse = lax.rsqrt(jnp.mean(source * source, axis=-1, keepdims=True) + epsilon)
    scaled = source * inverse
    upward = incoming * gain_vec
    return inverse * (upward - scaled * jnp.mean(upward * scaled, axis=-1, keepdims=True))


def matrix_product(first_op, second_op):
    return jnp.dot(first_op, second_op, preferred_element_type=jnp.float32)


def multiply_by_transpose(first_op, second_op):
    return lax.dot_general(
        first_op, second_op, (((1,), (1,)), ((), ())), preferred_element_type=jnp.float32
    )


def transpose_multiply(first_op, second_op):
    return lax.dot_general(
        first_op, second_op, (((0,), (0,)), ((), ())), preferred_element_type=jnp.float32
    )


def window_mask(query_segs, key_codes):
    query_count = query_segs.shape[0]
    key_total = key_codes.shape[0]
    distance = (key_total - query_count + jnp.arange(query_count))[:, None] - jnp.arange(key_total)[
        None, :
    ]
    same_doc = key_codes[None, :] == query_segs[:, None] + 1
    return (distance == 0) | (distance > 0) & (distance < WINDOW) & same_doc


def tp_sum_scatter(value):
    if lax.axis_size("tp") != 2:
        return lax.psum_scatter(value, "tp", scatter_dimension=0, tiled=True).astype(jnp.float32)
    half = value.shape[0] // 2
    tp_index = lax.axis_index("tp")
    mine = lax.dynamic_slice_in_dim(value, tp_index * half, half, 0)
    theirs = lax.dynamic_slice_in_dim(value, (1 - tp_index) * half, half, 0)
    received = lax.ppermute(theirs, "tp", [(0, 1), (1, 0)])
    return mine.astype(jnp.float32) + received.astype(jnp.float32)


def tp_gather(value):
    if lax.axis_size("tp") != 2:
        return lax.all_gather(value, "tp", axis=0, tiled=True)
    received = lax.ppermute(value, "tp", [(0, 1), (1, 0)])
    first = lax.axis_index("tp") == 0
    return jnp.concatenate(
        [jnp.where(first, value, received), jnp.where(first, received, value)], axis=0
    )


def ctx_sum(parts):
    count = lax.axis_size("ctx")
    if count & (count - 1):
        return [lax.psum(p.astype(jnp.bfloat16), "ctx").astype(jnp.float32) for p in parts]
    flat = jnp.concatenate([p.astype(jnp.float32).reshape(-1) for p in parts])
    step = 1
    while step < count:
        sent = flat.astype(jnp.bfloat16)
        received = lax.ppermute(sent, "ctx", [(i, i ^ step) for i in range(count)])
        flat = sent.astype(jnp.float32) + received.astype(jnp.float32)
        step *= 2
    results, offset = [], 0
    for p in parts:
        results.append(flat[offset : offset + p.size].reshape(p.shape))
        offset += p.size
    return results


def on_device(
    tokens,
    output_gradient,
    document_index,
    real_token_count,
    input_norm_gain,
    query_norm_gain,
    key_norm_gain,
    output_norm_gain,
    query_projection,
    key_projection,
    value_projection,
    output_projection,
    adapter_down_maps,
    adapter_query_up,
    adapter_key_up,
    adapter_value_up,
    adapter_output_down,
    adapter_output_up,
):
    row_count, model_width = tokens.shape
    shard_len = document_index.shape[0]
    head_dim = key_projection.shape[1]
    adapter_product = adapter_key_up.shape[0]
    heads_here = query_projection.shape[1] // head_dim
    ctx_size = lax.axis_size("ctx")
    tp_index = lax.axis_index("tp")
    slice_width = model_width // lax.axis_size("tp")
    reach_shards = WINDOW // shard_len
    send_count = min(reach_shards, ctx_size - 1)
    tok_float = tokens.astype(jnp.float32)
    normed_rows = norm_rows(tok_float, input_norm_gain).astype(jnp.bfloat16)
    normalized_input = tp_gather(normed_rows)
    query_width = query_projection.shape[1]
    key_end = query_width + head_dim
    value_end = key_end + head_dim
    all_weights = jnp.concatenate(
        [query_projection, key_projection, value_projection, adapter_down_maps], axis=1
    )
    projected = matrix_product(normalized_input, all_weights)
    middle_list = projected[:, value_end:].astype(jnp.bfloat16)
    middle_query = middle_list[:, :adapter_product]
    middle_key = middle_list[:, adapter_product : 2 * adapter_product]
    middle_value = middle_list[:, 2 * adapter_product :]
    query_before_norm = projected[:, :query_width] + adapter_scale * matrix_product(
        middle_query, adapter_query_up
    )
    key_before_norm = projected[:, query_width:key_end] + adapter_scale * matrix_product(
        middle_key, adapter_key_up
    )
    value_before_norm = projected[:, key_end:value_end] + adapter_scale * matrix_product(
        middle_value, adapter_value_up
    )
    query_heads = query_before_norm.reshape(shard_len, heads_here, head_dim)
    query_normed = norm_rows(query_heads, query_norm_gain).astype(jnp.bfloat16)
    key_normed = norm_rows(key_before_norm, key_norm_gain).astype(jnp.bfloat16)
    value_cast = value_before_norm.astype(jnp.bfloat16)
    positions = jnp.arange(shard_len)
    is_valid = positions < real_token_count[0]
    valid_rows = is_valid.astype(jnp.float32)
    local_codes = jnp.where(is_valid, document_index + 1, 0)
    local_pair = jnp.concatenate([key_normed, value_cast], axis=1)
    code_rows = jnp.zeros((16, local_pair.shape[1]), jnp.bfloat16)
    code_rows = code_rows.at[0, :shard_len].set(local_codes.astype(jnp.bfloat16))
    payload = jnp.concatenate([local_pair, code_rows], axis=0)
    payload_rows = payload.shape[0]
    if send_count == 4:
        two_back = passed_along(payload, "ctx", 2)
        odd_back = passed_along(jnp.concatenate([payload, two_back], axis=0), "ctx", 1)
        arrivals = [
            odd_back[:payload_rows],
            two_back,
            odd_back[payload_rows:],
            passed_along(two_back, "ctx", 2),
        ]
    else:
        arrivals = [
            passed_along(payload, "ctx", hop_index) for hop_index in range(1, send_count + 1)
        ]
    received = [
        (arrived[:shard_len], arrived[shard_len, :shard_len].astype(jnp.int32))
        for arrived in arrivals
    ]
    missing = reach_shards - send_count
    blank_pair = jnp.zeros_like(local_pair)
    blank_codes = jnp.zeros_like(local_codes)
    earlier = [(blank_pair, blank_codes)] * missing + list(reversed(received))
    key_pairs = jnp.concatenate([entry[0] for entry in earlier] + [local_pair], axis=0)
    key_codes_all = jnp.concatenate([entry[1] for entry in earlier] + [local_codes], axis=0)
    keys_all = key_pairs[:, :head_dim]
    values_all = key_pairs[:, head_dim:]
    allowed = window_mask(document_index, key_codes_all)
    scores = (
        jnp.einsum("thd,sd->hts", query_normed, keys_all, preferred_element_type=jnp.float32)
        * score_scale
    )
    weights = jnp.where(allowed[None], jnp.exp(scores), 0.0)
    attn_probs = weights / jnp.sum(weights, axis=-1, keepdims=True)
    probs_cast = attn_probs.astype(jnp.bfloat16)
    attention_result = jnp.einsum(
        "hts,sd->thd", probs_cast, values_all, preferred_element_type=jnp.float32
    )
    attention_result = (
        (attention_result * valid_rows[:, None, None])
        .astype(jnp.bfloat16)
        .reshape(shard_len, heads_here * head_dim)
    )
    part_out = matrix_product(attention_result, output_projection)
    partial_middle = matrix_product(attention_result, adapter_output_down)
    output_total = tp_sum_scatter(part_out.astype(jnp.bfloat16))
    mid_sum = tp_sum_scatter(partial_middle.astype(jnp.bfloat16))
    middle_output = mid_sum.astype(jnp.bfloat16)
    apply_prenorm = output_total + adapter_scale * matrix_product(middle_output, adapter_output_up)
    layer_out = norm_rows(apply_prenorm, output_norm_gain).astype(jnp.bfloat16)
    prenorm_gradient = norm_back(
        apply_prenorm, output_norm_gain, output_gradient.astype(jnp.float32)
    ).astype(jnp.bfloat16)
    middle_output_gradient = (
        adapter_scale * multiply_by_transpose(prenorm_gradient, adapter_output_up)
    ).astype(jnp.bfloat16)
    complete_gradient = tp_gather(prenorm_gradient)
    middle_pair = tp_gather(jnp.concatenate([middle_output_gradient, middle_output], axis=1))
    middle_complete_gradient = middle_pair[:, :adapter_product]
    middle_complete = middle_pair[:, adapter_product:]
    gradient_portion = lax.dynamic_slice_in_dim(
        complete_gradient, tp_index * slice_width, slice_width, 1
    )
    output_up_contribution = adapter_scale * transpose_multiply(middle_complete, gradient_portion)
    attention_gradient = multiply_by_transpose(
        complete_gradient, output_projection
    ) + multiply_by_transpose(middle_complete_gradient, adapter_output_down)
    attention_gradient = (attention_gradient * valid_rows[:, None]).astype(jnp.bfloat16)
    down_out_term = transpose_multiply(attention_result, middle_complete_gradient)
    grad_heads = attention_gradient.reshape(shard_len, heads_here, head_dim)
    grad_probs = jnp.einsum(
        "thd,sd->hts", grad_heads, values_all, preferred_element_type=jnp.float32
    )
    inner_sum = jnp.sum(attn_probs * grad_probs, axis=-1, keepdims=True)
    grad_scores = lax.optimization_barrier(
        (attn_probs * (grad_probs - inner_sum) * score_scale).astype(jnp.bfloat16)
    )
    grad_query = jnp.einsum(
        "hts,sd->thd", grad_scores, keys_all, preferred_element_type=jnp.float32
    )
    grad_keys = jnp.einsum(
        "hts,thd->sd", grad_scores, query_normed, preferred_element_type=jnp.float32
    )
    grad_values = jnp.einsum(
        "hts,thd->sd", probs_cast, grad_heads, preferred_element_type=jnp.float32
    )
    grad_pairs = jnp.concatenate([grad_keys, grad_values], axis=1)
    own_grads = grad_pairs[reach_shards * shard_len :]

    def hop_block(hop_index):
        first_row = (reach_shards - hop_index) * shard_len
        return grad_pairs[first_row : first_row + shard_len]

    if send_count == 4:
        far_start = (reach_shards - 4) * shard_len
        far = passed_along(
            grad_pairs[far_start : far_start + 2 * shard_len].astype(jnp.bfloat16), "ctx", -2
        ).astype(jnp.float32)
        near_sum = hop_block(1) + far[shard_len:]
        next_sum = hop_block(2) + far[:shard_len]
        own_grads = (
            own_grads
            + passed_along(near_sum.astype(jnp.bfloat16), "ctx", -1).astype(jnp.float32)
            + passed_along(next_sum.astype(jnp.bfloat16), "ctx", -2).astype(jnp.float32)
        )
    else:
        for hop_index in range(1, send_count + 1):
            own_grads = own_grads + passed_along(
                hop_block(hop_index).astype(jnp.bfloat16), "ctx", -hop_index
            ).astype(jnp.float32)
    query_prenorm_gradient = (
        norm_back(query_heads, query_norm_gain, grad_query)
        .reshape(shard_len, heads_here * head_dim)
        .astype(jnp.bfloat16)
    )
    key_prenorm_gradient = norm_back(
        key_before_norm, key_norm_gain, own_grads[:, :head_dim]
    ).astype(jnp.bfloat16)
    value_prenorm_gradient = own_grads[:, head_dim:].astype(jnp.bfloat16)
    query_up_contribution = adapter_scale * transpose_multiply(middle_query, query_prenorm_gradient)
    key_up_contribution = adapter_scale * transpose_multiply(middle_key, key_prenorm_gradient)
    value_up_contribution = adapter_scale * transpose_multiply(middle_value, value_prenorm_gradient)
    middle_gradients = jnp.concatenate(
        [
            adapter_scale * multiply_by_transpose(query_prenorm_gradient, adapter_query_up),
            adapter_scale * multiply_by_transpose(key_prenorm_gradient, adapter_key_up),
            adapter_scale * multiply_by_transpose(value_prenorm_gradient, adapter_value_up),
        ],
        axis=1,
    ).astype(jnp.bfloat16)
    grad_normed = multiply_by_transpose(
        jnp.concatenate(
            [query_prenorm_gradient, key_prenorm_gradient, value_prenorm_gradient, middle_gradients],
            axis=1,
        ),
        all_weights,
    )
    grad_normed_rows = tp_sum_scatter(grad_normed.astype(jnp.bfloat16))
    grad_in = norm_back(tok_float, input_norm_gain, grad_normed_rows).astype(jnp.bfloat16)
    down_term = tp_sum_scatter(
        transpose_multiply(normalized_input, middle_gradients).astype(jnp.bfloat16)
    )
    adapter_totals = ctx_sum(
        [
            down_term,
            query_up_contribution,
            key_up_contribution,
            value_up_contribution,
            down_out_term,
            output_up_contribution,
        ]
    )
    return (
        layer_out,
        grad_in,
        adapter_totals[0],
        adapter_totals[1],
        adapter_totals[2],
        adapter_totals[3],
        adapter_totals[4],
        adapter_totals[5],
    )


def solution(mesh):
    in_specs = (
        P(("groups", "ctx", "tp"), None),
        P(("groups", "ctx", "tp"), None),
        P(("groups", "ctx")),
        P(("groups", "ctx")),
        P(),
        P(),
        P(),
        P(),
        P(None, "tp"),
        P(None, "tp"),
        P(None, "tp"),
        P("tp", None),
        P(),
        P(None, "tp"),
        P(None, "tp"),
        P(None, "tp"),
        P("tp", None),
        P(),
    )
    out_specs = (
        P(("groups", "ctx", "tp"), None),
        P(("groups", "ctx", "tp"), None),
        P(("groups", "tp"), None),
        P("groups", "tp"),
        P("groups", "tp"),
        P("groups", "tp"),
        P(("groups", "tp"), None),
        P("groups", "tp"),
    )
    return jax.shard_map(
        on_device, mesh=mesh, in_specs=in_specs, out_specs=out_specs, check_vma=False
    )
```

```python
import jax
import jax.numpy as jnp
from jax import lax
from jax.sharding import PartitionSpec as P

WINDOW = 1024


epsilon = 1e-06
adapter_scale = 2.0
score_scale = 168.0 ** (-0.5)


def passed_along(value, axis, steps):
    count = lax.axis_size(axis)
    leading, last = (max(0, -steps), min(count, count - steps))
    return lax.ppermute(value, axis, [(source, source + steps) for source in range(leading, last)])


def norm_rows(source, gain_vec):
    inverse = lax.rsqrt(jnp.mean(source * source, axis=-1, keepdims=True) + epsilon)
    return source * inverse * gain_vec


def norm_back(source, gain_vec, incoming):
    inverse = lax.rsqrt(jnp.mean(source * source, axis=-1, keepdims=True) + epsilon)
    scaled = source * inverse
    upward = incoming * gain_vec
    return inverse * (upward - scaled * jnp.mean(upward * scaled, axis=-1, keepdims=True))


def matrix_product(first_op, second_op):
    return jnp.dot(first_op, second_op, preferred_element_type=jnp.float32)


def multiply_by_transpose(first_op, second_op):
    return lax.dot_general(
        first_op, second_op, (((1,), (1,)), ((), ())), preferred_element_type=jnp.float32
    )


def transpose_multiply(first_op, second_op):
    return lax.dot_general(
        first_op, second_op, (((0,), (0,)), ((), ())), preferred_element_type=jnp.float32
    )


def window_mask(query_segs, key_codes):
    query_count = query_segs.shape[0]
    key_total = key_codes.shape[0]
    distance = (key_total - query_count + jnp.arange(query_count))[:, None] - jnp.arange(key_total)[
        None, :
    ]
    same_doc = key_codes[None, :] == query_segs[:, None] + 1
    return (distance == 0) | (distance > 0) & (distance < WINDOW) & same_doc


def tp_sum_scatter(value):
    if lax.axis_size("tp") != 2:
        return lax.psum_scatter(value, "tp", scatter_dimension=0, tiled=True).astype(jnp.float32)
    half = value.shape[0] // 2
    tp_index = lax.axis_index("tp")
    mine = lax.dynamic_slice_in_dim(value, tp_index * half, half, 0)
    theirs = lax.dynamic_slice_in_dim(value, (1 - tp_index) * half, half, 0)
    received = lax.ppermute(theirs, "tp", [(0, 1), (1, 0)])
    return mine.astype(jnp.float32) + received.astype(jnp.float32)


def tp_gather(value):
    if lax.axis_size("tp") != 2:
        return lax.all_gather(value, "tp", axis=0, tiled=True)
    received = lax.ppermute(value, "tp", [(0, 1), (1, 0)])
    both = jnp.concatenate([received, received], axis=0)
    return lax.dynamic_update_slice_in_dim(
        both, value, lax.axis_index("tp") * value.shape[0], 0
    )


def ctx_sum(parts):
    count = lax.axis_size("ctx")
    if count & (count - 1):
        return [lax.psum(p.astype(jnp.bfloat16), "ctx").astype(jnp.float32) for p in parts]
    flat = jnp.concatenate([p.astype(jnp.float32).reshape(-1) for p in parts])
    step = 1
    while step < count:
        sent = flat.astype(jnp.bfloat16)
        received = lax.ppermute(sent, "ctx", [(i, i ^ step) for i in range(count)])
        flat = sent.astype(jnp.float32) + received.astype(jnp.float32)
        step *= 2
    results, offset = [], 0
    for p in parts:
        results.append(flat[offset : offset + p.size].reshape(p.shape))
        offset += p.size
    return results


def on_device(
    tokens,
    output_gradient,
    document_index,
    real_token_count,
    input_norm_gain,
    query_norm_gain,
    key_norm_gain,
    output_norm_gain,
    query_projection,
    key_projection,
    value_projection,
    output_projection,
    adapter_down_maps,
    adapter_query_up,
    adapter_key_up,
    adapter_value_up,
    adapter_output_down,
    adapter_output_up,
):
    row_count, model_width = tokens.shape
    shard_len = document_index.shape[0]
    head_dim = key_projection.shape[1]
    adapter_product = adapter_key_up.shape[0]
    heads_here = query_projection.shape[1] // head_dim
    ctx_size = lax.axis_size("ctx")
    tp_index = lax.axis_index("tp")
    slice_width = model_width // lax.axis_size("tp")
    reach_shards = WINDOW // shard_len
    send_count = min(reach_shards, ctx_size - 1)
    tok_float = tokens.astype(jnp.float32)
    normed_rows = norm_rows(tok_float, input_norm_gain).astype(jnp.bfloat16)
    normalized_input = tp_gather(normed_rows)
    query_width = query_projection.shape[1]
    key_end = query_width + head_dim
    value_end = key_end + head_dim
    all_weights = jnp.concatenate(
        [query_projection, key_projection, value_projection, adapter_down_maps], axis=1
    )
    projected = matrix_product(normalized_input, all_weights)
    middle_list = projected[:, value_end:].astype(jnp.bfloat16)
    middle_query = middle_list[:, :adapter_product]
    middle_key = middle_list[:, adapter_product : 2 * adapter_product]
    middle_value = middle_list[:, 2 * adapter_product :]
    query_before_norm = projected[:, :query_width] + adapter_scale * matrix_product(
        middle_query, adapter_query_up
    )
    key_before_norm = projected[:, query_width:key_end] + adapter_scale * matrix_product(
        middle_key, adapter_key_up
    )
    value_before_norm = projected[:, key_end:value_end] + adapter_scale * matrix_product(
        middle_value, adapter_value_up
    )
    query_heads = query_before_norm.reshape(shard_len, heads_here, head_dim)
    query_normed = norm_rows(query_heads, query_norm_gain).astype(jnp.bfloat16)
    key_normed = norm_rows(key_before_norm, key_norm_gain).astype(jnp.bfloat16)
    value_cast = value_before_norm.astype(jnp.bfloat16)
    positions = jnp.arange(shard_len)
    is_valid = positions < real_token_count[0]
    valid_rows = is_valid.astype(jnp.float32)
    local_codes = jnp.where(is_valid, document_index + 1, 0)
    local_pair = jnp.concatenate([key_normed, value_cast], axis=1)
    code_rows = jnp.zeros((16, local_pair.shape[1]), jnp.bfloat16)
    code_rows = code_rows.at[0, :shard_len].set(local_codes.astype(jnp.bfloat16))
    payload = jnp.concatenate([local_pair, code_rows], axis=0)
    payload_rows = payload.shape[0]
    if send_count == 4:
        two_back = passed_along(payload, "ctx", 2)
        odd_back = passed_along(jnp.concatenate([payload, two_back], axis=0), "ctx", 1)
        arrivals = [
            odd_back[:payload_rows],
            two_back,
            odd_back[payload_rows:],
            passed_along(two_back, "ctx", 2),
        ]
    else:
        arrivals = [
            passed_along(payload, "ctx", hop_index) for hop_index in range(1, send_count + 1)
        ]
    received = [
        (arrived[:shard_len], arrived[shard_len, :shard_len].astype(jnp.int32))
        for arrived in arrivals
    ]
    missing = reach_shards - send_count
    blank_pair = jnp.zeros_like(local_pair)
    blank_codes = jnp.zeros_like(local_codes)
    earlier = [(blank_pair, blank_codes)] * missing + list(reversed(received))
    key_pairs = jnp.concatenate([entry[0] for entry in earlier] + [local_pair], axis=0)
    key_codes_all = jnp.concatenate([entry[1] for entry in earlier] + [local_codes], axis=0)
    keys_all = key_pairs[:, :head_dim]
    values_all = key_pairs[:, head_dim:]
    allowed = window_mask(document_index, key_codes_all)
    scores = (
        jnp.einsum("thd,sd->hts", query_normed, keys_all, preferred_element_type=jnp.float32)
        * score_scale
    )
    weights = jnp.where(allowed[None], jnp.exp(scores), 0.0)
    attn_probs = weights / jnp.sum(weights, axis=-1, keepdims=True)
    probs_cast = attn_probs.astype(jnp.bfloat16)
    attention_result = jnp.einsum(
        "hts,sd->thd", probs_cast, values_all, preferred_element_type=jnp.float32
    )
    attention_result = (
        (attention_result * valid_rows[:, None, None])
        .astype(jnp.bfloat16)
        .reshape(shard_len, heads_here * head_dim)
    )
    part_out = matrix_product(attention_result, output_projection)
    partial_middle = matrix_product(attention_result, adapter_output_down)
    output_total = tp_sum_scatter(part_out.astype(jnp.bfloat16))
    mid_sum = tp_sum_scatter(partial_middle.astype(jnp.bfloat16))
    middle_output = mid_sum.astype(jnp.bfloat16)
    apply_prenorm = output_total + adapter_scale * matrix_product(middle_output, adapter_output_up)
    layer_out = norm_rows(apply_prenorm, output_norm_gain).astype(jnp.bfloat16)
    prenorm_gradient = norm_back(
        apply_prenorm, output_norm_gain, output_gradient.astype(jnp.float32)
    ).astype(jnp.bfloat16)
    middle_output_gradient = (
        adapter_scale * multiply_by_transpose(prenorm_gradient, adapter_output_up)
    ).astype(jnp.bfloat16)
    complete_gradient = tp_gather(prenorm_gradient)
    middle_pair = tp_gather(jnp.concatenate([middle_output_gradient, middle_output], axis=1))
    middle_complete_gradient = middle_pair[:, :adapter_product]
    middle_complete = middle_pair[:, adapter_product:]
    gradient_portion = lax.dynamic_slice_in_dim(
        complete_gradient, tp_index * slice_width, slice_width, 1
    )
    output_up_contribution = adapter_scale * transpose_multiply(middle_complete, gradient_portion)
    attention_gradient = multiply_by_transpose(
        complete_gradient, output_projection
    ) + multiply_by_transpose(middle_complete_gradient, adapter_output_down)
    attention_gradient = (attention_gradient * valid_rows[:, None]).astype(jnp.bfloat16)
    down_out_term = transpose_multiply(attention_result, middle_complete_gradient)
    grad_heads = attention_gradient.reshape(shard_len, heads_here, head_dim)
    grad_probs = jnp.einsum(
        "thd,sd->hts", grad_heads, values_all, preferred_element_type=jnp.float32
    )
    inner_sum = jnp.sum(attn_probs * grad_probs, axis=-1, keepdims=True)
    grad_scores = lax.optimization_barrier(
        (attn_probs * (grad_probs - inner_sum) * score_scale).astype(jnp.bfloat16)
    )
    grad_query = jnp.einsum(
        "hts,sd->thd", grad_scores, keys_all, preferred_element_type=jnp.float32
    )
    grad_keys = jnp.einsum(
        "hts,thd->sd", grad_scores, query_normed, preferred_element_type=jnp.float32
    )
    grad_values = jnp.einsum(
        "hts,thd->sd", probs_cast, grad_heads, preferred_element_type=jnp.float32
    )
    grad_pairs = jnp.concatenate([grad_keys, grad_values], axis=1)
    own_grads = grad_pairs[reach_shards * shard_len :]

    def hop_block(hop_index):
        first_row = (reach_shards - hop_index) * shard_len
        return grad_pairs[first_row : first_row + shard_len]

    if send_count == 4:
        far = passed_along(
            jnp.concatenate([hop_block(3), hop_block(4)], axis=0).astype(jnp.bfloat16), "ctx", -2
        ).astype(jnp.float32)
        near_sum = hop_block(1) + far[:shard_len]
        next_sum = hop_block(2) + far[shard_len:]
        own_grads = (
            own_grads
            + passed_along(near_sum.astype(jnp.bfloat16), "ctx", -1).astype(jnp.float32)
            + passed_along(next_sum.astype(jnp.bfloat16), "ctx", -2).astype(jnp.float32)
        )
    else:
        for hop_index in range(1, send_count + 1):
            own_grads = own_grads + passed_along(
                hop_block(hop_index).astype(jnp.bfloat16), "ctx", -hop_index
            ).astype(jnp.float32)
    query_prenorm_gradient = (
        norm_back(query_heads, query_norm_gain, grad_query)
        .reshape(shard_len, heads_here * head_dim)
        .astype(jnp.bfloat16)
    )
    key_prenorm_gradient = norm_back(
        key_before_norm, key_norm_gain, own_grads[:, :head_dim]
    ).astype(jnp.bfloat16)
    value_prenorm_gradient = own_grads[:, head_dim:].astype(jnp.bfloat16)
    query_up_contribution = adapter_scale * transpose_multiply(middle_query, query_prenorm_gradient)
    key_up_contribution = adapter_scale * transpose_multiply(middle_key, key_prenorm_gradient)
    value_up_contribution = adapter_scale * transpose_multiply(middle_value, value_prenorm_gradient)
    middle_gradients = jnp.concatenate(
        [
            adapter_scale * multiply_by_transpose(query_prenorm_gradient, adapter_query_up),
            adapter_scale * multiply_by_transpose(key_prenorm_gradient, adapter_key_up),
            adapter_scale * multiply_by_transpose(value_prenorm_gradient, adapter_value_up),
        ],
        axis=1,
    ).astype(jnp.bfloat16)
    grad_normed = multiply_by_transpose(
        jnp.concatenate(
            [query_prenorm_gradient, key_prenorm_gradient, value_prenorm_gradient, middle_gradients],
            axis=1,
        ),
        all_weights,
    )
    grad_normed_rows = tp_sum_scatter(grad_normed.astype(jnp.bfloat16))
    grad_in = norm_back(tok_float, input_norm_gain, grad_normed_rows).astype(jnp.bfloat16)
    down_term = tp_sum_scatter(
        transpose_multiply(normalized_input, middle_gradients).astype(jnp.bfloat16)
    )
    adapter_totals = ctx_sum(
        [
            down_term,
            query_up_contribution,
            key_up_contribution,
            value_up_contribution,
            down_out_term,
            output_up_contribution,
        ]
    )
    return (
        layer_out,
        grad_in,
        adapter_totals[0],
        adapter_totals[1],
        adapter_totals[2],
        adapter_totals[3],
        adapter_totals[4],
        adapter_totals[5],
    )


def solution(mesh):
    in_specs = (
        P(("groups", "ctx", "tp"), None),
        P(("groups", "ctx", "tp"), None),
        P(("groups", "ctx")),
        P(("groups", "ctx")),
        P(),
        P(),
        P(),
        P(),
        P(None, "tp"),
        P(None, "tp"),
        P(None, "tp"),
        P("tp", None),
        P(),
        P(None, "tp"),
        P(None, "tp"),
        P(None, "tp"),
        P("tp", None),
        P(),
    )
    out_specs = (
        P(("groups", "ctx", "tp"), None),
        P(("groups", "ctx", "tp"), None),
        P(("groups", "tp"), None),
        P("groups", "tp"),
        P("groups", "tp"),
        P("groups", "tp"),
        P(("groups", "tp"), None),
        P("groups", "tp"),
    )
    return jax.shard_map(
        on_device, mesh=mesh, in_specs=in_specs, out_specs=out_specs, check_vma=False
    )
```
